32 devices in a mesh: ctx: 16 (over z, x, core), head: 2 (over y).
Axes of the slice: x: 2, y: 2, z: 4, core: 2. Of those that a mesh axis runs over, the one named last changes fastest.
Arguments:
- query_rows: bfloat16 [4096, 1024], P(('ctx', 'head')), may hold values from -6 to 6
- key_rows: bfloat16 [4096, 1024], P(('ctx', 'head')), may hold values from -6 to 6
- value_rows: bfloat16 [4096, 2048], P(('ctx', 'head')), may hold values from -6 to 6
- output_gate: bfloat16 [4096, 2048], P(('ctx', 'head')), may hold values from -6 to 6
- beta_logit: bfloat16 [4096, 16], P(('ctx', 'head')), may hold values from -7 to -3.5
- log_decay: bfloat16 [4096, 16], P(('ctx', 'head')), may hold values from -1 to 0
- norm_gain: bfloat16 [128], replicated, may hold values from 0.5 to 1.5
Outputs:
- layer_out: bfloat16 [4096, 2048], P(('ctx', 'head'))
The draws below stay inside these ranges and needn't reach their ends.
All inputs are finite; a program needn't handle non-finite values.
Results may differ from the reference program's by a relative error of at most 0.0049.
Values may be sent and summed in bfloat16 or wider, within the bound.
No kernel may reach another device: no remote copies, remote signals or barrier semaphores. Data moves between devices by JAX's collectives and lax.ppermute only.
A program may use at most 128 MiB of HBM per device.

```python
import math
import jax
import jax.numpy as jnp
from jax import lax

DK = 128
DV = 128
KHEADS = 8
VALUE_HEAD_COUNT = 16
TOKEN_TOTAL = 4096


def draw_log_decay(key, part):
    key_sequence = jax.random.split(key, 6)
    fast_share = 0.5
    lower_end = 0.5
    upper_end = 1.5
    chosen = jax.random.uniform(key_sequence[0], (VALUE_HEAD_COUNT,), jnp.float32)
    fast_rate = jnp.exp(jax.random.uniform(key_sequence[1], (VALUE_HEAD_COUNT,), jnp.float32, math.log(1.0 / 50.0), math.log(1.0 / 30.0)))
    slow_rate = jnp.exp(jax.random.uniform(key_sequence[2], (VALUE_HEAD_COUNT,), jnp.float32, math.log(0.25), 0.0)) / TOKEN_TOTAL
    decay_factor = jnp.where(chosen < fast_share, fast_rate, slow_rate)
    random_noise = jax.random.uniform(key_sequence[3], (TOKEN_TOTAL, VALUE_HEAD_COUNT), jnp.float32, lower_end, upper_end)
    spike_position = jax.random.randint(key_sequence[4], (2, VALUE_HEAD_COUNT), 0, TOKEN_TOTAL)
    token_position = lax.broadcasted_iota(jnp.int32, (TOKEN_TOTAL, VALUE_HEAD_COUNT), 0)
    spike_hit_mask = (token_position == spike_position[0]) | (token_position == spike_position[1])
    spike_log_decay = jnp.log(jax.random.uniform(key_sequence[5], (TOKEN_TOTAL, VALUE_HEAD_COUNT), jnp.float32, 0.5, 0.8))
    layer_result = -decay_factor * random_noise + jnp.where(spike_hit_mask, spike_log_decay, 0.0)
    return layer_result.astype(jnp.bfloat16)


def shard_levels(stream_key, extent, cuts, smallest, largest):
    level, own = 1.0, jax.random.fold_in(stream_key, 6)
    for dim, blocks in cuts:
        steps = jnp.exp(jax.random.uniform(jax.random.fold_in(own, dim), (blocks,), jnp.float32, smallest / len(cuts), largest / len(cuts)))
        level = level * jnp.repeat(steps, extent[dim] // blocks).reshape([-1 if axis == dim else 1 for axis in range(len(extent))])
    return level


def bell_draw(own_key, dims, scale, bound, cuts=(), held_as=jnp.bfloat16):
    gain = shard_levels(own_key, dims, cuts, -0.22, 0.18) if cuts else 1.0
    array = jax.random.normal(own_key, dims, jnp.float32) * scale * gain
    return jnp.minimum(jnp.maximum(array, -bound), bound).astype(held_as)


def setup_inputs(seed: int = 0) -> dict:
    arg_keys = jax.random.split(jax.random.key(seed), 8)
    query_rows = bell_draw(arg_keys[0], (TOKEN_TOTAL, KHEADS * DK), 1.0, 6.0, ((0, 32),))
    key_rows = bell_draw(arg_keys[1], (TOKEN_TOTAL, KHEADS * DK), 1.0, 6.0, ((0, 32),))
    value_rows = bell_draw(arg_keys[2], (TOKEN_TOTAL, VALUE_HEAD_COUNT * DV), 1.0, 6.0, ((0, 32),))
    output_gate = bell_draw(arg_keys[3], (TOKEN_TOTAL, VALUE_HEAD_COUNT * DV), 1.0, 6.0, ((0, 32),))
    beta_logit = jnp.clip(-7.0 + 3.5 * jax.random.uniform(arg_keys[4], (TOKEN_TOTAL, VALUE_HEAD_COUNT), jnp.float32) ** shard_levels(arg_keys[4], (TOKEN_TOTAL, VALUE_HEAD_COUNT), ((0, 32),), -0.2, 0.2), -7.0, -3.5).astype(jnp.bfloat16)
    log_decay = draw_log_decay(jax.random.fold_in(arg_keys[7], 71), 0)
    norm_gain = jnp.clip(1.0 + 0.1 * jax.random.normal(arg_keys[6], (DV,), jnp.float32), 0.5, 1.5).astype(jnp.bfloat16)
    return {"query_rows": query_rows, "key_rows": key_rows, "value_rows": value_rows, "output_gate": output_gate, "beta_logit": beta_logit, "log_decay": log_decay, "norm_gain": norm_gain}


FULL_PRECISION = lax.Precision.HIGHEST

def unit_rows(rows):
    return rows * lax.rsqrt(lax.optimization_barrier(jnp.sum(rows * rows, axis=-1, keepdims=True)) + 1e-06)

def gated_norm(core_rows, output_gate, norm_gain):
    token_count = core_rows.shape[0]
    head_count = core_rows.shape[1] // DV
    core_f = core_rows.astype(jnp.float32).reshape(token_count, head_count, DV)
    inv_rms = lax.rsqrt(lax.optimization_barrier(jnp.mean(core_f * core_f, axis=-1, keepdims=True)) + 1e-06)
    gate_f = output_gate.astype(jnp.float32).reshape(token_count, head_count, DV)
    gated_rows = core_f * inv_rms * norm_gain.astype(jnp.float32) * jax.nn.silu(gate_f)
    return gated_rows.reshape(token_count, head_count * DV).astype(jnp.bfloat16)

def reference(query_rows, key_rows, value_rows, output_gate, beta_logit, log_decay, norm_gain):
    group_size = VALUE_HEAD_COUNT // KHEADS
    query_in = query_rows.reshape(TOKEN_TOTAL, KHEADS, DK)
    key_in = key_rows.reshape(TOKEN_TOTAL, KHEADS, DK)
    value_in = value_rows.reshape(TOKEN_TOTAL, VALUE_HEAD_COUNT, DV)

    def advance(recurrent_state, inputs):
        q_now, k_now, v_now, b_now, d_now = inputs
        query_normalized = jnp.repeat(unit_rows(q_now.astype(jnp.float32)) * DK ** (-0.5), group_size, axis=0)
        key_normalized = jnp.repeat(unit_rows(k_now.astype(jnp.float32)), group_size, axis=0)
        beta_now = jax.nn.sigmoid(b_now.astype(jnp.float32))
        decay_now = jnp.exp(d_now.astype(jnp.float32))
        state_readout = jnp.einsum('ew,ewy->ey', key_normalized, recurrent_state, precision=FULL_PRECISION)
        erased = recurrent_state - beta_now[:, None, None] * key_normalized[:, :, None] * state_readout[:, None, :]
        recurrent_state = decay_now[:, None, None] * erased + beta_now[:, None, None] * key_normalized[:, :, None] * v_now.astype(jnp.float32)[:, None, :]
        current_core_output = jnp.einsum('ew,ewy->ey', query_normalized, recurrent_state, precision=FULL_PRECISION).astype(jnp.bfloat16)
        return (recurrent_state, current_core_output)
    start = jnp.zeros((VALUE_HEAD_COUNT, DK, DV), jnp.float32)
    _, core_all = lax.scan(advance, start, (query_in, key_in, value_in, beta_logit, log_decay))
    core_rows = lax.optimization_barrier(core_all.reshape(TOKEN_TOTAL, VALUE_HEAD_COUNT * DV))
    return gated_norm(core_rows, output_gate, norm_gain)
```

```python
import jax
import jax.numpy as jnp
from jax import lax
from jax.sharding import PartitionSpec as P

DK = 128
DV = 128
SPAN = 128


FULL_PRECISION = lax.Precision.HIGHEST


def unit_rows(rows):
    return rows * lax.rsqrt(jnp.sum(rows * rows, axis=-1, keepdims=True) + 1e-06)


def compose(earlier, later):
    return (
        jnp.matmul(later[0], earlier[0], precision=FULL_PRECISION),
        jnp.matmul(later[0], earlier[1], precision=FULL_PRECISION) + later[1],
    )


def arrange(key_part, value_part, beta_part, decay_part):
    blocks = key_part.shape[0] // SPAN
    key_heads = key_part.shape[1] // DK
    value_heads = value_part.shape[1] // DV
    key_unit = unit_rows(
        key_part.astype(jnp.float32).reshape(blocks, SPAN, key_heads, DK)
    ).transpose(2, 0, 1, 3)
    value_f = (
        value_part.astype(jnp.float32).reshape(blocks, SPAN, value_heads, DV).transpose(2, 0, 1, 3)
    )
    beta_gate = (
        jax.nn.sigmoid(beta_part.astype(jnp.float32))
        .reshape(blocks, SPAN, value_heads)
        .transpose(2, 0, 1)
    )
    decay_log = decay_part.astype(jnp.float32).reshape(blocks, SPAN, value_heads).transpose(2, 0, 1)
    return (key_unit, value_f, beta_gate, decay_log)


def arrange_query(query_part):
    blocks = query_part.shape[0] // SPAN
    key_heads = query_part.shape[1] // DK
    query_f = query_part.astype(jnp.float32).reshape(blocks, SPAN, key_heads, DK)
    return (unit_rows(query_f) * DK ** (-0.5)).transpose(2, 0, 1, 3)


def block_total(carry_mat, write_mat):
    head_count = carry_mat.shape[0]
    start = (
        jnp.broadcast_to(jnp.eye(DK, dtype=jnp.float32), (head_count, DK, DK)),
        jnp.zeros((head_count, DK, DV), jnp.float32),
    )

    def step(acc, pair):
        return (compose(acc, pair), None)

    total, _ = lax.scan(step, start, (jnp.moveaxis(carry_mat, 1, 0), jnp.moveaxis(write_mat, 1, 0)))
    return total


def block_states(carry_mat, write_mat, state_in):

    def step(state, pair):
        return (jnp.matmul(pair[0], state, precision=FULL_PRECISION) + pair[1], state)

    _, states = lax.scan(
        step, state_in, (jnp.moveaxis(carry_mat, 1, 0), jnp.moveaxis(write_mat, 1, 0))
    )
    return jnp.moveaxis(states, 0, 1)


def unit_lower_inverse(strictly_lower):
    inverse = jnp.eye(SPAN, dtype=jnp.float32) - strictly_lower
    power = strictly_lower
    covered = 2
    while covered < SPAN:
        power = jnp.matmul(power, power, precision=FULL_PRECISION)
        inverse = inverse + jnp.matmul(inverse, power, precision=FULL_PRECISION)
        covered = covered * 2
    return inverse


def span_pass(key_unit, value_f, beta_gate, decay_log, group_size):
    rowpos = lax.broadcasted_iota(jnp.int32, (SPAN, SPAN), 0)
    colpos = lax.broadcasted_iota(jnp.int32, (SPAN, SPAN), 1)
    cum_log = jnp.cumsum(decay_log, axis=2)
    spread = cum_log[..., :, None] - cum_log[..., None, :]
    strict = jnp.exp(jnp.where(colpos < rowpos, spread, -jnp.inf))
    key_inner = jnp.repeat(
        jnp.einsum("hmik,hmjk->hmij", key_unit, key_unit, precision=FULL_PRECISION),
        group_size,
        axis=0,
    )
    inverse = unit_lower_inverse(beta_gate[..., :, None] * strict * key_inner)
    wide_keys = jnp.repeat(key_unit, group_size, axis=0)
    targets = jnp.concatenate(
        [beta_gate[..., None] * value_f, (beta_gate * jnp.exp(cum_log))[..., None] * wide_keys],
        axis=-1,
    )
    solved = jnp.matmul(inverse, targets, precision=FULL_PRECISION)
    written = solved[..., :DV]
    weights = solved[..., DV:]
    faded_keys = wide_keys * jnp.exp(cum_log[..., -1:] - cum_log)[..., None]
    tail_decay = jnp.exp(cum_log[..., -1])
    carry_mat = tail_decay[..., None, None] * jnp.eye(DK, dtype=jnp.float32) - jnp.einsum(
        "hmck,hmcj->hmkj", faded_keys, weights, precision=FULL_PRECISION
    )
    write_mat = jnp.einsum("hmck,hmcv->hmkv", faded_keys, written, precision=FULL_PRECISION)
    total_carry, total_write = block_total(carry_mat, write_mat)
    return (cum_log, spread, written, weights, carry_mat, write_mat, total_carry, total_write)


def span_out(query_unit, key_unit, group_size, pieces, state_in):
    cum_log, spread, written, weights, carry_mat, write_mat = pieces[:6]
    states = block_states(carry_mat, write_mat, state_in)
    rowpos = lax.broadcasted_iota(jnp.int32, (SPAN, SPAN), 0)
    colpos = lax.broadcasted_iota(jnp.int32, (SPAN, SPAN), 1)
    within = jnp.exp(jnp.where(colpos <= rowpos, spread, -jnp.inf))
    scores = (
        jnp.repeat(
            jnp.einsum("hmik,hmjk->hmij", query_unit, key_unit, precision=FULL_PRECISION),
            group_size,
            axis=0,
        )
        * within
    )
    new_values = written - jnp.einsum("hmck,hmkv->hmcv", weights, states, precision=FULL_PRECISION)
    wide_query = jnp.repeat(query_unit, group_size, axis=0)
    carried = (
        jnp.einsum("hmck,hmkv->hmcv", wide_query, states, precision=FULL_PRECISION)
        * jnp.exp(cum_log)[..., None]
    )
    return carried + jnp.einsum("hmij,hmjv->hmiv", scores, new_values, precision=FULL_PRECISION)


def to_rows(core_out):
    head_count, blocks = (core_out.shape[0], core_out.shape[1])
    return core_out.transpose(1, 2, 0, 3).reshape(blocks * SPAN, head_count * DV)


def chain_states(block_carry, block_write):
    size = lax.axis_size("ctx")
    carry, write = (block_carry, block_write)
    shift = 1
    while 2 * shift < size:
        pairs = [(i, i + shift) for i in range(size - shift)]
        carry_in, write_in = lax.ppermute((carry, write), "ctx", pairs)
        carry, write = compose((carry_in, write_in), (carry, write))
        shift *= 2
    if shift < size:
        pairs = [(i, i + shift) for i in range(size - shift)]
        write_in = lax.ppermute(write, "ctx", pairs)
        write = jnp.matmul(carry, write_in, precision=FULL_PRECISION) + write
    return lax.ppermute(write, "ctx", [(i, i + 1) for i in range(size - 1)])


def gated_norm(core_rows, output_gate, norm_gain):
    token_count = core_rows.shape[0]
    head_count = core_rows.shape[1] // DV
    core_f = core_rows.astype(jnp.float32).reshape(token_count, head_count, DV)
    inv_rms = lax.rsqrt(jnp.mean(core_f * core_f, axis=-1, keepdims=True) + 1e-06)
    gate_f = output_gate.astype(jnp.float32).reshape(token_count, head_count, DV)
    gated_rows = core_f * inv_rms * norm_gain.astype(jnp.float32) * jax.nn.silu(gate_f)
    return gated_rows.reshape(token_count, head_count * DV).astype(jnp.bfloat16)


def on_device(query_rows, key_rows, value_rows, output_gate, beta_logit, log_decay, norm_gain):
    q_head, k_head, v_head, b_head, d_head = (
        lax.all_to_all(query_rows, "head", split_axis=1, concat_axis=0, tiled=True),
        lax.all_to_all(key_rows, "head", split_axis=1, concat_axis=0, tiled=True),
        lax.all_to_all(value_rows, "head", split_axis=1, concat_axis=0, tiled=True),
        lax.all_to_all(beta_logit, "head", split_axis=1, concat_axis=0, tiled=True),
        lax.all_to_all(log_decay, "head", split_axis=1, concat_axis=0, tiled=True),
    )
    key_unit, value_f, beta_gate, decay_log = arrange(k_head, v_head, b_head, d_head)
    group_size = value_f.shape[0] // key_unit.shape[0]
    pieces = span_pass(key_unit, value_f, beta_gate, decay_log, group_size)
    query_unit = arrange_query(q_head)
    state_in = chain_states(pieces[6], pieces[7])
    core_out = span_out(query_unit, key_unit, group_size, pieces, state_in)
    core_rows = lax.all_to_all(
        to_rows(core_out).astype(jnp.bfloat16), "head", split_axis=0, concat_axis=1, tiled=True
    )
    return gated_norm(core_rows, output_gate, norm_gain)


def solution(mesh):
    placed = (
        P(("ctx", "head"), None),
        P(("ctx", "head"), None),
        P(("ctx", "head"), None),
        P(("ctx", "head"), None),
        P(("ctx", "head"), None),
        P(("ctx", "head"), None),
        P(),
    )
    return jax.shard_map(
        on_device, mesh=mesh, in_specs=placed, out_specs=P(("ctx", "head"), None), check_vma=False
    )
```

```python
import jax
import jax.numpy as jnp
from jax import lax
from jax.sharding import PartitionSpec as P

DK = 128
DV = 128
SPAN = 128


FULL_PRECISION = lax.Precision.HIGHEST


def unit_rows(rows):
    return rows * lax.rsqrt(jnp.sum(rows * rows, axis=-1, keepdims=True) + 1e-06)


def compose(earlier, later):
    return (
        jnp.matmul(later[0], earlier[0], precision=FULL_PRECISION),
        jnp.matmul(later[0], earlier[1], precision=FULL_PRECISION) + later[1],
    )


def arrange(key_part, value_part, beta_part, decay_part):
    blocks = key_part.shape[0] // SPAN
    key_heads = key_part.shape[1] // DK
    value_heads = value_part.shape[1] // DV
    key_unit = unit_rows(
        key_part.astype(jnp.float32).reshape(blocks, SPAN, key_heads, DK)
    ).transpose(2, 0, 1, 3)
    value_f = (
        value_part.astype(jnp.float32).reshape(blocks, SPAN, value_heads, DV).transpose(2, 0, 1, 3)
    )
    beta_gate = (
        jax.nn.sigmoid(beta_part.astype(jnp.float32))
        .reshape(blocks, SPAN, value_heads)
        .transpose(2, 0, 1)
    )
    decay_log = decay_part.astype(jnp.float32).reshape(blocks, SPAN, value_heads).transpose(2, 0, 1)
    return (key_unit, value_f, beta_gate, decay_log)


def arrange_query(query_part):
    blocks = query_part.shape[0] // SPAN
    key_heads = query_part.shape[1] // DK
    query_f = query_part.astype(jnp.float32).reshape(blocks, SPAN, key_heads, DK)
    return (unit_rows(query_f) * DK ** (-0.5)).transpose(2, 0, 1, 3)


def unit_lower_inverse(strictly_lower):
    inverse = jnp.eye(SPAN, dtype=jnp.float32) - strictly_lower
    power = jnp.matmul(strictly_lower, strictly_lower, precision=FULL_PRECISION)
    covered = 2
    while covered < SPAN:
        if 2 * covered < SPAN:
            both = jnp.matmul(
                jnp.concatenate([inverse, power], axis=-2), power, precision=FULL_PRECISION
            )
            inverse = inverse + both[..., :SPAN, :]
            power = both[..., SPAN:, :]
        else:
            inverse = inverse + jnp.matmul(inverse, power, precision=FULL_PRECISION)
        covered = covered * 2
    return inverse


def span_pass(key_unit, value_f, beta_gate, decay_log, group_size):
    rowpos = lax.broadcasted_iota(jnp.int32, (SPAN, SPAN), 0)
    colpos = lax.broadcasted_iota(jnp.int32, (SPAN, SPAN), 1)
    cum_log = jnp.cumsum(decay_log, axis=2)
    spread = cum_log[..., :, None] - cum_log[..., None, :]
    strict = jnp.exp(jnp.where(colpos < rowpos, spread, -jnp.inf))
    key_inner = jnp.repeat(
        jnp.einsum("hmik,hmjk->hmij", key_unit, key_unit, precision=FULL_PRECISION),
        group_size,
        axis=0,
    )
    inverse = unit_lower_inverse(beta_gate[..., :, None] * strict * key_inner)
    wide_keys = jnp.repeat(key_unit, group_size, axis=0)
    targets = jnp.concatenate(
        [beta_gate[..., None] * value_f, (beta_gate * jnp.exp(cum_log))[..., None] * wide_keys],
        axis=-1,
    )
    solved = jnp.matmul(inverse, targets, precision=FULL_PRECISION)
    written = solved[..., :DV]
    weights = solved[..., DV:]
    faded_keys = wide_keys * jnp.exp(cum_log[..., -1:] - cum_log)[..., None]
    tail_decay = jnp.exp(cum_log[..., -1])
    carry_mat = tail_decay[..., None, None] * jnp.eye(DK, dtype=jnp.float32) - jnp.einsum(
        "hmck,hmcj->hmkj", faded_keys, weights, precision=FULL_PRECISION
    )
    write_mat = jnp.einsum("hmck,hmcv->hmkv", faded_keys, written, precision=FULL_PRECISION)
    return (cum_log, spread, written, weights, carry_mat, write_mat)


def span_prep(query_unit, key_unit, group_size, pieces):
    cum_log, spread, written, weights, carry_mat, write_mat = pieces
    rowpos = lax.broadcasted_iota(jnp.int32, (SPAN, SPAN), 0)
    colpos = lax.broadcasted_iota(jnp.int32, (SPAN, SPAN), 1)
    within = jnp.exp(jnp.where(colpos <= rowpos, spread, -jnp.inf))
    scores = (
        jnp.repeat(
            jnp.einsum("hmik,hmjk->hmij", query_unit, key_unit, precision=FULL_PRECISION),
            group_size,
            axis=0,
        )
        * within
    )
    wide_query = jnp.repeat(query_unit, group_size, axis=0)
    inner = jnp.einsum("hmij,hmjv->hmiv", scores, written, precision=FULL_PRECISION)
    reach = wide_query * jnp.exp(cum_log)[..., None] - jnp.einsum(
        "hmij,hmjk->hmik", scores, weights, precision=FULL_PRECISION
    )
    head_count, blocks = (carry_mat.shape[0], carry_mat.shape[1])
    reach_map = jnp.broadcast_to(jnp.eye(DK, dtype=jnp.float32), (head_count, DK, DK))
    reach_add = jnp.zeros((head_count, DK, DV), jnp.float32)
    fixed, scaled = ([], [])
    for m in range(blocks):
        if m == 0:
            fixed.append(inner[:, m])
            scaled.append(reach[:, m])
        else:
            fixed.append(
                inner[:, m]
                + jnp.matmul(reach[:, m], reach_add, precision=FULL_PRECISION)
            )
            scaled.append(jnp.matmul(reach[:, m], reach_map, precision=FULL_PRECISION))
        reach_map, reach_add = compose((reach_map, reach_add), (carry_mat[:, m], write_mat[:, m]))
    return (jnp.stack(fixed, axis=1), jnp.stack(scaled, axis=1), reach_map, reach_add)


def span_out(fixed, scaled, state_in):
    return fixed + jnp.einsum("hmck,hkv->hmcv", scaled, state_in, precision=FULL_PRECISION)


def to_rows(core_out):
    head_count, blocks = (core_out.shape[0], core_out.shape[1])
    return core_out.transpose(1, 2, 0, 3).reshape(blocks * SPAN, head_count * DV)


def chain_states(block_carry, block_write):
    size = lax.axis_size("ctx")
    carry, write = (block_carry, block_write)
    shift = 1
    while 2 * shift < size:
        pairs = [(i, i + shift) for i in range(size - shift)]
        carry_in, write_in = lax.ppermute((carry, write), "ctx", pairs)
        carry, write = compose((carry_in, write_in), (carry, write))
        shift *= 2
    if shift < size:
        pairs = [(i, i + shift) for i in range(size - shift)]
        write_in = lax.ppermute(write, "ctx", pairs)
        write = jnp.matmul(carry, write_in, precision=FULL_PRECISION) + write
    return lax.ppermute(write, "ctx", [(i, i + 1) for i in range(size - 1)])


def gated_norm(core_rows, output_gate, norm_gain):
    token_count = core_rows.shape[0]
    head_count = core_rows.shape[1] // DV
    core_f = core_rows.astype(jnp.float32).reshape(token_count, head_count, DV)
    inv_rms = lax.rsqrt(jnp.mean(core_f * core_f, axis=-1, keepdims=True) + 1e-06)
    gate_f = output_gate.astype(jnp.float32).reshape(token_count, head_count, DV)
    gated_rows = core_f * inv_rms * norm_gain.astype(jnp.float32) * jax.nn.silu(gate_f)
    return gated_rows.reshape(token_count, head_count * DV).astype(jnp.bfloat16)


def on_device(query_rows, key_rows, value_rows, output_gate, beta_logit, log_decay, norm_gain):
    parts = lax.axis_size("head")
    tokens = query_rows.shape[0]
    pieces_in = [query_rows, key_rows, value_rows, beta_logit, log_decay]
    widths = [part.shape[1] // parts for part in pieces_in]
    packed = jnp.concatenate(
        [part.reshape(tokens, parts, width) for part, width in zip(pieces_in, widths)], axis=-1
    )
    packed = lax.all_to_all(packed, "head", split_axis=1, concat_axis=0, tiled=True)
    packed = packed.reshape(tokens * parts, sum(widths))
    ends = [sum(widths[: i + 1]) for i in range(len(widths))]
    q_head, k_head, v_head, b_head, d_head = (
        packed[:, end - width : end] for end, width in zip(ends, widths)
    )
    key_unit, value_f, beta_gate, decay_log = arrange(k_head, v_head, b_head, d_head)
    group_size = value_f.shape[0] // key_unit.shape[0]
    pieces = span_pass(key_unit, value_f, beta_gate, decay_log, group_size)
    query_unit = arrange_query(q_head)
    fixed, scaled, total_carry, total_write = span_prep(query_unit, key_unit, group_size, pieces)
    state_in = chain_states(total_carry, total_write)
    core_out = span_out(fixed, scaled, state_in)
    core_rows = lax.all_to_all(
        to_rows(core_out).astype(jnp.bfloat16), "head", split_axis=0, concat_axis=1, tiled=True
    )
    return gated_norm(core_rows, output_gate, norm_gain)


def solution(mesh):
    placed = (
        P(("ctx", "head"), None),
        P(("ctx", "head"), None),
        P(("ctx", "head"), None),
        P(("ctx", "head"), None),
        P(("ctx", "head"), None),
        P(("ctx", "head"), None),
        P(),
    )
    return jax.shard_map(
        on_device, mesh=mesh, in_specs=placed, out_specs=P(("ctx", "head"), None), check_vma=False
    )
```

```python
import jax
import jax.numpy as jnp
from jax import lax
from jax.sharding import PartitionSpec as P

DK = 128
DV = 128
SPAN = 128


FULL_PRECISION = lax.Precision.HIGHEST


def unit_rows(rows):
    return rows * lax.rsqrt(jnp.sum(rows * rows, axis=-1, keepdims=True) + 1e-06)


def compose(earlier, later):
    return (
        jnp.matmul(later[0], earlier[0], precision=FULL_PRECISION),
        jnp.matmul(later[0], earlier[1], precision=FULL_PRECISION) + later[1],
    )


def arrange(key_part, value_part, beta_part, decay_part):
    blocks = key_part.shape[0] // SPAN
    key_heads = key_part.shape[1] // DK
    value_heads = value_part.shape[1] // DV
    key_unit = unit_rows(
        key_part.astype(jnp.float32).reshape(blocks, SPAN, key_heads, DK)
    ).transpose(2, 0, 1, 3)
    value_f = (
        value_part.astype(jnp.float32).reshape(blocks, SPAN, value_heads, DV).transpose(2, 0, 1, 3)
    )
    beta_gate = (
        jax.nn.sigmoid(beta_part.astype(jnp.float32))
        .reshape(blocks, SPAN, value_heads)
        .transpose(2, 0, 1)
    )
    decay_log = decay_part.astype(jnp.float32).reshape(blocks, SPAN, value_heads).transpose(2, 0, 1)
    return (key_unit, value_f, beta_gate, decay_log)


def arrange_query(query_part):
    blocks = query_part.shape[0] // SPAN
    key_heads = query_part.shape[1] // DK
    query_f = query_part.astype(jnp.float32).reshape(blocks, SPAN, key_heads, DK)
    return (unit_rows(query_f) * DK ** (-0.5)).transpose(2, 0, 1, 3)


def unit_lower_inverse(strictly_lower):
    inverse = jnp.eye(SPAN, dtype=jnp.float32) - strictly_lower
    power = jnp.matmul(strictly_lower, strictly_lower, precision=FULL_PRECISION)
    covered = 2
    while covered < SPAN:
        if 2 * covered < SPAN:
            both = jnp.matmul(
                jnp.concatenate([inverse, power], axis=-2), power, precision=FULL_PRECISION
            )
            inverse = inverse + both[..., :SPAN, :]
            power = both[..., SPAN:, :]
        else:
            inverse = inverse + jnp.matmul(inverse, power, precision=FULL_PRECISION)
        covered = covered * 2
    return inverse


def span_pass(key_unit, value_f, beta_gate, decay_log, group_size):
    rowpos = lax.broadcasted_iota(jnp.int32, (SPAN, SPAN), 0)
    colpos = lax.broadcasted_iota(jnp.int32, (SPAN, SPAN), 1)
    cum_log = jnp.cumsum(decay_log, axis=2)
    spread = cum_log[..., :, None] - cum_log[..., None, :]
    strict = jnp.exp(jnp.where(colpos < rowpos, spread, -jnp.inf))
    key_inner = jnp.repeat(
        jnp.einsum("hmik,hmjk->hmij", key_unit, key_unit, precision=FULL_PRECISION),
        group_size,
        axis=0,
    )
    inverse = unit_lower_inverse(beta_gate[..., :, None] * strict * key_inner)
    wide_keys = jnp.repeat(key_unit, group_size, axis=0)
    targets = jnp.concatenate(
        [beta_gate[..., None] * value_f, (beta_gate * jnp.exp(cum_log))[..., None] * wide_keys],
        axis=-1,
    )
    solved = jnp.matmul(inverse, targets, precision=FULL_PRECISION)
    written = solved[..., :DV]
    weights = solved[..., DV:]
    faded_keys = wide_keys * jnp.exp(cum_log[..., -1:] - cum_log)[..., None]
    tail_decay = jnp.exp(cum_log[..., -1])
    carry_mat = tail_decay[..., None, None] * jnp.eye(DK, dtype=jnp.float32) - jnp.einsum(
        "hmck,hmcj->hmkj", faded_keys, weights, precision=FULL_PRECISION
    )
    write_mat = jnp.einsum("hmck,hmcv->hmkv", faded_keys, written, precision=FULL_PRECISION)
    return (cum_log, spread, written, weights, carry_mat, write_mat)


def span_prep(query_unit, key_unit, group_size, pieces):
    cum_log, spread, written, weights, carry_mat, write_mat = pieces
    rowpos = lax.broadcasted_iota(jnp.int32, (SPAN, SPAN), 0)
    colpos = lax.broadcasted_iota(jnp.int32, (SPAN, SPAN), 1)
    within = jnp.exp(jnp.where(colpos <= rowpos, spread, -jnp.inf))
    scores = (
        jnp.repeat(
            jnp.einsum("hmik,hmjk->hmij", query_unit, key_unit, precision=FULL_PRECISION),
            group_size,
            axis=0,
        )
        * within
    )
    wide_query = jnp.repeat(query_unit, group_size, axis=0)
    inner = jnp.einsum("hmij,hmjv->hmiv", scores, written, precision=FULL_PRECISION)
    reach = wide_query * jnp.exp(cum_log)[..., None] - jnp.einsum(
        "hmij,hmjk->hmik", scores, weights, precision=FULL_PRECISION
    )
    head_count, blocks = (carry_mat.shape[0], carry_mat.shape[1])
    reach_map = jnp.broadcast_to(jnp.eye(DK, dtype=jnp.float32), (head_count, DK, DK))
    reach_add = jnp.zeros((head_count, DK, DV), jnp.float32)
    fixed, scaled = ([], [])
    for m in range(blocks):
        if m == 0:
            fixed.append(inner[:, m])
            scaled.append(reach[:, m])
        else:
            fixed.append(
                inner[:, m]
                + jnp.matmul(reach[:, m], reach_add, precision=FULL_PRECISION)
            )
            scaled.append(jnp.matmul(reach[:, m], reach_map, precision=FULL_PRECISION))
        reach_map, reach_add = compose((reach_map, reach_add), (carry_mat[:, m], write_mat[:, m]))
    return (jnp.stack(fixed, axis=1), jnp.stack(scaled, axis=1), reach_map, reach_add)


def span_out(fixed, scaled, state_in):
    return fixed + jnp.einsum("hmck,hkv->hmcv", scaled, state_in, precision=FULL_PRECISION)


def to_rows(core_out):
    head_count, blocks = (core_out.shape[0], core_out.shape[1])
    return core_out.transpose(1, 2, 0, 3).reshape(blocks * SPAN, head_count * DV)


def joined(carry, write):
    return jnp.concatenate([carry, write], axis=-1)


def inclusive_scan(carry, write, size, stride):
    count = size // stride
    shift = 1
    while shift < count:
        pairs = [(i, i + shift * stride) for i in range(size - shift * stride)]
        if 2 * shift < count:
            got = lax.ppermute(joined(carry, write), "ctx", pairs)
            carry, write = compose((got[..., :DK], got[..., DK:]), (carry, write))
        else:
            got = lax.ppermute(write, "ctx", pairs)
            write = jnp.matmul(carry, got, precision=FULL_PRECISION) + write
        shift *= 2
    return write


def chain_states(block_carry, block_write):
    size = lax.axis_size("ctx")
    head_count = block_carry.shape[0]
    if size % 2 or head_count % 2:
        write = inclusive_scan(block_carry, block_write, size, 1)
        return lax.ppermute(write, "ctx", [(i, i + 1) for i in range(size - 1)])
    half = head_count // 2
    odd = lax.axis_index("ctx") % 2 == 1
    both = joined(block_carry, block_write)
    mine = jnp.where(odd, both[half:], both[:half])
    other = jnp.where(odd, both[:half], both[half:])
    swap = [(i, i ^ 1) for i in range(size)]
    got = lax.ppermute(other, "ctx", swap)
    earlier = jnp.where(odd, got, mine)
    later = jnp.where(odd, mine, got)
    pair_carry, pair_write = compose(
        (earlier[..., :DK], earlier[..., DK:]), (later[..., :DK], later[..., DK:])
    )
    pair_write = inclusive_scan(pair_carry, pair_write, size, 2)
    from_odd = lax.ppermute(pair_write, "ctx", [(i, i + 1) for i in range(1, size - 1, 2)])
    from_even = lax.ppermute(pair_write, "ctx", [(i, i + 2) for i in range(0, size - 2, 2)])
    even_state = jnp.concatenate([from_even, from_odd], axis=0)
    odd_state = (
        jnp.matmul(block_carry, even_state, precision=FULL_PRECISION) + block_write
    )
    odd_state = lax.ppermute(odd_state, "ctx", [(i, i + 1) for i in range(0, size, 2)])
    return jnp.where(odd, odd_state, even_state)


def gated_norm(core_rows, output_gate, norm_gain):
    token_count = core_rows.shape[0]
    head_count = core_rows.shape[1] // DV
    core_f = core_rows.astype(jnp.float32).reshape(token_count, head_count, DV)
    inv_rms = lax.rsqrt(jnp.mean(core_f * core_f, axis=-1, keepdims=True) + 1e-06)
    gate_f = output_gate.astype(jnp.float32).reshape(token_count, head_count, DV)
    gated_rows = core_f * inv_rms * norm_gain.astype(jnp.float32) * jax.nn.silu(gate_f)
    return gated_rows.reshape(token_count, head_count * DV).astype(jnp.bfloat16)


def on_device(query_rows, key_rows, value_rows, output_gate, beta_logit, log_decay, norm_gain):
    parts = lax.axis_size("head")
    tokens = query_rows.shape[0]
    pieces_in = [query_rows, key_rows, value_rows, beta_logit, log_decay]
    widths = [part.shape[1] // parts for part in pieces_in]
    packed = jnp.concatenate(
        [part.reshape(tokens, parts, width) for part, width in zip(pieces_in, widths)], axis=-1
    )
    packed = lax.all_to_all(packed, "head", split_axis=1, concat_axis=0, tiled=True)
    packed = packed.reshape(tokens * parts, sum(widths))
    ends = [sum(widths[: i + 1]) for i in range(len(widths))]
    q_head, k_head, v_head, b_head, d_head = (
        packed[:, end - width : end] for end, width in zip(ends, widths)
    )
    key_unit, value_f, beta_gate, decay_log = arrange(k_head, v_head, b_head, d_head)
    group_size = value_f.shape[0] // key_unit.shape[0]
    pieces = span_pass(key_unit, value_f, beta_gate, decay_log, group_size)
    query_unit = arrange_query(q_head)
    fixed, scaled, total_carry, total_write = span_prep(query_unit, key_unit, group_size, pieces)
    state_in = chain_states(total_carry, total_write)
    core_out = span_out(fixed, scaled, state_in)
    core_rows = lax.all_to_all(
        to_rows(core_out).astype(jnp.bfloat16), "head", split_axis=0, concat_axis=1, tiled=True
    )
    return gated_norm(core_rows, output_gate, norm_gain)


def solution(mesh):
    placed = (
        P(("ctx", "head"), None),
        P(("ctx", "head"), None),
        P(("ctx", "head"), None),
        P(("ctx", "head"), None),
        P(("ctx", "head"), None),
        P(("ctx", "head"), None),
        P(),
    )
    return jax.shard_map(
        on_device, mesh=mesh, in_specs=placed, out_specs=P(("ctx", "head"), None), check_vma=False
    )
```

```python
import jax
import jax.numpy as jnp
from jax import lax
from jax.sharding import PartitionSpec as P

DK = 128
DV = 128
SPAN = 128


FULL_PRECISION = lax.Precision.HIGHEST
LOCAL_PRECISION = lax.Precision.HIGH


def unit_rows(rows):
    return rows * lax.rsqrt(jnp.sum(rows * rows, axis=-1, keepdims=True) + 1e-06)


def compose(earlier, later):
    return (
        jnp.matmul(later[0], earlier[0], precision=FULL_PRECISION),
        jnp.matmul(later[0], earlier[1], precision=FULL_PRECISION) + later[1],
    )


def arrange(key_part, value_part, beta_part, decay_part):
    blocks = key_part.shape[0] // SPAN
    key_heads = key_part.shape[1] // DK
    value_heads = value_part.shape[1] // DV
    key_unit = unit_rows(
        key_part.astype(jnp.float32).reshape(blocks, SPAN, key_heads, DK)
    ).transpose(2, 0, 1, 3)
    value_f = (
        value_part.astype(jnp.float32).reshape(blocks, SPAN, value_heads, DV).transpose(2, 0, 1, 3)
    )
    beta_gate = (
        jax.nn.sigmoid(beta_part.astype(jnp.float32))
        .reshape(blocks, SPAN, value_heads)
        .transpose(2, 0, 1)
    )
    decay_log = decay_part.astype(jnp.float32).reshape(blocks, SPAN, value_heads).transpose(2, 0, 1)
    return (key_unit, value_f, beta_gate, decay_log)


def arrange_query(query_part):
    blocks = query_part.shape[0] // SPAN
    key_heads = query_part.shape[1] // DK
    query_f = query_part.astype(jnp.float32).reshape(blocks, SPAN, key_heads, DK)
    return (unit_rows(query_f) * DK ** (-0.5)).transpose(2, 0, 1, 3)


def unit_lower_inverse(strictly_lower):
    inverse = jnp.eye(SPAN, dtype=jnp.float32) - strictly_lower
    power = jnp.matmul(strictly_lower, strictly_lower, precision=LOCAL_PRECISION)
    covered = 2
    while covered < SPAN:
        if 2 * covered < SPAN:
            both = jnp.matmul(
                jnp.concatenate([inverse, power], axis=-2), power, precision=LOCAL_PRECISION
            )
            inverse = inverse + both[..., :SPAN, :]
            power = both[..., SPAN:, :]
        else:
            inverse = inverse + jnp.matmul(inverse, power, precision=LOCAL_PRECISION)
        covered = covered * 2
    return inverse


def span_pass(key_unit, value_f, beta_gate, decay_log, group_size):
    rowpos = lax.broadcasted_iota(jnp.int32, (SPAN, SPAN), 0)
    colpos = lax.broadcasted_iota(jnp.int32, (SPAN, SPAN), 1)
    cum_log = jnp.cumsum(decay_log, axis=2)
    spread = cum_log[..., :, None] - cum_log[..., None, :]
    strict = jnp.exp(jnp.where(colpos < rowpos, spread, -jnp.inf))
    key_inner = jnp.repeat(
        jnp.einsum("hmik,hmjk->hmij", key_unit, key_unit, precision=LOCAL_PRECISION),
        group_size,
        axis=0,
    )
    inverse = unit_lower_inverse(beta_gate[..., :, None] * strict * key_inner)
    wide_keys = jnp.repeat(key_unit, group_size, axis=0)
    targets = jnp.concatenate(
        [beta_gate[..., None] * value_f, (beta_gate * jnp.exp(cum_log))[..., None] * wide_keys],
        axis=-1,
    )
    solved = jnp.matmul(inverse, targets, precision=LOCAL_PRECISION)
    written = solved[..., :DV]
    weights = solved[..., DV:]
    faded_keys = wide_keys * jnp.exp(cum_log[..., -1:] - cum_log)[..., None]
    tail_decay = jnp.exp(cum_log[..., -1])
    carry_mat = tail_decay[..., None, None] * jnp.eye(DK, dtype=jnp.float32) - jnp.einsum(
        "hmck,hmcj->hmkj", faded_keys, weights, precision=LOCAL_PRECISION
    )
    write_mat = jnp.einsum("hmck,hmcv->hmkv", faded_keys, written, precision=LOCAL_PRECISION)
    return (cum_log, spread, written, weights, carry_mat, write_mat)


def span_prep(query_unit, key_unit, group_size, pieces):
    cum_log, spread, written, weights, carry_mat, write_mat = pieces
    rowpos = lax.broadcasted_iota(jnp.int32, (SPAN, SPAN), 0)
    colpos = lax.broadcasted_iota(jnp.int32, (SPAN, SPAN), 1)
    within = jnp.exp(jnp.where(colpos <= rowpos, spread, -jnp.inf))
    scores = (
        jnp.repeat(
            jnp.einsum("hmik,hmjk->hmij", query_unit, key_unit, precision=LOCAL_PRECISION),
            group_size,
            axis=0,
        )
        * within
    )
    wide_query = jnp.repeat(query_unit, group_size, axis=0)
    inner = jnp.einsum("hmij,hmjv->hmiv", scores, written, precision=LOCAL_PRECISION)
    reach = wide_query * jnp.exp(cum_log)[..., None] - jnp.einsum(
        "hmij,hmjk->hmik", scores, weights, precision=LOCAL_PRECISION
    )
    head_count, blocks = (carry_mat.shape[0], carry_mat.shape[1])
    reach_map = jnp.broadcast_to(jnp.eye(DK, dtype=jnp.float32), (head_count, DK, DK))
    reach_add = jnp.zeros((head_count, DK, DV), jnp.float32)
    fixed, scaled = ([], [])
    for m in range(blocks):
        if m == 0:
            fixed.append(inner[:, m])
            scaled.append(reach[:, m])
        else:
            fixed.append(
                inner[:, m]
                + jnp.matmul(reach[:, m], reach_add, precision=LOCAL_PRECISION)
            )
            scaled.append(jnp.matmul(reach[:, m], reach_map, precision=LOCAL_PRECISION))
        reach_map, reach_add = compose((reach_map, reach_add), (carry_mat[:, m], write_mat[:, m]))
    return (jnp.stack(fixed, axis=1), jnp.stack(scaled, axis=1), reach_map, reach_add)


def span_out(fixed, scaled, state_in):
    return fixed + jnp.einsum("hmck,hkv->hmcv", scaled, state_in, precision=FULL_PRECISION)


def to_rows(core_out):
    head_count, blocks = (core_out.shape[0], core_out.shape[1])
    return core_out.transpose(1, 2, 0, 3).reshape(blocks * SPAN, head_count * DV)


def joined(carry, write):
    return jnp.concatenate([carry, write], axis=-1)


def inclusive_scan(carry, write, size, stride):
    count = size // stride
    shift = 1
    while shift < count:
        pairs = [(i, i + shift * stride) for i in range(size - shift * stride)]
        if 2 * shift < count:
            got = lax.ppermute(joined(carry, write), "ctx", pairs)
            carry, write = compose((got[..., :DK], got[..., DK:]), (carry, write))
        else:
            got = lax.ppermute(write, "ctx", pairs)
            write = jnp.matmul(carry, got, precision=FULL_PRECISION) + write
        shift *= 2
    return write


def chain_states(block_carry, block_write):
    size = lax.axis_size("ctx")
    head_count = block_carry.shape[0]
    if size % 2 or head_count % 2:
        write = inclusive_scan(block_carry, block_write, size, 1)
        return lax.ppermute(write, "ctx", [(i, i + 1) for i in range(size - 1)])
    half = head_count // 2
    odd = lax.axis_index("ctx") % 2 == 1
    both = joined(block_carry, block_write)
    mine = jnp.where(odd, both[half:], both[:half])
    other = jnp.where(odd, both[:half], both[half:])
    swap = [(i, i ^ 1) for i in range(size)]
    got = lax.ppermute(other, "ctx", swap)
    earlier = jnp.where(odd, got, mine)
    later = jnp.where(odd, mine, got)
    pair_carry, pair_write = compose(
        (earlier[..., :DK], earlier[..., DK:]), (later[..., :DK], later[..., DK:])
    )
    pair_write = inclusive_scan(pair_carry, pair_write, size, 2)
    from_odd = lax.ppermute(pair_write, "ctx", [(i, i + 1) for i in range(1, size - 1, 2)])
    from_even = lax.ppermute(pair_write, "ctx", [(i, i + 2) for i in range(0, size - 2, 2)])
    even_state = jnp.concatenate([from_even, from_odd], axis=0)
    odd_state = (
        jnp.matmul(block_carry, even_state, precision=FULL_PRECISION) + block_write
    )
    odd_state = lax.ppermute(odd_state, "ctx", [(i, i + 1) for i in range(0, size, 2)])
    return jnp.where(odd, odd_state, even_state)


def gated_norm(core_rows, output_gate, norm_gain):
    token_count = core_rows.shape[0]
    head_count = core_rows.shape[1] // DV
    core_f = core_rows.astype(jnp.float32).reshape(token_count, head_count, DV)
    inv_rms = lax.rsqrt(jnp.mean(core_f * core_f, axis=-1, keepdims=True) + 1e-06)
    gate_f = output_gate.astype(jnp.float32).reshape(token_count, head_count, DV)
    gated_rows = core_f * inv_rms * norm_gain.astype(jnp.float32) * jax.nn.silu(gate_f)
    return gated_rows.reshape(token_count, head_count * DV).astype(jnp.bfloat16)


def on_device(query_rows, key_rows, value_rows, output_gate, beta_logit, log_decay, norm_gain):
    parts = lax.axis_size("head")
    tokens = query_rows.shape[0]
    pieces_in = [query_rows, key_rows, value_rows, beta_logit, log_decay]
    widths = [part.shape[1] // parts for part in pieces_in]
    packed = jnp.concatenate(
        [part.reshape(tokens, parts, width) for part, width in zip(pieces_in, widths)], axis=-1
    )
    packed = lax.all_to_all(packed, "head", split_axis=1, concat_axis=0, tiled=True)
    packed = packed.reshape(tokens * parts, sum(widths))
    ends = [sum(widths[: i + 1]) for i in range(len(widths))]
    q_head, k_head, v_head, b_head, d_head = (
        packed[:, end - width : end] for end, width in zip(ends, widths)
    )
    key_unit, value_f, beta_gate, decay_log = arrange(k_head, v_head, b_head, d_head)
    group_size = value_f.shape[0] // key_unit.shape[0]
    pieces = span_pass(key_unit, value_f, beta_gate, decay_log, group_size)
    query_unit = arrange_query(q_head)
    fixed, scaled, total_carry, total_write = span_prep(query_unit, key_unit, group_size, pieces)
    state_in = chain_states(total_carry, total_write)
    core_out = span_out(fixed, scaled, state_in)
    core_rows = lax.all_to_all(
        to_rows(core_out).astype(jnp.bfloat16), "head", split_axis=0, concat_axis=1, tiled=True
    )
    return gated_norm(core_rows, output_gate, norm_gain)


def solution(mesh):
    placed = (
        P(("ctx", "head"), None),
        P(("ctx", "head"), None),
        P(("ctx", "head"), None),
        P(("ctx", "head"), None),
        P(("ctx", "head"), None),
        P(("ctx", "head"), None),
        P(),
    )
    return jax.shard_map(
        on_device, mesh=mesh, in_specs=placed, out_specs=P(("ctx", "head"), None), check_vma=False
    )
```

```python
import jax
import jax.numpy as jnp
from jax import lax
from jax.sharding import PartitionSpec as P

DK = 128
DV = 128
SPAN = 128


FULL_PRECISION = lax.Precision.HIGHEST
LOCAL_PRECISION = lax.Precision.HIGH


def unit_rows(rows):
    return rows * lax.rsqrt(jnp.sum(rows * rows, axis=-1, keepdims=True) + 1e-06)


def compose(earlier, later):
    return (
        jnp.matmul(later[0], earlier[0], precision=FULL_PRECISION),
        jnp.matmul(later[0], earlier[1], precision=FULL_PRECISION) + later[1],
    )


def arrange(key_part, value_part, beta_part, decay_part):
    blocks = key_part.shape[0] // SPAN
    key_heads = key_part.shape[1] // DK
    value_heads = value_part.shape[1] // DV
    key_unit = unit_rows(
        key_part.astype(jnp.float32).reshape(blocks, SPAN, key_heads, DK)
    ).transpose(2, 0, 1, 3)
    value_f = (
        value_part.astype(jnp.float32).reshape(blocks, SPAN, value_heads, DV).transpose(2, 0, 1, 3)
    )
    beta_gate = (
        jax.nn.sigmoid(beta_part.astype(jnp.float32))
        .reshape(blocks, SPAN, value_heads)
        .transpose(2, 0, 1)
    )
    decay_log = decay_part.astype(jnp.float32).reshape(blocks, SPAN, value_heads).transpose(2, 0, 1)
    return (key_unit, value_f, beta_gate, decay_log)


def arrange_query(query_part):
    blocks = query_part.shape[0] // SPAN
    key_heads = query_part.shape[1] // DK
    query_f = query_part.astype(jnp.float32).reshape(blocks, SPAN, key_heads, DK)
    return (unit_rows(query_f) * DK ** (-0.5)).transpose(2, 0, 1, 3)


def unit_lower_inverse(strictly_lower):
    inverse = jnp.eye(SPAN, dtype=jnp.float32) - strictly_lower
    power = jnp.matmul(strictly_lower, strictly_lower, precision=LOCAL_PRECISION)
    covered = 2
    while covered < SPAN:
        if 2 * covered < SPAN:
            both = jnp.matmul(
                jnp.concatenate([inverse, power], axis=-2), power, precision=LOCAL_PRECISION
            )
            inverse = inverse + both[..., :SPAN, :]
            power = both[..., SPAN:, :]
        else:
            inverse = inverse + jnp.matmul(inverse, power, precision=LOCAL_PRECISION)
        covered = covered * 2
    return inverse


def span_pass(key_unit, value_f, beta_gate, decay_log, group_size):
    rowpos = lax.broadcasted_iota(jnp.int32, (SPAN, SPAN), 0)
    colpos = lax.broadcasted_iota(jnp.int32, (SPAN, SPAN), 1)
    cum_log = jnp.cumsum(decay_log, axis=2)
    spread = cum_log[..., :, None] - cum_log[..., None, :]
    strict = jnp.exp(jnp.where(colpos < rowpos, spread, -jnp.inf))
    key_inner = jnp.repeat(
        jnp.einsum("hmik,hmjk->hmij", key_unit, key_unit, precision=LOCAL_PRECISION),
        group_size,
        axis=0,
    )
    inverse = unit_lower_inverse(beta_gate[..., :, None] * strict * key_inner)
    wide_keys = jnp.repeat(key_unit, group_size, axis=0)
    targets = jnp.concatenate(
        [beta_gate[..., None] * value_f, (beta_gate * jnp.exp(cum_log))[..., None] * wide_keys],
        axis=-1,
    )
    solved = jnp.matmul(inverse, targets, precision=LOCAL_PRECISION)
    written = solved[..., :DV]
    weights = solved[..., DV:]
    faded_keys = wide_keys * jnp.exp(cum_log[..., -1:] - cum_log)[..., None]
    tail_decay = jnp.exp(cum_log[..., -1])
    carry_mat = tail_decay[..., None, None] * jnp.eye(DK, dtype=jnp.float32) - jnp.einsum(
        "hmck,hmcj->hmkj", faded_keys, weights, precision=LOCAL_PRECISION
    )
    write_mat = jnp.einsum("hmck,hmcv->hmkv", faded_keys, written, precision=LOCAL_PRECISION)
    return (cum_log, spread, written, weights, carry_mat, write_mat)


def span_prep(query_unit, key_unit, group_size, pieces):
    cum_log, spread, written, weights, carry_mat, write_mat = pieces
    rowpos = lax.broadcasted_iota(jnp.int32, (SPAN, SPAN), 0)
    colpos = lax.broadcasted_iota(jnp.int32, (SPAN, SPAN), 1)
    within = jnp.exp(jnp.where(colpos <= rowpos, spread, -jnp.inf))
    scores = (
        jnp.repeat(
            jnp.einsum("hmik,hmjk->hmij", query_unit, key_unit, precision=LOCAL_PRECISION),
            group_size,
            axis=0,
        )
        * within
    )
    wide_query = jnp.repeat(query_unit, group_size, axis=0)
    inner = jnp.einsum("hmij,hmjv->hmiv", scores, written, precision=LOCAL_PRECISION)
    reach = wide_query * jnp.exp(cum_log)[..., None] - jnp.einsum(
        "hmij,hmjk->hmik", scores, weights, precision=LOCAL_PRECISION
    )
    head_count, blocks = (carry_mat.shape[0], carry_mat.shape[1])
    reach_map = jnp.broadcast_to(jnp.eye(DK, dtype=jnp.float32), (head_count, DK, DK))
    reach_add = jnp.zeros((head_count, DK, DV), jnp.float32)
    fixed, scaled = ([], [])
    for m in range(blocks):
        if m == 0:
            fixed.append(inner[:, m])
            scaled.append(reach[:, m])
        else:
            fixed.append(
                inner[:, m]
                + jnp.matmul(reach[:, m], reach_add, precision=LOCAL_PRECISION)
            )
            scaled.append(jnp.matmul(reach[:, m], reach_map, precision=LOCAL_PRECISION))
        reach_map, reach_add = compose((reach_map, reach_add), (carry_mat[:, m], write_mat[:, m]))
    return (jnp.stack(fixed, axis=1), jnp.stack(scaled, axis=1), reach_map, reach_add)


def span_out(fixed, scaled, state_in):
    return fixed + jnp.einsum("hmck,hkv->hmcv", scaled, state_in, precision=FULL_PRECISION)


def to_rows(core_out):
    head_count, blocks = (core_out.shape[0], core_out.shape[1])
    return core_out.transpose(1, 2, 0, 3).reshape(blocks * SPAN, head_count * DV)


def joined(carry, write):
    return jnp.concatenate([carry, write], axis=-1)


def inclusive_scan(carry, write, size, stride):
    count = size // stride
    shift = 1
    while shift < count:
        pairs = [(i, i + shift * stride) for i in range(size - shift * stride)]
        if 2 * shift < count:
            got = lax.ppermute(joined(carry, write), "ctx", pairs)
            carry, write = compose((got[..., :DK], got[..., DK:]), (carry, write))
        else:
            got = lax.ppermute(write, "ctx", pairs)
            write = jnp.matmul(carry, got, precision=FULL_PRECISION) + write
        shift *= 2
    return write


def chain_states(block_carry, block_write):
    size = lax.axis_size("ctx")
    head_count = block_carry.shape[0]
    if size % 2 or head_count % 2:
        write = inclusive_scan(block_carry, block_write, size, 1)
        return lax.ppermute(write, "ctx", [(i, i + 1) for i in range(size - 1)])
    half = head_count // 2
    odd = lax.axis_index("ctx") % 2 == 1
    both = joined(block_carry, block_write)
    mine = jnp.where(odd, both[half:], both[:half])
    other = jnp.where(odd, both[:half], both[half:])
    swap = [(i, i ^ 1) for i in range(size)]
    got = lax.ppermute(other, "ctx", swap)
    earlier = jnp.where(odd, got, mine)
    later = jnp.where(odd, mine, got)
    pair_carry, pair_write = compose(
        (earlier[..., :DK], earlier[..., DK:]), (later[..., :DK], later[..., DK:])
    )
    pair_write = inclusive_scan(pair_carry, pair_write, size, 2)
    from_odd = lax.ppermute(pair_write, "ctx", [(i, i + 1) for i in range(1, size - 1, 2)])
    from_even = lax.ppermute(pair_write, "ctx", [(i, i + 2) for i in range(0, size - 2, 2)])
    even_state = jnp.concatenate([from_even, from_odd], axis=0)
    odd_state = (
        jnp.matmul(block_carry, even_state, precision=FULL_PRECISION) + block_write
    )
    odd_state = lax.ppermute(odd_state, "ctx", [(i, i + 1) for i in range(0, size, 2)])
    return jnp.where(odd, odd_state, even_state)


def gated_norm(core_rows, output_gate, norm_gain):
    token_count = core_rows.shape[0]
    head_count = core_rows.shape[1] // DV
    core_f = core_rows.astype(jnp.float32).reshape(token_count, head_count, DV)
    inv_rms = lax.rsqrt(jnp.mean(core_f * core_f, axis=-1, keepdims=True) + 1e-06)
    gate_f = output_gate.astype(jnp.float32).reshape(token_count, head_count, DV)
    gated_rows = core_f * inv_rms * norm_gain.astype(jnp.float32) * jax.nn.silu(gate_f)
    return gated_rows.reshape(token_count, head_count * DV).astype(jnp.bfloat16)


def head_swap(rows):
    width = rows.shape[1] // 2
    first = lax.axis_index("head") == 0
    own = jnp.where(first, rows[:, :width], rows[:, width:])
    sent = jnp.where(first, rows[:, width:], rows[:, :width])
    got = lax.ppermute(sent, "head", [(0, 1), (1, 0)])
    return jnp.where(first, jnp.concatenate([own, got], 0), jnp.concatenate([got, own], 0))


def head_return(rows):
    tokens = rows.shape[0] // 2
    first = lax.axis_index("head") == 0
    own = jnp.where(first, rows[:tokens], rows[tokens:])
    sent = jnp.where(first, rows[tokens:], rows[:tokens])
    got = lax.ppermute(sent, "head", [(0, 1), (1, 0)])
    return jnp.where(first, jnp.concatenate([own, got], 1), jnp.concatenate([got, own], 1))


def head_inputs(pieces_in):
    parts = lax.axis_size("head")
    if parts == 2:
        return [head_swap(part) for part in pieces_in]
    tokens = pieces_in[0].shape[0]
    widths = [part.shape[1] // parts for part in pieces_in]
    packed = jnp.concatenate(
        [part.reshape(tokens, parts, width) for part, width in zip(pieces_in, widths)], axis=-1
    )
    packed = lax.all_to_all(packed, "head", split_axis=1, concat_axis=0, tiled=True)
    packed = packed.reshape(tokens * parts, sum(widths))
    ends = [sum(widths[: i + 1]) for i in range(len(widths))]
    return [packed[:, end - width : end] for end, width in zip(ends, widths)]


def head_outputs(rows):
    if lax.axis_size("head") == 2:
        return head_return(rows)
    return lax.all_to_all(rows, "head", split_axis=0, concat_axis=1, tiled=True)


def on_device(query_rows, key_rows, value_rows, output_gate, beta_logit, log_decay, norm_gain):
    q_head, k_head, v_head, b_head, d_head = head_inputs(
        [query_rows, key_rows, value_rows, beta_logit, log_decay]
    )
    key_unit, value_f, beta_gate, decay_log = arrange(k_head, v_head, b_head, d_head)
    group_size = value_f.shape[0] // key_unit.shape[0]
    pieces = span_pass(key_unit, value_f, beta_gate, decay_log, group_size)
    query_unit = arrange_query(q_head)
    fixed, scaled, total_carry, total_write = span_prep(query_unit, key_unit, group_size, pieces)
    state_in = chain_states(total_carry, total_write)
    core_out = span_out(fixed, scaled, state_in)
    core_rows = head_outputs(to_rows(core_out).astype(jnp.bfloat16))
    return gated_norm(core_rows, output_gate, norm_gain)


def solution(mesh):
    placed = (
        P(("ctx", "head"), None),
        P(("ctx", "head"), None),
        P(("ctx", "head"), None),
        P(("ctx", "head"), None),
        P(("ctx", "head"), None),
        P(("ctx", "head"), None),
        P(),
    )
    return jax.shard_map(
        on_device, mesh=mesh, in_specs=placed, out_specs=P(("ctx", "head"), None), check_vma=False
    )
```

```python
import jax
import jax.numpy as jnp
from jax import lax
from jax.sharding import PartitionSpec as P

DK = 128
DV = 128
SPAN = 128


FULL_PRECISION = lax.Precision.HIGHEST
LOCAL_PRECISION = lax.Precision.HIGH


def unit_rows(rows):
    return rows * lax.rsqrt(jnp.sum(rows * rows, axis=-1, keepdims=True) + 1e-06)


def compose(earlier, later):
    return (
        jnp.matmul(later[0], earlier[0], precision=FULL_PRECISION),
        jnp.matmul(later[0], earlier[1], precision=FULL_PRECISION) + later[1],
    )


def arrange(key_part, value_part, beta_part, decay_part):
    blocks = key_part.shape[0] // SPAN
    key_heads = key_part.shape[1] // DK
    value_heads = value_part.shape[1] // DV
    key_unit = unit_rows(
        key_part.astype(jnp.float32).reshape(blocks, SPAN, key_heads, DK)
    ).transpose(2, 0, 1, 3)
    value_f = (
        value_part.astype(jnp.float32).reshape(blocks, SPAN, value_heads, DV).transpose(2, 0, 1, 3)
    )
    beta_gate = (
        jax.nn.sigmoid(beta_part.astype(jnp.float32))
        .reshape(blocks, SPAN, value_heads)
        .transpose(2, 0, 1)
    )
    decay_log = decay_part.astype(jnp.float32).reshape(blocks, SPAN, value_heads).transpose(2, 0, 1)
    return (key_unit, value_f, beta_gate, decay_log)


def arrange_query(query_part):
    blocks = query_part.shape[0] // SPAN
    key_heads = query_part.shape[1] // DK
    query_f = query_part.astype(jnp.float32).reshape(blocks, SPAN, key_heads, DK)
    return (unit_rows(query_f) * DK ** (-0.5)).transpose(2, 0, 1, 3)


def unit_lower_inverse(strictly_lower):
    inverse = jnp.eye(SPAN, dtype=jnp.float32) - strictly_lower
    power = jnp.matmul(strictly_lower, strictly_lower, precision=LOCAL_PRECISION)
    covered = 2
    while covered < SPAN:
        if 2 * covered < SPAN:
            both = jnp.matmul(
                jnp.concatenate([inverse, power], axis=-2), power, precision=LOCAL_PRECISION
            )
            inverse = inverse + both[..., :SPAN, :]
            power = both[..., SPAN:, :]
        else:
            inverse = inverse + jnp.matmul(inverse, power, precision=LOCAL_PRECISION)
        covered = covered * 2
    return inverse


def span_pass(key_unit, value_f, beta_gate, decay_log, group_size):
    rowpos = lax.broadcasted_iota(jnp.int32, (SPAN, SPAN), 0)
    colpos = lax.broadcasted_iota(jnp.int32, (SPAN, SPAN), 1)
    cum_log = jnp.cumsum(decay_log, axis=2)
    spread = cum_log[..., :, None] - cum_log[..., None, :]
    strict = jnp.exp(jnp.where(colpos < rowpos, spread, -jnp.inf))
    key_inner = jnp.repeat(
        jnp.einsum("hmik,hmjk->hmij", key_unit, key_unit, precision=LOCAL_PRECISION),
        group_size,
        axis=0,
    )
    inverse = unit_lower_inverse(beta_gate[..., :, None] * strict * key_inner)
    wide_keys = jnp.repeat(key_unit, group_size, axis=0)
    targets = jnp.concatenate(
        [beta_gate[..., None] * value_f, (beta_gate * jnp.exp(cum_log))[..., None] * wide_keys],
        axis=-1,
    )
    solved = jnp.matmul(inverse, targets, precision=LOCAL_PRECISION)
    written = solved[..., :DV]
    weights = solved[..., DV:]
    faded_keys = wide_keys * jnp.exp(cum_log[..., -1:] - cum_log)[..., None]
    tail_decay = jnp.exp(cum_log[..., -1])
    carry_mat = tail_decay[..., None, None] * jnp.eye(DK, dtype=jnp.float32) - jnp.einsum(
        "hmck,hmcj->hmkj", faded_keys, weights, precision=LOCAL_PRECISION
    )
    write_mat = jnp.einsum("hmck,hmcv->hmkv", faded_keys, written, precision=LOCAL_PRECISION)
    return (cum_log, spread, written, weights, carry_mat, write_mat)


def span_prep(query_unit, key_unit, group_size, pieces):
    cum_log, spread, written, weights, carry_mat, write_mat = pieces
    rowpos = lax.broadcasted_iota(jnp.int32, (SPAN, SPAN), 0)
    colpos = lax.broadcasted_iota(jnp.int32, (SPAN, SPAN), 1)
    within = jnp.exp(jnp.where(colpos <= rowpos, spread, -jnp.inf))
    scores = (
        jnp.repeat(
            jnp.einsum("hmik,hmjk->hmij", query_unit, key_unit, precision=LOCAL_PRECISION),
            group_size,
            axis=0,
        )
        * within
    )
    wide_query = jnp.repeat(query_unit, group_size, axis=0)
    inner = jnp.einsum("hmij,hmjv->hmiv", scores, written, precision=LOCAL_PRECISION)
    reach = wide_query * jnp.exp(cum_log)[..., None] - jnp.einsum(
        "hmij,hmjk->hmik", scores, weights, precision=LOCAL_PRECISION
    )
    head_count, blocks = (carry_mat.shape[0], carry_mat.shape[1])
    reach_map = jnp.broadcast_to(jnp.eye(DK, dtype=jnp.float32), (head_count, DK, DK))
    reach_add = jnp.zeros((head_count, DK, DV), jnp.float32)
    fixed, scaled = ([], [])
    for m in range(blocks):
        if m == 0:
            fixed.append(inner[:, m])
            scaled.append(reach[:, m])
        else:
            fixed.append(
                inner[:, m]
                + jnp.matmul(reach[:, m], reach_add, precision=LOCAL_PRECISION)
            )
            scaled.append(jnp.matmul(reach[:, m], reach_map, precision=LOCAL_PRECISION))
        reach_map, reach_add = compose((reach_map, reach_add), (carry_mat[:, m], write_mat[:, m]))
    return (jnp.stack(fixed, axis=1), jnp.stack(scaled, axis=1), reach_map, reach_add)


def span_out(fixed, scaled, state_in):
    return fixed + jnp.einsum("hmck,hkv->hmcv", scaled, state_in, precision=FULL_PRECISION)


def to_rows(core_out):
    head_count, blocks = (core_out.shape[0], core_out.shape[1])
    return core_out.transpose(1, 2, 0, 3).reshape(blocks * SPAN, head_count * DV)


def joined(carry, write):
    return jnp.concatenate([carry, write], axis=-1)


def split(both):
    return (both[..., :DK], both[..., DK:])


def exclusive_scan(carry, write, size, stride):
    count = size // stride
    if count == 1:
        return jnp.zeros_like(write)
    rounds = 0
    while 2 ** (rounds + 1) < count:
        rounds += 1
    shift = 1
    for _ in range(rounds):
        pairs = [(i, i + shift * stride) for i in range(size - shift * stride)]
        got = lax.ppermute(joined(carry, write), "ctx", pairs)
        carry, write = compose(split(got), (carry, write))
        shift *= 2
    near = [(i, i + stride) for i in range(size - stride)]
    far = 2**rounds + 1
    if far >= count:
        return lax.ppermute(write, "ctx", near)
    got_carry, got_write = split(lax.ppermute(joined(carry, write), "ctx", near))
    far_write = lax.ppermute(
        write, "ctx", [(i, i + far * stride) for i in range(size - far * stride)]
    )
    return jnp.matmul(got_carry, far_write, precision=FULL_PRECISION) + got_write


def chain_states(block_carry, block_write):
    size = lax.axis_size("ctx")
    me = lax.axis_index("ctx")
    levels = 0
    while size % 2 ** (levels + 1) == 0 and block_carry.shape[0] % 2 ** (levels + 1) == 0:
        levels += 1
    current = joined(block_carry, block_write)
    saved = []
    for level in range(levels):
        stride = 2**level
        upper = (me // stride) % 2 == 1
        half = current.shape[0] // 2
        mine = jnp.where(upper, current[half:], current[:half])
        other = jnp.where(upper, current[:half], current[half:])
        got = lax.ppermute(other, "ctx", [(i, i ^ stride) for i in range(size)])
        earlier = jnp.where(upper, got, mine)
        later = jnp.where(upper, mine, got)
        saved.append((upper, earlier))
        current = joined(*compose(split(earlier), split(later)))
    state = exclusive_scan(*split(current), size, 2**levels)
    for level in reversed(range(levels)):
        stride = 2**level
        upper, earlier = saved[level]
        earlier_carry, earlier_write = split(earlier)
        after = jnp.matmul(earlier_carry, state, precision=FULL_PRECISION) + earlier_write
        mine = jnp.where(upper, after, state)
        other = jnp.where(upper, state, after)
        got = lax.ppermute(other, "ctx", [(i, i ^ stride) for i in range(size)])
        state = jnp.where(
            upper, jnp.concatenate([got, mine], axis=0), jnp.concatenate([mine, got], axis=0)
        )
    return state


def gated_norm(core_rows, output_gate, norm_gain):
    token_count = core_rows.shape[0]
    head_count = core_rows.shape[1] // DV
    core_f = core_rows.astype(jnp.float32).reshape(token_count, head_count, DV)
    inv_rms = lax.rsqrt(jnp.mean(core_f * core_f, axis=-1, keepdims=True) + 1e-06)
    gate_f = output_gate.astype(jnp.float32).reshape(token_count, head_count, DV)
    gated_rows = core_f * inv_rms * norm_gain.astype(jnp.float32) * jax.nn.silu(gate_f)
    return gated_rows.reshape(token_count, head_count * DV).astype(jnp.bfloat16)


def head_swap(rows):
    width = rows.shape[1] // 2
    first = lax.axis_index("head") == 0
    own = jnp.where(first, rows[:, :width], rows[:, width:])
    sent = jnp.where(first, rows[:, width:], rows[:, :width])
    got = lax.ppermute(sent, "head", [(0, 1), (1, 0)])
    return jnp.where(first, jnp.concatenate([own, got], 0), jnp.concatenate([got, own], 0))


def head_return(rows):
    tokens = rows.shape[0] // 2
    first = lax.axis_index("head") == 0
    own = jnp.where(first, rows[:tokens], rows[tokens:])
    sent = jnp.where(first, rows[tokens:], rows[:tokens])
    got = lax.ppermute(sent, "head", [(0, 1), (1, 0)])
    return jnp.where(first, jnp.concatenate([own, got], 1), jnp.concatenate([got, own], 1))


def head_inputs(pieces_in):
    parts = lax.axis_size("head")
    if parts == 2:
        return [head_swap(part) for part in pieces_in]
    tokens = pieces_in[0].shape[0]
    widths = [part.shape[1] // parts for part in pieces_in]
    packed = jnp.concatenate(
        [part.reshape(tokens, parts, width) for part, width in zip(pieces_in, widths)], axis=-1
    )
    packed = lax.all_to_all(packed, "head", split_axis=1, concat_axis=0, tiled=True)
    packed = packed.reshape(tokens * parts, sum(widths))
    ends = [sum(widths[: i + 1]) for i in range(len(widths))]
    return [packed[:, end - width : end] for end, width in zip(ends, widths)]


def head_outputs(rows):
    if lax.axis_size("head") == 2:
        return head_return(rows)
    return lax.all_to_all(rows, "head", split_axis=0, concat_axis=1, tiled=True)


def on_device(query_rows, key_rows, value_rows, output_gate, beta_logit, log_decay, norm_gain):
    q_head, k_head, v_head, b_head, d_head = head_inputs(
        [query_rows, key_rows, value_rows, beta_logit, log_decay]
    )
    key_unit, value_f, beta_gate, decay_log = arrange(k_head, v_head, b_head, d_head)
    group_size = value_f.shape[0] // key_unit.shape[0]
    pieces = span_pass(key_unit, value_f, beta_gate, decay_log, group_size)
    query_unit = arrange_query(q_head)
    fixed, scaled, total_carry, total_write = span_prep(query_unit, key_unit, group_size, pieces)
    state_in = chain_states(total_carry, total_write)
    core_out = span_out(fixed, scaled, state_in)
    core_rows = head_outputs(to_rows(core_out).astype(jnp.bfloat16))
    return gated_norm(core_rows, output_gate, norm_gain)


def solution(mesh):
    placed = (
        P(("ctx", "head"), None),
        P(("ctx", "head"), None),
        P(("ctx", "head"), None),
        P(("ctx", "head"), None),
        P(("ctx", "head"), None),
        P(("ctx", "head"), None),
        P(),
    )
    return jax.shard_map(
        on_device, mesh=mesh, in_specs=placed, out_specs=P(("ctx", "head"), None), check_vma=False
    )
```

```python
import jax
import jax.numpy as jnp
from jax import lax
from jax.sharding import PartitionSpec as P

DK = 128
DV = 128
SPAN = 128


FULL_PRECISION = lax.Precision.HIGHEST
LOCAL_PRECISION = lax.Precision.HIGH


def unit_rows(rows):
    return rows * lax.rsqrt(jnp.sum(rows * rows, axis=-1, keepdims=True) + 1e-06)


def compose(earlier, later):
    return (
        jnp.matmul(later[0], earlier[0], precision=FULL_PRECISION),
        jnp.matmul(later[0], earlier[1], precision=FULL_PRECISION) + later[1],
    )


def arrange(key_part, value_part, beta_part, decay_part):
    blocks = key_part.shape[0] // SPAN
    key_heads = key_part.shape[1] // DK
    value_heads = value_part.shape[1] // DV
    key_unit = unit_rows(
        key_part.astype(jnp.float32).reshape(blocks, SPAN, key_heads, DK)
    ).transpose(2, 0, 1, 3)
    value_f = (
        value_part.astype(jnp.float32).reshape(blocks, SPAN, value_heads, DV).transpose(2, 0, 1, 3)
    )
    beta_gate = (
        jax.nn.sigmoid(beta_part.astype(jnp.float32))
        .reshape(blocks, SPAN, value_heads)
        .transpose(2, 0, 1)
    )
    decay_log = decay_part.astype(jnp.float32).reshape(blocks, SPAN, value_heads).transpose(2, 0, 1)
    return (key_unit, value_f, beta_gate, decay_log)


def arrange_query(query_part):
    blocks = query_part.shape[0] // SPAN
    key_heads = query_part.shape[1] // DK
    query_f = query_part.astype(jnp.float32).reshape(blocks, SPAN, key_heads, DK)
    return (unit_rows(query_f) * DK ** (-0.5)).transpose(2, 0, 1, 3)


def unit_lower_inverse(strictly_lower):
    inverse = jnp.eye(SPAN, dtype=jnp.float32) - strictly_lower
    power = jnp.matmul(strictly_lower, strictly_lower, precision=LOCAL_PRECISION)
    covered = 2
    while covered < SPAN:
        if 2 * covered < SPAN:
            both = jnp.matmul(
                jnp.concatenate([inverse, power], axis=-2), power, precision=LOCAL_PRECISION
            )
            inverse = inverse + both[..., :SPAN, :]
            power = both[..., SPAN:, :]
        else:
            inverse = inverse + jnp.matmul(inverse, power, precision=LOCAL_PRECISION)
        covered = covered * 2
    return inverse


def span_pass(key_unit, value_f, beta_gate, decay_log, group_size):
    rowpos = lax.broadcasted_iota(jnp.int32, (SPAN, SPAN), 0)
    colpos = lax.broadcasted_iota(jnp.int32, (SPAN, SPAN), 1)
    cum_log = jnp.cumsum(decay_log, axis=2)
    spread = cum_log[..., :, None] - cum_log[..., None, :]
    strict = jnp.exp(jnp.where(colpos < rowpos, spread, -jnp.inf))
    key_inner = jnp.repeat(
        jnp.einsum("hmik,hmjk->hmij", key_unit, key_unit, precision=LOCAL_PRECISION),
        group_size,
        axis=0,
    )
    inverse = unit_lower_inverse(beta_gate[..., :, None] * strict * key_inner)
    wide_keys = jnp.repeat(key_unit, group_size, axis=0)
    targets = jnp.concatenate(
        [beta_gate[..., None] * value_f, (beta_gate * jnp.exp(cum_log))[..., None] * wide_keys],
        axis=-1,
    )
    solved = jnp.matmul(inverse, targets, precision=LOCAL_PRECISION)
    written = solved[..., :DV]
    weights = solved[..., DV:]
    faded_keys = wide_keys * jnp.exp(cum_log[..., -1:] - cum_log)[..., None]
    tail_decay = jnp.exp(cum_log[..., -1])
    carry_mat = tail_decay[..., None, None] * jnp.eye(DK, dtype=jnp.float32) - jnp.einsum(
        "hmck,hmcj->hmkj", faded_keys, weights, precision=LOCAL_PRECISION
    )
    write_mat = jnp.einsum("hmck,hmcv->hmkv", faded_keys, written, precision=LOCAL_PRECISION)
    return (cum_log, spread, written, weights, carry_mat, write_mat)


def span_prep(query_unit, key_unit, group_size, pieces):
    cum_log, spread, written, weights, carry_mat, write_mat = pieces
    rowpos = lax.broadcasted_iota(jnp.int32, (SPAN, SPAN), 0)
    colpos = lax.broadcasted_iota(jnp.int32, (SPAN, SPAN), 1)
    within = jnp.exp(jnp.where(colpos <= rowpos, spread, -jnp.inf))
    scores = (
        jnp.repeat(
            jnp.einsum("hmik,hmjk->hmij", query_unit, key_unit, precision=LOCAL_PRECISION),
            group_size,
            axis=0,
        )
        * within
    )
    wide_query = jnp.repeat(query_unit, group_size, axis=0)
    inner = jnp.einsum("hmij,hmjv->hmiv", scores, written, precision=LOCAL_PRECISION)
    reach = wide_query * jnp.exp(cum_log)[..., None] - jnp.einsum(
        "hmij,hmjk->hmik", scores, weights, precision=LOCAL_PRECISION
    )
    head_count, blocks = (carry_mat.shape[0], carry_mat.shape[1])
    reach_map = jnp.broadcast_to(jnp.eye(DK, dtype=jnp.float32), (head_count, DK, DK))
    reach_add = jnp.zeros((head_count, DK, DV), jnp.float32)
    fixed, scaled = ([], [])
    for m in range(blocks):
        if m == 0:
            fixed.append(inner[:, m])
            scaled.append(reach[:, m])
        else:
            fixed.append(
                inner[:, m]
                + jnp.matmul(reach[:, m], reach_add, precision=LOCAL_PRECISION)
            )
            scaled.append(jnp.matmul(reach[:, m], reach_map, precision=LOCAL_PRECISION))
        reach_map, reach_add = compose((reach_map, reach_add), (carry_mat[:, m], write_mat[:, m]))
    return (jnp.stack(fixed, axis=1), jnp.stack(scaled, axis=1), reach_map, reach_add)


def span_out(fixed, scaled, state_in):
    return fixed + jnp.einsum("hmck,hkv->hmcv", scaled, state_in, precision=FULL_PRECISION)


def to_rows(core_out):
    head_count, blocks = (core_out.shape[0], core_out.shape[1])
    return core_out.transpose(1, 2, 0, 3).reshape(blocks * SPAN, head_count * DV)


def joined(carry, write):
    return jnp.concatenate([carry, write], axis=-1)


def split(both):
    return (both[..., :DK], both[..., DK:])


def exclusive_scan(carry, write, size, stride):
    count = size // stride
    if count == 1:
        return jnp.zeros_like(write)
    rounds = 0
    while 2 ** (rounds + 1) < count:
        rounds += 1
    shift = 1
    for _ in range(rounds):
        pairs = [(i, i + shift * stride) for i in range(size - shift * stride)]
        got = lax.ppermute(joined(carry, write), "ctx", pairs)
        carry, write = compose(split(got), (carry, write))
        shift *= 2
    near = [(i, i + stride) for i in range(size - stride)]
    far = 2**rounds + 1
    if far >= count:
        return lax.ppermute(write, "ctx", near)
    got_carry, got_write = split(lax.ppermute(joined(carry, write), "ctx", near))
    far_write = lax.ppermute(
        write, "ctx", [(i, i + far * stride) for i in range(size - far * stride)]
    )
    return jnp.matmul(got_carry, far_write, precision=FULL_PRECISION) + got_write


def chain_states(block_carry, block_write):
    size = lax.axis_size("ctx")
    me = lax.axis_index("ctx")
    levels = 0
    while size % 2 ** (levels + 1) == 0 and block_carry.shape[0] % 2 ** (levels + 1) == 0:
        levels += 1
    current = joined(block_carry, block_write)
    saved = []
    for level in range(levels):
        stride = 2**level
        upper = (me // stride) % 2 == 1
        half = current.shape[0] // 2
        bit = (me // stride) % 2
        mine = lax.dynamic_slice_in_dim(current, bit * half, half, 0)
        other = lax.dynamic_slice_in_dim(current, (1 - bit) * half, half, 0)
        got = lax.ppermute(other, "ctx", [(i, i ^ stride) for i in range(size)])
        earlier = jnp.where(upper, got, mine)
        later = jnp.where(upper, mine, got)
        saved.append((upper, earlier))
        current = joined(*compose(split(earlier), split(later)))
    state = exclusive_scan(*split(current), size, 2**levels)
    for level in reversed(range(levels)):
        stride = 2**level
        upper, earlier = saved[level]
        earlier_carry, earlier_write = split(earlier)
        after = jnp.matmul(earlier_carry, state, precision=FULL_PRECISION) + earlier_write
        mine = jnp.where(upper, after, state)
        other = jnp.where(upper, state, after)
        got = lax.ppermute(other, "ctx", [(i, i ^ stride) for i in range(size)])
        state = jnp.where(
            upper, jnp.concatenate([got, mine], axis=0), jnp.concatenate([mine, got], axis=0)
        )
    return state


def gated_norm(core_rows, output_gate, norm_gain):
    token_count = core_rows.shape[0]
    head_count = core_rows.shape[1] // DV
    core_f = core_rows.astype(jnp.float32).reshape(token_count, head_count, DV)
    inv_rms = lax.rsqrt(jnp.mean(core_f * core_f, axis=-1, keepdims=True) + 1e-06)
    gate_f = output_gate.astype(jnp.float32).reshape(token_count, head_count, DV)
    gated_rows = core_f * inv_rms * norm_gain.astype(jnp.float32) * jax.nn.silu(gate_f)
    return gated_rows.reshape(token_count, head_count * DV).astype(jnp.bfloat16)


def head_swap(pieces_in):
    half = lax.axis_index("head")
    widths = [part.shape[1] // 2 for part in pieces_in]
    own = jnp.concatenate(
        [lax.dynamic_slice_in_dim(p, half * w, w, 1) for p, w in zip(pieces_in, widths)], axis=1
    )
    sent = jnp.concatenate(
        [lax.dynamic_slice_in_dim(p, (1 - half) * w, w, 1) for p, w in zip(pieces_in, widths)],
        axis=1,
    )
    got = lax.ppermute(sent, "head", [(0, 1), (1, 0)])
    rows = jnp.where(half == 0, jnp.concatenate([own, got], 0), jnp.concatenate([got, own], 0))
    ends = [sum(widths[: i + 1]) for i in range(len(widths))]
    return [rows[:, end - w : end] for end, w in zip(ends, widths)]


def head_return(rows):
    tokens = rows.shape[0] // 2
    first = lax.axis_index("head") == 0
    own = jnp.where(first, rows[:tokens], rows[tokens:])
    sent = jnp.where(first, rows[tokens:], rows[:tokens])
    got = lax.ppermute(sent, "head", [(0, 1), (1, 0)])
    return jnp.where(first, jnp.concatenate([own, got], 1), jnp.concatenate([got, own], 1))


def head_inputs(pieces_in):
    parts = lax.axis_size("head")
    if parts == 2:
        wide = head_swap(pieces_in[:3])
        return wide + head_swap(pieces_in[3:])
    tokens = pieces_in[0].shape[0]
    widths = [part.shape[1] // parts for part in pieces_in]
    packed = jnp.concatenate(
        [part.reshape(tokens, parts, width) for part, width in zip(pieces_in, widths)], axis=-1
    )
    packed = lax.all_to_all(packed, "head", split_axis=1, concat_axis=0, tiled=True)
    packed = packed.reshape(tokens * parts, sum(widths))
    ends = [sum(widths[: i + 1]) for i in range(len(widths))]
    return [packed[:, end - width : end] for end, width in zip(ends, widths)]


def head_outputs(rows):
    if lax.axis_size("head") == 2:
        return head_return(rows)
    return lax.all_to_all(rows, "head", split_axis=0, concat_axis=1, tiled=True)


def on_device(query_rows, key_rows, value_rows, output_gate, beta_logit, log_decay, norm_gain):
    q_head, k_head, v_head, b_head, d_head = head_inputs(
        [query_rows, key_rows, value_rows, beta_logit, log_decay]
    )
    key_unit, value_f, beta_gate, decay_log = arrange(k_head, v_head, b_head, d_head)
    group_size = value_f.shape[0] // key_unit.shape[0]
    pieces = span_pass(key_unit, value_f, beta_gate, decay_log, group_size)
    query_unit = arrange_query(q_head)
    fixed, scaled, total_carry, total_write = span_prep(query_unit, key_unit, group_size, pieces)
    state_in = chain_states(total_carry, total_write)
    core_out = span_out(fixed, scaled, state_in)
    core_rows = head_outputs(to_rows(core_out).astype(jnp.bfloat16))
    return gated_norm(core_rows, output_gate, norm_gain)


def solution(mesh):
    placed = (
        P(("ctx", "head"), None),
        P(("ctx", "head"), None),
        P(("ctx", "head"), None),
        P(("ctx", "head"), None),
        P(("ctx", "head"), None),
        P(("ctx", "head"), None),
        P(),
    )
    return jax.shard_map(
        on_device, mesh=mesh, in_specs=placed, out_specs=P(("ctx", "head"), None), check_vma=False
    )
```

```python
import jax
import jax.numpy as jnp
from jax import lax
from jax.sharding import PartitionSpec as P

DK = 128
DV = 128
SPAN = 128


FULL_PRECISION = lax.Precision.HIGHEST
LOCAL_PRECISION = lax.Precision.HIGH


def unit_rows(rows):
    return rows * lax.rsqrt(jnp.sum(rows * rows, axis=-1, keepdims=True) + 1e-06)


def compose(earlier, later):
    return (
        jnp.matmul(later[0], earlier[0], precision=FULL_PRECISION),
        jnp.matmul(later[0], earlier[1], precision=FULL_PRECISION) + later[1],
    )


def arrange(key_part, value_part, beta_part, decay_part):
    blocks = key_part.shape[0] // SPAN
    key_heads = key_part.shape[1] // DK
    value_heads = value_part.shape[1] // DV
    key_unit = unit_rows(
        key_part.astype(jnp.float32).reshape(blocks, SPAN, key_heads, DK)
    ).transpose(2, 0, 1, 3)
    value_f = (
        value_part.astype(jnp.float32).reshape(blocks, SPAN, value_heads, DV).transpose(2, 0, 1, 3)
    )
    beta_gate = (
        jax.nn.sigmoid(beta_part.astype(jnp.float32))
        .reshape(blocks, SPAN, value_heads)
        .transpose(2, 0, 1)
    )
    decay_log = decay_part.astype(jnp.float32).reshape(blocks, SPAN, value_heads).transpose(2, 0, 1)
    return (key_unit, value_f, beta_gate, decay_log)


def arrange_query(query_part):
    blocks = query_part.shape[0] // SPAN
    key_heads = query_part.shape[1] // DK
    query_f = query_part.astype(jnp.float32).reshape(blocks, SPAN, key_heads, DK)
    return (unit_rows(query_f) * DK ** (-0.5)).transpose(2, 0, 1, 3)


def unit_lower_inverse(strictly_lower):
    inverse = jnp.eye(SPAN, dtype=jnp.float32) - strictly_lower
    power = jnp.matmul(strictly_lower, strictly_lower, precision=LOCAL_PRECISION)
    covered = 2
    while covered < SPAN:
        if 2 * covered < SPAN:
            both = jnp.matmul(
                jnp.concatenate([inverse, power], axis=-2), power, precision=LOCAL_PRECISION
            )
            inverse = inverse + both[..., :SPAN, :]
            power = both[..., SPAN:, :]
        else:
            inverse = inverse + jnp.matmul(inverse, power, precision=LOCAL_PRECISION)
        covered = covered * 2
    return inverse


def span_pass(key_unit, value_f, beta_gate, decay_log, group_size):
    rowpos = lax.broadcasted_iota(jnp.int32, (SPAN, SPAN), 0)
    colpos = lax.broadcasted_iota(jnp.int32, (SPAN, SPAN), 1)
    cum_log = jnp.cumsum(decay_log, axis=2)
    spread = cum_log[..., :, None] - cum_log[..., None, :]
    strict = jnp.exp(jnp.where(colpos < rowpos, spread, -jnp.inf))
    key_inner = jnp.repeat(
        jnp.einsum("hmik,hmjk->hmij", key_unit, key_unit, precision=LOCAL_PRECISION),
        group_size,
        axis=0,
    )
    inverse = unit_lower_inverse(beta_gate[..., :, None] * strict * key_inner)
    wide_keys = jnp.repeat(key_unit, group_size, axis=0)
    targets = jnp.concatenate(
        [beta_gate[..., None] * value_f, (beta_gate * jnp.exp(cum_log))[..., None] * wide_keys],
        axis=-1,
    )
    solved = jnp.matmul(inverse, targets, precision=LOCAL_PRECISION)
    written = solved[..., :DV]
    weights = solved[..., DV:]
    faded_keys = wide_keys * jnp.exp(cum_log[..., -1:] - cum_log)[..., None]
    tail_decay = jnp.exp(cum_log[..., -1])
    carry_mat = tail_decay[..., None, None] * jnp.eye(DK, dtype=jnp.float32) - jnp.einsum(
        "hmck,hmcj->hmkj", faded_keys, weights, precision=LOCAL_PRECISION
    )
    write_mat = jnp.einsum("hmck,hmcv->hmkv", faded_keys, written, precision=LOCAL_PRECISION)
    return (cum_log, spread, written, weights, carry_mat, write_mat)


def span_prep(query_unit, key_unit, group_size, pieces):
    cum_log, spread, written, weights, carry_mat, write_mat = pieces
    rowpos = lax.broadcasted_iota(jnp.int32, (SPAN, SPAN), 0)
    colpos = lax.broadcasted_iota(jnp.int32, (SPAN, SPAN), 1)
    within = jnp.exp(jnp.where(colpos <= rowpos, spread, -jnp.inf))
    scores = (
        jnp.repeat(
            jnp.einsum("hmik,hmjk->hmij", query_unit, key_unit, precision=LOCAL_PRECISION),
            group_size,
            axis=0,
        )
        * within
    )
    wide_query = jnp.repeat(query_unit, group_size, axis=0)
    inner = jnp.einsum("hmij,hmjv->hmiv", scores, written, precision=LOCAL_PRECISION)
    reach = wide_query * jnp.exp(cum_log)[..., None] - jnp.einsum(
        "hmij,hmjk->hmik", scores, weights, precision=LOCAL_PRECISION
    )
    blocks = carry_mat.shape[1]
    fixed, scaled = ([inner[:, 0]], [reach[:, 0]])
    reach_map, reach_add = (carry_mat[:, 0], write_mat[:, 0])
    for m in range(1, blocks):
        fixed.append(
            inner[:, m] + jnp.matmul(reach[:, m], reach_add, precision=LOCAL_PRECISION)
        )
        scaled.append(jnp.matmul(reach[:, m], reach_map, precision=LOCAL_PRECISION))
        reach_map, reach_add = compose((reach_map, reach_add), (carry_mat[:, m], write_mat[:, m]))
    return (jnp.stack(fixed, axis=1), jnp.stack(scaled, axis=1), reach_map, reach_add)


def span_out(fixed, scaled, state_in):
    return fixed + jnp.einsum("hmck,hkv->hmcv", scaled, state_in, precision=FULL_PRECISION)


def to_rows(core_out):
    head_count, blocks = (core_out.shape[0], core_out.shape[1])
    return core_out.transpose(1, 2, 0, 3).reshape(blocks * SPAN, head_count * DV)


def joined(carry, write):
    return jnp.concatenate([carry, write], axis=-1)


def split(both):
    return (both[..., :DK], both[..., DK:])


def exclusive_scan(carry, write, size, stride):
    count = size // stride
    if count == 1:
        return jnp.zeros_like(write)
    rounds = 0
    while 2 ** (rounds + 1) < count:
        rounds += 1
    shift = 1
    for _ in range(rounds):
        pairs = [(i, i + shift * stride) for i in range(size - shift * stride)]
        got = lax.ppermute(joined(carry, write), "ctx", pairs)
        carry, write = compose(split(got), (carry, write))
        shift *= 2
    near = [(i, i + stride) for i in range(size - stride)]
    far = 2**rounds + 1
    if far >= count:
        return lax.ppermute(write, "ctx", near)
    got_carry, got_write = split(lax.ppermute(joined(carry, write), "ctx", near))
    far_write = lax.ppermute(
        write, "ctx", [(i, i + far * stride) for i in range(size - far * stride)]
    )
    return jnp.matmul(got_carry, far_write, precision=FULL_PRECISION) + got_write


def chain_states(block_carry, block_write):
    size = lax.axis_size("ctx")
    me = lax.axis_index("ctx")
    levels = 0
    while size % 2 ** (levels + 1) == 0 and block_carry.shape[0] % 2 ** (levels + 1) == 0:
        levels += 1
    current = joined(block_carry, block_write)
    saved = []
    for level in range(levels):
        stride = 2**level
        upper = (me // stride) % 2 == 1
        half = current.shape[0] // 2
        mine = jnp.where(upper, current[half:], current[:half])
        other = jnp.where(upper, current[:half], current[half:])
        got = lax.ppermute(other, "ctx", [(i, i ^ stride) for i in range(size)])
        earlier = jnp.where(upper, got, mine)
        later = jnp.where(upper, mine, got)
        saved.append((upper, earlier))
        current = joined(*compose(split(earlier), split(later)))
    state = exclusive_scan(*split(current), size, 2**levels)
    for level in reversed(range(levels)):
        stride = 2**level
        upper, earlier = saved[level]
        earlier_carry, earlier_write = split(earlier)
        after = jnp.matmul(earlier_carry, state, precision=FULL_PRECISION) + earlier_write
        mine = jnp.where(upper, after, state)
        other = jnp.where(upper, state, after)
        got = lax.ppermute(other, "ctx", [(i, i ^ stride) for i in range(size)])
        state = jnp.where(
            upper, jnp.concatenate([got, mine], axis=0), jnp.concatenate([mine, got], axis=0)
        )
    return state


def gated_norm(core_rows, output_gate, norm_gain):
    token_count = core_rows.shape[0]
    head_count = core_rows.shape[1] // DV
    core_f = core_rows.astype(jnp.float32).reshape(token_count, head_count, DV)
    inv_rms = lax.rsqrt(jnp.mean(core_f * core_f, axis=-1, keepdims=True) + 1e-06)
    gate_f = output_gate.astype(jnp.float32).reshape(token_count, head_count, DV)
    gated_rows = core_f * inv_rms * norm_gain.astype(jnp.float32) * jax.nn.silu(gate_f)
    return gated_rows.reshape(token_count, head_count * DV).astype(jnp.bfloat16)


def head_swap(rows):
    width = rows.shape[1] // 2
    first = lax.axis_index("head") == 0
    own = jnp.where(first, rows[:, :width], rows[:, width:])
    sent = jnp.where(first, rows[:, width:], rows[:, :width])
    got = lax.ppermute(sent, "head", [(0, 1), (1, 0)])
    return jnp.where(first, jnp.concatenate([own, got], 0), jnp.concatenate([got, own], 0))


def head_return(rows):
    tokens = rows.shape[0] // 2
    first = lax.axis_index("head") == 0
    own = jnp.where(first, rows[:tokens], rows[tokens:])
    sent = jnp.where(first, rows[tokens:], rows[:tokens])
    got = lax.ppermute(sent, "head", [(0, 1), (1, 0)])
    return jnp.where(first, jnp.concatenate([own, got], 1), jnp.concatenate([got, own], 1))


def head_inputs(pieces_in):
    parts = lax.axis_size("head")
    if parts == 2:
        return [head_swap(part) for part in pieces_in]
    tokens = pieces_in[0].shape[0]
    widths = [part.shape[1] // parts for part in pieces_in]
    packed = jnp.concatenate(
        [part.reshape(tokens, parts, width) for part, width in zip(pieces_in, widths)], axis=-1
    )
    packed = lax.all_to_all(packed, "head", split_axis=1, concat_axis=0, tiled=True)
    packed = packed.reshape(tokens * parts, sum(widths))
    ends = [sum(widths[: i + 1]) for i in range(len(widths))]
    return [packed[:, end - width : end] for end, width in zip(ends, widths)]


def head_outputs(rows):
    if lax.axis_size("head") == 2:
        return head_return(rows)
    return lax.all_to_all(rows, "head", split_axis=0, concat_axis=1, tiled=True)


def on_device(query_rows, key_rows, value_rows, output_gate, beta_logit, log_decay, norm_gain):
    q_head, k_head, v_head, b_head, d_head = head_inputs(
        [query_rows, key_rows, value_rows, beta_logit, log_decay]
    )
    key_unit, value_f, beta_gate, decay_log = arrange(k_head, v_head, b_head, d_head)
    group_size = value_f.shape[0] // key_unit.shape[0]
    pieces = span_pass(key_unit, value_f, beta_gate, decay_log, group_size)
    query_unit = arrange_query(q_head)
    fixed, scaled, total_carry, total_write = span_prep(query_unit, key_unit, group_size, pieces)
    state_in = chain_states(total_carry, total_write)
    core_out = span_out(fixed, scaled, state_in)
    core_rows = head_outputs(to_rows(core_out).astype(jnp.bfloat16))
    return gated_norm(core_rows, output_gate, norm_gain)


def solution(mesh):
    placed = (
        P(("ctx", "head"), None),
        P(("ctx", "head"), None),
        P(("ctx", "head"), None),
        P(("ctx", "head"), None),
        P(("ctx", "head"), None),
        P(("ctx", "head"), None),
        P(),
    )
    return jax.shard_map(
        on_device, mesh=mesh, in_specs=placed, out_specs=P(("ctx", "head"), None), check_vma=False
    )
```

```python
import jax
import jax.numpy as jnp
from jax import lax
from jax.sharding import PartitionSpec as P

DK = 128
DV = 128
SPAN = 128


FULL_PRECISION = lax.Precision.HIGHEST
LOCAL_PRECISION = lax.Precision.HIGH


def unit_rows(rows):
    return rows * lax.rsqrt(jnp.sum(rows * rows, axis=-1, keepdims=True) + 1e-06)


def compose(earlier, later):
    return (
        jnp.matmul(later[0], earlier[0], precision=FULL_PRECISION),
        jnp.matmul(later[0], earlier[1], precision=FULL_PRECISION) + later[1],
    )


def arrange(key_part, value_part, beta_part, decay_part):
    blocks = key_part.shape[0] // SPAN
    key_heads = key_part.shape[1] // DK
    value_heads = value_part.shape[1] // DV
    key_unit = unit_rows(
        key_part.astype(jnp.float32).reshape(blocks, SPAN, key_heads, DK)
    ).transpose(2, 0, 1, 3)
    value_f = (
        value_part.astype(jnp.float32).reshape(blocks, SPAN, value_heads, DV).transpose(2, 0, 1, 3)
    )
    beta_gate = (
        jax.nn.sigmoid(beta_part.astype(jnp.float32))
        .reshape(blocks, SPAN, value_heads)
        .transpose(2, 0, 1)
    )
    decay_log = decay_part.astype(jnp.float32).reshape(blocks, SPAN, value_heads).transpose(2, 0, 1)
    return (key_unit, value_f, beta_gate, decay_log)


def arrange_query(query_part):
    blocks = query_part.shape[0] // SPAN
    key_heads = query_part.shape[1] // DK
    query_f = query_part.astype(jnp.float32).reshape(blocks, SPAN, key_heads, DK)
    return (unit_rows(query_f) * DK ** (-0.5)).transpose(2, 0, 1, 3)


def unit_lower_inverse(strictly_lower):
    inverse = jnp.eye(SPAN, dtype=jnp.float32) - strictly_lower
    power = jnp.matmul(strictly_lower, strictly_lower, precision=LOCAL_PRECISION)
    covered = 2
    while covered < SPAN:
        if 2 * covered < SPAN:
            both = jnp.matmul(
                jnp.concatenate([inverse, power], axis=-2), power, precision=LOCAL_PRECISION
            )
            inverse = inverse + both[..., :SPAN, :]
            power = both[..., SPAN:, :]
        else:
            inverse = inverse + jnp.matmul(inverse, power, precision=LOCAL_PRECISION)
        covered = covered * 2
    return inverse


def span_pass(key_unit, value_f, beta_gate, decay_log, group_size):
    rowpos = lax.broadcasted_iota(jnp.int32, (SPAN, SPAN), 0)
    colpos = lax.broadcasted_iota(jnp.int32, (SPAN, SPAN), 1)
    cum_log = jnp.cumsum(decay_log, axis=2)
    spread = cum_log[..., :, None] - cum_log[..., None, :]
    strict = jnp.exp(jnp.where(colpos < rowpos, spread, -jnp.inf))
    key_inner = jnp.repeat(
        jnp.einsum("hmik,hmjk->hmij", key_unit, key_unit, precision=LOCAL_PRECISION),
        group_size,
        axis=0,
    )
    inverse = unit_lower_inverse(beta_gate[..., :, None] * strict * key_inner)
    wide_keys = jnp.repeat(key_unit, group_size, axis=0)
    targets = jnp.concatenate(
        [beta_gate[..., None] * value_f, (beta_gate * jnp.exp(cum_log))[..., None] * wide_keys],
        axis=-1,
    )
    solved = jnp.matmul(inverse, targets, precision=LOCAL_PRECISION)
    written = solved[..., :DV]
    weights = solved[..., DV:]
    faded_keys = wide_keys * jnp.exp(cum_log[..., -1:] - cum_log)[..., None]
    tail_decay = jnp.exp(cum_log[..., -1])
    carry_mat = tail_decay[..., None, None] * jnp.eye(DK, dtype=jnp.float32) - jnp.einsum(
        "hmck,hmcj->hmkj", faded_keys, weights, precision=LOCAL_PRECISION
    )
    write_mat = jnp.einsum("hmck,hmcv->hmkv", faded_keys, written, precision=LOCAL_PRECISION)
    return (cum_log, spread, written, weights, carry_mat, write_mat)


def span_prep(query_unit, key_unit, group_size, pieces):
    cum_log, spread, written, weights, carry_mat, write_mat = pieces
    rowpos = lax.broadcasted_iota(jnp.int32, (SPAN, SPAN), 0)
    colpos = lax.broadcasted_iota(jnp.int32, (SPAN, SPAN), 1)
    within = jnp.exp(jnp.where(colpos <= rowpos, spread, -jnp.inf))
    scores = (
        jnp.repeat(
            jnp.einsum("hmik,hmjk->hmij", query_unit, key_unit, precision=LOCAL_PRECISION),
            group_size,
            axis=0,
        )
        * within
    )
    wide_query = jnp.repeat(query_unit, group_size, axis=0)
    inner = jnp.einsum("hmij,hmjv->hmiv", scores, written, precision=LOCAL_PRECISION)
    reach = wide_query * jnp.exp(cum_log)[..., None] - jnp.einsum(
        "hmij,hmjk->hmik", scores, weights, precision=LOCAL_PRECISION
    )
    blocks = carry_mat.shape[1]
    fixed, scaled = ([inner[:, 0]], [reach[:, 0]])
    reach_map, reach_add = (carry_mat[:, 0], write_mat[:, 0])
    for m in range(1, blocks):
        fixed.append(
            inner[:, m] + jnp.matmul(reach[:, m], reach_add, precision=LOCAL_PRECISION)
        )
        scaled.append(jnp.matmul(reach[:, m], reach_map, precision=LOCAL_PRECISION))
        reach_map, reach_add = compose((reach_map, reach_add), (carry_mat[:, m], write_mat[:, m]))
    return (jnp.stack(fixed, axis=1), jnp.stack(scaled, axis=1), reach_map, reach_add)


def span_out(fixed, scaled, state_in):
    return fixed + jnp.einsum("hmck,hkv->hmcv", scaled, state_in, precision=FULL_PRECISION)


def to_rows(core_out):
    head_count, blocks = (core_out.shape[0], core_out.shape[1])
    return core_out.transpose(1, 2, 0, 3).reshape(blocks * SPAN, head_count * DV)


def joined(carry, write):
    return jnp.concatenate([carry, write], axis=-1)


def split(both):
    return (both[..., :DK], both[..., DK:])


def exclusive_scan(carry, write, size, stride):
    count = size // stride
    if count == 1:
        return jnp.zeros_like(write)
    rounds = 0
    while 2 ** (rounds + 1) < count:
        rounds += 1
    shift = 1
    for _ in range(rounds):
        pairs = [(i, i + shift * stride) for i in range(size - shift * stride)]
        got = lax.ppermute(joined(carry, write), "ctx", pairs)
        carry, write = compose(split(got), (carry, write))
        shift *= 2
    near = [(i, i + stride) for i in range(size - stride)]
    far = 2**rounds + 1
    if far >= count:
        return lax.ppermute(write, "ctx", near)
    got_carry, got_write = split(lax.ppermute(joined(carry, write), "ctx", near))
    far_write = lax.ppermute(
        write, "ctx", [(i, i + far * stride) for i in range(size - far * stride)]
    )
    return jnp.matmul(got_carry, far_write, precision=FULL_PRECISION) + got_write


def chain_states(block_carry, block_write):
    size = lax.axis_size("ctx")
    me = lax.axis_index("ctx")
    levels = 0
    while size % 2 ** (levels + 1) == 0 and block_carry.shape[0] % 2 ** (levels + 1) == 0:
        levels += 1
    current = joined(block_carry, block_write)
    saved = []
    for level in range(levels):
        stride = 2**level
        upper = (me // stride) % 2 == 1
        half = current.shape[0] // 2
        mine = jnp.where(upper, current[half:], current[:half])
        other = jnp.where(upper, current[:half], current[half:])
        got = lax.ppermute(other, "ctx", [(i, i ^ stride) for i in range(size)])
        earlier = jnp.where(upper, got, mine)
        later = jnp.where(upper, mine, got)
        saved.append((upper, earlier))
        current = joined(*compose(split(earlier), split(later)))
    state = exclusive_scan(*split(current), size, 2**levels)
    for level in reversed(range(levels)):
        stride = 2**level
        upper, earlier = saved[level]
        earlier_carry, earlier_write = split(earlier)
        after = jnp.matmul(earlier_carry, state, precision=FULL_PRECISION) + earlier_write
        mine = jnp.where(upper, after, state)
        other = jnp.where(upper, state, after)
        got = lax.ppermute(other, "ctx", [(i, i ^ stride) for i in range(size)])
        state = jnp.where(
            upper, jnp.concatenate([got, mine], axis=0), jnp.concatenate([mine, got], axis=0)
        )
    return state


def gated_norm(core_rows, output_gate, norm_gain):
    token_count = core_rows.shape[0]
    head_count = core_rows.shape[1] // DV
    core_f = core_rows.astype(jnp.float32).reshape(token_count, head_count, DV)
    inv_rms = lax.rsqrt(jnp.mean(core_f * core_f, axis=-1, keepdims=True) + 1e-06)
    gate_f = output_gate.astype(jnp.float32).reshape(token_count, head_count, DV)
    gated_rows = core_f * inv_rms * norm_gain.astype(jnp.float32) * jax.nn.silu(gate_f)
    return gated_rows.reshape(token_count, head_count * DV).astype(jnp.bfloat16)


def head_swap(rows):
    width = rows.shape[1] // 2
    first = lax.axis_index("head") == 0
    half = lax.axis_index("head")
    own = lax.dynamic_slice_in_dim(rows, half * width, width, 1)
    sent = lax.dynamic_slice_in_dim(rows, (1 - half) * width, width, 1)
    got = lax.ppermute(sent, "head", [(0, 1), (1, 0)])
    return jnp.where(first, jnp.concatenate([own, got], 0), jnp.concatenate([got, own], 0))


def head_return(rows):
    tokens = rows.shape[0] // 2
    first = lax.axis_index("head") == 0
    own = jnp.where(first, rows[:tokens], rows[tokens:])
    sent = jnp.where(first, rows[tokens:], rows[:tokens])
    got = lax.ppermute(sent, "head", [(0, 1), (1, 0)])
    return jnp.where(first, jnp.concatenate([own, got], 1), jnp.concatenate([got, own], 1))


def head_inputs(pieces_in):
    parts = lax.axis_size("head")
    if parts == 2:
        return [head_swap(part) for part in pieces_in]
    tokens = pieces_in[0].shape[0]
    widths = [part.shape[1] // parts for part in pieces_in]
    packed = jnp.concatenate(
        [part.reshape(tokens, parts, width) for part, width in zip(pieces_in, widths)], axis=-1
    )
    packed = lax.all_to_all(packed, "head", split_axis=1, concat_axis=0, tiled=True)
    packed = packed.reshape(tokens * parts, sum(widths))
    ends = [sum(widths[: i + 1]) for i in range(len(widths))]
    return [packed[:, end - width : end] for end, width in zip(ends, widths)]


def head_outputs(rows):
    if lax.axis_size("head") == 2:
        return head_return(rows)
    return lax.all_to_all(rows, "head", split_axis=0, concat_axis=1, tiled=True)


def on_device(query_rows, key_rows, value_rows, output_gate, beta_logit, log_decay, norm_gain):
    q_head, k_head, v_head, b_head, d_head = head_inputs(
        [query_rows, key_rows, value_rows, beta_logit, log_decay]
    )
    key_unit, value_f, beta_gate, decay_log = arrange(k_head, v_head, b_head, d_head)
    group_size = value_f.shape[0] // key_unit.shape[0]
    pieces = span_pass(key_unit, value_f, beta_gate, decay_log, group_size)
    query_unit = arrange_query(q_head)
    fixed, scaled, total_carry, total_write = span_prep(query_unit, key_unit, group_size, pieces)
    state_in = chain_states(total_carry, total_write)
    core_out = span_out(fixed, scaled, state_in)
    core_rows = head_outputs(to_rows(core_out).astype(jnp.bfloat16))
    return gated_norm(core_rows, output_gate, norm_gain)


def solution(mesh):
    placed = (
        P(("ctx", "head"), None),
        P(("ctx", "head"), None),
        P(("ctx", "head"), None),
        P(("ctx", "head"), None),
        P(("ctx", "head"), None),
        P(("ctx", "head"), None),
        P(),
    )
    return jax.shard_map(
        on_device, mesh=mesh, in_specs=placed, out_specs=P(("ctx", "head"), None), check_vma=False
    )
```

```python
import jax
import jax.numpy as jnp
from jax import lax
from jax.sharding import PartitionSpec as P

DK = 128
DV = 128
SPAN = 128


FULL_PRECISION = lax.Precision.HIGH
LOCAL_PRECISION = lax.Precision.HIGH


def unit_rows(rows):
    return rows * lax.rsqrt(jnp.sum(rows * rows, axis=-1, keepdims=True) + 1e-06)


def compose(earlier, later):
    return (
        jnp.matmul(later[0], earlier[0], precision=FULL_PRECISION),
        jnp.matmul(later[0], earlier[1], precision=FULL_PRECISION) + later[1],
    )


def arrange(key_part, value_part, beta_part, decay_part):
    blocks = key_part.shape[0] // SPAN
    key_heads = key_part.shape[1] // DK
    value_heads = value_part.shape[1] // DV
    key_unit = unit_rows(
        key_part.astype(jnp.float32).reshape(blocks, SPAN, key_heads, DK)
    ).transpose(2, 0, 1, 3)
    value_f = (
        value_part.astype(jnp.float32).reshape(blocks, SPAN, value_heads, DV).transpose(2, 0, 1, 3)
    )
    beta_gate = (
        jax.nn.sigmoid(beta_part.astype(jnp.float32))
        .reshape(blocks, SPAN, value_heads)
        .transpose(2, 0, 1)
    )
    decay_log = decay_part.astype(jnp.float32).reshape(blocks, SPAN, value_heads).transpose(2, 0, 1)
    return (key_unit, value_f, beta_gate, decay_log)


def arrange_query(query_part):
    blocks = query_part.shape[0] // SPAN
    key_heads = query_part.shape[1] // DK
    query_f = query_part.astype(jnp.float32).reshape(blocks, SPAN, key_heads, DK)
    return (unit_rows(query_f) * DK ** (-0.5)).transpose(2, 0, 1, 3)


def unit_lower_inverse(strictly_lower):
    inverse = jnp.eye(SPAN, dtype=jnp.float32) - strictly_lower
    power = jnp.matmul(strictly_lower, strictly_lower, precision=LOCAL_PRECISION)
    covered = 2
    while covered < SPAN:
        if 2 * covered < SPAN:
            both = jnp.matmul(
                jnp.concatenate([inverse, power], axis=-2), power, precision=LOCAL_PRECISION
            )
            inverse = inverse + both[..., :SPAN, :]
            power = both[..., SPAN:, :]
        else:
            inverse = inverse + jnp.matmul(inverse, power, precision=LOCAL_PRECISION)
        covered = covered * 2
    return inverse


def span_pass(key_unit, value_f, beta_gate, decay_log, group_size):
    rowpos = lax.broadcasted_iota(jnp.int32, (SPAN, SPAN), 0)
    colpos = lax.broadcasted_iota(jnp.int32, (SPAN, SPAN), 1)
    cum_log = jnp.cumsum(decay_log, axis=2)
    spread = cum_log[..., :, None] - cum_log[..., None, :]
    strict = jnp.exp(jnp.where(colpos < rowpos, spread, -jnp.inf))
    key_inner = jnp.repeat(
        jnp.einsum("hmik,hmjk->hmij", key_unit, key_unit, precision=LOCAL_PRECISION),
        group_size,
        axis=0,
    )
    inverse = unit_lower_inverse(beta_gate[..., :, None] * strict * key_inner)
    wide_keys = jnp.repeat(key_unit, group_size, axis=0)
    targets = jnp.concatenate(
        [beta_gate[..., None] * value_f, (beta_gate * jnp.exp(cum_log))[..., None] * wide_keys],
        axis=-1,
    )
    solved = jnp.matmul(inverse, targets, precision=LOCAL_PRECISION)
    written = solved[..., :DV]
    weights = solved[..., DV:]
    faded_keys = wide_keys * jnp.exp(cum_log[..., -1:] - cum_log)[..., None]
    tail_decay = jnp.exp(cum_log[..., -1])
    carry_mat = tail_decay[..., None, None] * jnp.eye(DK, dtype=jnp.float32) - jnp.einsum(
        "hmck,hmcj->hmkj", faded_keys, weights, precision=LOCAL_PRECISION
    )
    write_mat = jnp.einsum("hmck,hmcv->hmkv", faded_keys, written, precision=LOCAL_PRECISION)
    return (cum_log, spread, written, weights, carry_mat, write_mat)


def span_prep(query_unit, key_unit, group_size, pieces):
    cum_log, spread, written, weights, carry_mat, write_mat = pieces
    rowpos = lax.broadcasted_iota(jnp.int32, (SPAN, SPAN), 0)
    colpos = lax.broadcasted_iota(jnp.int32, (SPAN, SPAN), 1)
    within = jnp.exp(jnp.where(colpos <= rowpos, spread, -jnp.inf))
    scores = (
        jnp.repeat(
            jnp.einsum("hmik,hmjk->hmij", query_unit, key_unit, precision=LOCAL_PRECISION),
            group_size,
            axis=0,
        )
        * within
    )
    wide_query = jnp.repeat(query_unit, group_size, axis=0)
    inner = jnp.einsum("hmij,hmjv->hmiv", scores, written, precision=LOCAL_PRECISION)
    reach = wide_query * jnp.exp(cum_log)[..., None] - jnp.einsum(
        "hmij,hmjk->hmik", scores, weights, precision=LOCAL_PRECISION
    )
    blocks = carry_mat.shape[1]
    fixed, scaled = ([inner[:, 0]], [reach[:, 0]])
    reach_map, reach_add = (carry_mat[:, 0], write_mat[:, 0])
    for m in range(1, blocks):
        fixed.append(
            inner[:, m] + jnp.matmul(reach[:, m], reach_add, precision=LOCAL_PRECISION)
        )
        scaled.append(jnp.matmul(reach[:, m], reach_map, precision=LOCAL_PRECISION))
        reach_map, reach_add = compose((reach_map, reach_add), (carry_mat[:, m], write_mat[:, m]))
    return (jnp.stack(fixed, axis=1), jnp.stack(scaled, axis=1), reach_map, reach_add)


def span_out(fixed, scaled, state_in):
    return fixed + jnp.einsum("hmck,hkv->hmcv", scaled, state_in, precision=FULL_PRECISION)


def to_rows(core_out):
    head_count, blocks = (core_out.shape[0], core_out.shape[1])
    return core_out.transpose(1, 2, 0, 3).reshape(blocks * SPAN, head_count * DV)


def joined(carry, write):
    return jnp.concatenate([carry, write], axis=-1)


def split(both):
    return (both[..., :DK], both[..., DK:])


def exclusive_scan(carry, write, size, stride):
    count = size // stride
    if count == 1:
        return jnp.zeros_like(write)
    rounds = 0
    while 2 ** (rounds + 1) < count:
        rounds += 1
    shift = 1
    for _ in range(rounds):
        pairs = [(i, i + shift * stride) for i in range(size - shift * stride)]
        got = lax.ppermute(joined(carry, write), "ctx", pairs)
        carry, write = compose(split(got), (carry, write))
        shift *= 2
    near = [(i, i + stride) for i in range(size - stride)]
    far = 2**rounds + 1
    if far >= count:
        return lax.ppermute(write, "ctx", near)
    got_carry, got_write = split(lax.ppermute(joined(carry, write), "ctx", near))
    far_write = lax.ppermute(
        write, "ctx", [(i, i + far * stride) for i in range(size - far * stride)]
    )
    return jnp.matmul(got_carry, far_write, precision=FULL_PRECISION) + got_write


def chain_states(block_carry, block_write):
    size = lax.axis_size("ctx")
    me = lax.axis_index("ctx")
    levels = 0
    while size % 2 ** (levels + 1) == 0 and block_carry.shape[0] % 2 ** (levels + 1) == 0:
        levels += 1
    current = joined(block_carry, block_write)
    saved = []
    for level in range(levels):
        stride = 2**level
        upper = (me // stride) % 2 == 1
        half = current.shape[0] // 2
        mine = jnp.where(upper, current[half:], current[:half])
        other = jnp.where(upper, current[:half], current[half:])
        got = lax.ppermute(other, "ctx", [(i, i ^ stride) for i in range(size)])
        earlier = jnp.where(upper, got, mine)
        later = jnp.where(upper, mine, got)
        saved.append((upper, earlier))
        current = joined(*compose(split(earlier), split(later)))
    state = exclusive_scan(*split(current), size, 2**levels)
    for level in reversed(range(levels)):
        stride = 2**level
        upper, earlier = saved[level]
        earlier_carry, earlier_write = split(earlier)
        after = jnp.matmul(earlier_carry, state, precision=FULL_PRECISION) + earlier_write
        mine = jnp.where(upper, after, state)
        other = jnp.where(upper, state, after)
        got = lax.ppermute(other, "ctx", [(i, i ^ stride) for i in range(size)])
        state = jnp.where(
            upper, jnp.concatenate([got, mine], axis=0), jnp.concatenate([mine, got], axis=0)
        )
    return state


def gated_norm(core_rows, output_gate, norm_gain):
    token_count = core_rows.shape[0]
    head_count = core_rows.shape[1] // DV
    core_f = core_rows.astype(jnp.float32).reshape(token_count, head_count, DV)
    inv_rms = lax.rsqrt(jnp.mean(core_f * core_f, axis=-1, keepdims=True) + 1e-06)
    gate_f = output_gate.astype(jnp.float32).reshape(token_count, head_count, DV)
    gated_rows = core_f * inv_rms * norm_gain.astype(jnp.float32) * jax.nn.silu(gate_f)
    return gated_rows.reshape(token_count, head_count * DV).astype(jnp.bfloat16)


def head_swap(rows):
    width = rows.shape[1] // 2
    first = lax.axis_index("head") == 0
    own = jnp.where(first, rows[:, :width], rows[:, width:])
    sent = jnp.where(first, rows[:, width:], rows[:, :width])
    got = lax.ppermute(sent, "head", [(0, 1), (1, 0)])
    return jnp.where(first, jnp.concatenate([own, got], 0), jnp.concatenate([got, own], 0))


def head_return(rows):
    tokens = rows.shape[0] // 2
    first = lax.axis_index("head") == 0
    own = jnp.where(first, rows[:tokens], rows[tokens:])
    sent = jnp.where(first, rows[tokens:], rows[:tokens])
    got = lax.ppermute(sent, "head", [(0, 1), (1, 0)])
    return jnp.where(first, jnp.concatenate([own, got], 1), jnp.concatenate([got, own], 1))


def head_inputs(pieces_in):
    parts = lax.axis_size("head")
    if parts == 2:
        return [head_swap(part) for part in pieces_in]
    tokens = pieces_in[0].shape[0]
    widths = [part.shape[1] // parts for part in pieces_in]
    packed = jnp.concatenate(
        [part.reshape(tokens, parts, width) for part, width in zip(pieces_in, widths)], axis=-1
    )
    packed = lax.all_to_all(packed, "head", split_axis=1, concat_axis=0, tiled=True)
    packed = packed.reshape(tokens * parts, sum(widths))
    ends = [sum(widths[: i + 1]) for i in range(len(widths))]
    return [packed[:, end - width : end] for end, width in zip(ends, widths)]


def head_outputs(rows):
    if lax.axis_size("head") == 2:
        return head_return(rows)
    return lax.all_to_all(rows, "head", split_axis=0, concat_axis=1, tiled=True)


def on_device(query_rows, key_rows, value_rows, output_gate, beta_logit, log_decay, norm_gain):
    q_head, k_head, v_head, b_head, d_head = head_inputs(
        [query_rows, key_rows, value_rows, beta_logit, log_decay]
    )
    key_unit, value_f, beta_gate, decay_log = arrange(k_head, v_head, b_head, d_head)
    group_size = value_f.shape[0] // key_unit.shape[0]
    pieces = span_pass(key_unit, value_f, beta_gate, decay_log, group_size)
    query_unit = arrange_query(q_head)
    fixed, scaled, total_carry, total_write = span_prep(query_unit, key_unit, group_size, pieces)
    state_in = chain_states(total_carry, total_write)
    core_out = span_out(fixed, scaled, state_in)
    core_rows = head_outputs(to_rows(core_out).astype(jnp.bfloat16))
    return gated_norm(core_rows, output_gate, norm_gain)


def solution(mesh):
    placed = (
        P(("ctx", "head"), None),
        P(("ctx", "head"), None),
        P(("ctx", "head"), None),
        P(("ctx", "head"), None),
        P(("ctx", "head"), None),
        P(("ctx", "head"), None),
        P(),
    )
    return jax.shard_map(
        on_device, mesh=mesh, in_specs=placed, out_specs=P(("ctx", "head"), None), check_vma=False
    )
```

```python
import jax
import jax.numpy as jnp
from jax import lax
from jax.sharding import PartitionSpec as P

DK = 128
DV = 128
SPAN = 128


FULL_PRECISION = lax.Precision.HIGH
LOCAL_PRECISION = lax.Precision.HIGH


def unit_rows(rows):
    return rows * lax.rsqrt(jnp.sum(rows * rows, axis=-1, keepdims=True) + 1e-06)


def compose(earlier, later):
    return (
        jnp.matmul(later[0], earlier[0], precision=FULL_PRECISION),
        jnp.matmul(later[0], earlier[1], precision=FULL_PRECISION) + later[1],
    )


def arrange(key_part, value_part, beta_part, decay_part):
    blocks = key_part.shape[0] // SPAN
    key_heads = key_part.shape[1] // DK
    value_heads = value_part.shape[1] // DV
    key_unit = unit_rows(
        key_part.astype(jnp.float32).reshape(blocks, SPAN, key_heads, DK)
    ).transpose(2, 0, 1, 3)
    value_f = (
        value_part.astype(jnp.float32).reshape(blocks, SPAN, value_heads, DV).transpose(2, 0, 1, 3)
    )
    beta_gate = (
        jax.nn.sigmoid(beta_part.astype(jnp.float32))
        .reshape(blocks, SPAN, value_heads)
        .transpose(2, 0, 1)
    )
    decay_log = decay_part.astype(jnp.float32).reshape(blocks, SPAN, value_heads).transpose(2, 0, 1)
    return (key_unit, value_f, beta_gate, decay_log)


def arrange_query(query_part):
    blocks = query_part.shape[0] // SPAN
    key_heads = query_part.shape[1] // DK
    query_f = query_part.astype(jnp.float32).reshape(blocks, SPAN, key_heads, DK)
    return (unit_rows(query_f) * DK ** (-0.5)).transpose(2, 0, 1, 3)


def unit_lower_inverse(strictly_lower):
    inverse = jnp.eye(SPAN, dtype=jnp.float32) - strictly_lower
    power = jnp.matmul(strictly_lower, strictly_lower, precision=LOCAL_PRECISION)
    covered = 2
    while covered < SPAN:
        if 2 * covered < SPAN:
            both = jnp.matmul(
                jnp.concatenate([inverse, power], axis=-2), power, precision=LOCAL_PRECISION
            )
            inverse = inverse + both[..., :SPAN, :]
            power = both[..., SPAN:, :]
        else:
            inverse = inverse + jnp.matmul(inverse, power, precision=LOCAL_PRECISION)
        covered = covered * 2
    return inverse


def span_pass(key_unit, value_f, beta_gate, decay_log, group_size):
    rowpos = lax.broadcasted_iota(jnp.int32, (SPAN, SPAN), 0)
    colpos = lax.broadcasted_iota(jnp.int32, (SPAN, SPAN), 1)
    cum_log = jnp.cumsum(decay_log, axis=2)
    spread = cum_log[..., :, None] - cum_log[..., None, :]
    strict = jnp.exp(jnp.where(colpos < rowpos, spread, -jnp.inf))
    key_inner = jnp.repeat(
        jnp.einsum("hmik,hmjk->hmij", key_unit, key_unit, precision=LOCAL_PRECISION),
        group_size,
        axis=0,
    )
    inverse = unit_lower_inverse(beta_gate[..., :, None] * strict * key_inner)
    wide_keys = jnp.repeat(key_unit, group_size, axis=0)
    targets = jnp.concatenate(
        [beta_gate[..., None] * value_f, (beta_gate * jnp.exp(cum_log))[..., None] * wide_keys],
        axis=-1,
    )
    solved = jnp.matmul(inverse, targets, precision=LOCAL_PRECISION)
    written = solved[..., :DV]
    weights = solved[..., DV:]
    faded_keys = wide_keys * jnp.exp(cum_log[..., -1:] - cum_log)[..., None]
    tail_decay = jnp.exp(cum_log[..., -1])
    carry_mat = tail_decay[..., None, None] * jnp.eye(DK, dtype=jnp.float32) - jnp.einsum(
        "hmck,hmcj->hmkj", faded_keys, weights, precision=LOCAL_PRECISION
    )
    write_mat = jnp.einsum("hmck,hmcv->hmkv", faded_keys, written, precision=LOCAL_PRECISION)
    return (cum_log, spread, written, weights, carry_mat, write_mat)


def span_prep(query_unit, key_unit, group_size, pieces):
    cum_log, spread, written, weights, carry_mat, write_mat = pieces
    rowpos = lax.broadcasted_iota(jnp.int32, (SPAN, SPAN), 0)
    colpos = lax.broadcasted_iota(jnp.int32, (SPAN, SPAN), 1)
    within = jnp.exp(jnp.where(colpos <= rowpos, spread, -jnp.inf))
    scores = (
        jnp.repeat(
            jnp.einsum("hmik,hmjk->hmij", query_unit, key_unit, precision=LOCAL_PRECISION),
            group_size,
            axis=0,
        )
        * within
    )
    wide_query = jnp.repeat(query_unit, group_size, axis=0)
    inner = jnp.einsum("hmij,hmjv->hmiv", scores, written, precision=LOCAL_PRECISION)
    reach = wide_query * jnp.exp(cum_log)[..., None] - jnp.einsum(
        "hmij,hmjk->hmik", scores, weights, precision=LOCAL_PRECISION
    )
    blocks = carry_mat.shape[1]
    fixed, scaled = ([inner[:, 0]], [reach[:, 0]])
    reach_map, reach_add = (carry_mat[:, 0], write_mat[:, 0])
    for m in range(1, blocks):
        fixed.append(
            inner[:, m] + jnp.matmul(reach[:, m], reach_add, precision=LOCAL_PRECISION)
        )
        scaled.append(jnp.matmul(reach[:, m], reach_map, precision=LOCAL_PRECISION))
        reach_map, reach_add = compose((reach_map, reach_add), (carry_mat[:, m], write_mat[:, m]))
    return (jnp.stack(fixed, axis=1), jnp.stack(scaled, axis=1), reach_map, reach_add)


def span_out(fixed, scaled, state_in):
    return fixed + jnp.einsum("hmck,hkv->hmcv", scaled, state_in, precision=FULL_PRECISION)


def to_rows(core_out):
    head_count, blocks = (core_out.shape[0], core_out.shape[1])
    return core_out.transpose(1, 2, 0, 3).reshape(blocks * SPAN, head_count * DV)


def joined(carry, write):
    return jnp.concatenate([carry, write], axis=-1)


def split(both):
    return (both[..., :DK], both[..., DK:])


def exclusive_scan(carry, write, size, stride):
    count = size // stride
    if count == 1:
        return jnp.zeros_like(write)
    rounds = 0
    while 2 ** (rounds + 1) < count:
        rounds += 1
    shift = 1
    for _ in range(rounds):
        pairs = [(i, i + shift * stride) for i in range(size - shift * stride)]
        got = lax.ppermute(joined(carry, write), "ctx", pairs)
        carry, write = compose(split(got), (carry, write))
        shift *= 2
    near = [(i, i + stride) for i in range(size - stride)]
    far = 2**rounds + 1
    if far >= count:
        return lax.ppermute(write, "ctx", near)
    got_carry, got_write = split(lax.ppermute(joined(carry, write), "ctx", near))
    far_write = lax.ppermute(
        write, "ctx", [(i, i + far * stride) for i in range(size - far * stride)]
    )
    return jnp.matmul(got_carry, far_write, precision=FULL_PRECISION) + got_write


def chain_states(block_carry, block_write):
    size = lax.axis_size("ctx")
    me = lax.axis_index("ctx")
    levels = 0
    while size % 2 ** (levels + 1) == 0 and block_carry.shape[0] % 2 ** (levels + 1) == 0:
        levels += 1
    current = joined(block_carry, block_write)
    saved = []
    for level in range(levels):
        stride = 2**level
        upper = (me // stride) % 2 == 1
        half = current.shape[0] // 2
        mine = jnp.where(upper, current[half:], current[:half])
        other = jnp.where(upper, current[:half], current[half:])
        got = lax.ppermute(other, "ctx", [(i, i ^ stride) for i in range(size)])
        earlier = jnp.where(upper, got, mine)
        later = jnp.where(upper, mine, got)
        saved.append((upper, earlier))
        current = joined(*compose(split(earlier), split(later)))
    state = exclusive_scan(*split(current), size, 2**levels)
    for level in reversed(range(levels)):
        stride = 2**level
        upper, earlier = saved[level]
        earlier_carry, earlier_write = split(earlier)
        after = jnp.matmul(earlier_carry, state, precision=FULL_PRECISION) + earlier_write
        mine = jnp.where(upper, after, state)
        other = jnp.where(upper, state, after)
        got = lax.ppermute(other, "ctx", [(i, i ^ stride) for i in range(size)])
        state = jnp.where(
            upper, jnp.concatenate([got, mine], axis=0), jnp.concatenate([mine, got], axis=0)
        )
    return state


def gated_norm(core_rows, output_gate, norm_gain):
    token_count = core_rows.shape[0]
    head_count = core_rows.shape[1] // DV
    core_f = core_rows.astype(jnp.float32).reshape(token_count, head_count, DV)
    inv_rms = lax.rsqrt(jnp.mean(core_f * core_f, axis=-1, keepdims=True) + 1e-06)
    gate_f = output_gate.astype(jnp.float32).reshape(token_count, head_count, DV)
    gated_rows = core_f * inv_rms * norm_gain.astype(jnp.float32) * jax.nn.silu(gate_f)
    return gated_rows.reshape(token_count, head_count * DV).astype(jnp.bfloat16)


def head_swap(rows):
    width = rows.shape[-1] // 2
    first = lax.axis_index("head") == 0
    own = jnp.where(first, rows[..., :width], rows[..., width:])
    sent = jnp.where(first, rows[..., width:], rows[..., :width])
    got = lax.ppermute(sent, "head", [(0, 1), (1, 0)])
    axis = rows.ndim - 2
    return jnp.where(
        first, jnp.concatenate([own, got], axis), jnp.concatenate([got, own], axis)
    )


def head_return(rows):
    tokens = rows.shape[0] // 2
    first = lax.axis_index("head") == 0
    own = jnp.where(first, rows[:tokens], rows[tokens:])
    sent = jnp.where(first, rows[tokens:], rows[:tokens])
    got = lax.ppermute(sent, "head", [(0, 1), (1, 0)])
    return jnp.where(first, jnp.concatenate([own, got], 1), jnp.concatenate([got, own], 1))


def head_inputs(pieces_in):
    parts = lax.axis_size("head")
    if parts == 2:
        query_rows, key_rows, value_rows, beta_logit, log_decay = pieces_in
        query_key = head_swap(jnp.stack([query_rows, key_rows]))
        gates = head_swap(jnp.stack([beta_logit, log_decay]))
        return [query_key[0], query_key[1], head_swap(value_rows), gates[0], gates[1]]
    tokens = pieces_in[0].shape[0]
    widths = [part.shape[1] // parts for part in pieces_in]
    packed = jnp.concatenate(
        [part.reshape(tokens, parts, width) for part, width in zip(pieces_in, widths)], axis=-1
    )
    packed = lax.all_to_all(packed, "head", split_axis=1, concat_axis=0, tiled=True)
    packed = packed.reshape(tokens * parts, sum(widths))
    ends = [sum(widths[: i + 1]) for i in range(len(widths))]
    return [packed[:, end - width : end] for end, width in zip(ends, widths)]


def head_outputs(rows):
    if lax.axis_size("head") == 2:
        return head_return(rows)
    return lax.all_to_all(rows, "head", split_axis=0, concat_axis=1, tiled=True)


def on_device(query_rows, key_rows, value_rows, output_gate, beta_logit, log_decay, norm_gain):
    q_head, k_head, v_head, b_head, d_head = head_inputs(
        [query_rows, key_rows, value_rows, beta_logit, log_decay]
    )
    key_unit, value_f, beta_gate, decay_log = arrange(k_head, v_head, b_head, d_head)
    group_size = value_f.shape[0] // key_unit.shape[0]
    pieces = span_pass(key_unit, value_f, beta_gate, decay_log, group_size)
    query_unit = arrange_query(q_head)
    fixed, scaled, total_carry, total_write = span_prep(query_unit, key_unit, group_size, pieces)
    state_in = chain_states(total_carry, total_write)
    core_out = span_out(fixed, scaled, state_in)
    core_rows = head_outputs(to_rows(core_out).astype(jnp.bfloat16))
    return gated_norm(core_rows, output_gate, norm_gain)


def solution(mesh):
    placed = (
        P(("ctx", "head"), None),
        P(("ctx", "head"), None),
        P(("ctx", "head"), None),
        P(("ctx", "head"), None),
        P(("ctx", "head"), None),
        P(("ctx", "head"), None),
        P(),
    )
    return jax.shard_map(
        on_device, mesh=mesh, in_specs=placed, out_specs=P(("ctx", "head"), None), check_vma=False
    )
```

```python
import jax
import jax.numpy as jnp
from jax import lax
from jax.sharding import PartitionSpec as P

DK = 128
DV = 128
SPAN = 128


FULL_PRECISION = lax.Precision.HIGH
LOCAL_PRECISION = lax.Precision.HIGH


def unit_rows(rows):
    return rows * lax.rsqrt(jnp.sum(rows * rows, axis=-1, keepdims=True) + 1e-06)


def compose(earlier, later):
    return (
        jnp.matmul(later[0], earlier[0], precision=FULL_PRECISION),
        jnp.matmul(later[0], earlier[1], precision=FULL_PRECISION) + later[1],
    )


def arrange(key_part, value_part, beta_part, decay_part):
    blocks = key_part.shape[0] // SPAN
    key_heads = key_part.shape[1] // DK
    value_heads = value_part.shape[1] // DV
    key_unit = unit_rows(
        key_part.astype(jnp.float32).reshape(blocks, SPAN, key_heads, DK)
    ).transpose(2, 0, 1, 3)
    value_f = (
        value_part.astype(jnp.float32).reshape(blocks, SPAN, value_heads, DV).transpose(2, 0, 1, 3)
    )
    beta_gate = (
        jax.nn.sigmoid(beta_part.astype(jnp.float32))
        .reshape(blocks, SPAN, value_heads)
        .transpose(2, 0, 1)
    )
    decay_log = decay_part.astype(jnp.float32).reshape(blocks, SPAN, value_heads).transpose(2, 0, 1)
    return (key_unit, value_f, beta_gate, decay_log)


def arrange_query(query_part):
    blocks = query_part.shape[0] // SPAN
    key_heads = query_part.shape[1] // DK
    query_f = query_part.astype(jnp.float32).reshape(blocks, SPAN, key_heads, DK)
    return (unit_rows(query_f) * DK ** (-0.5)).transpose(2, 0, 1, 3)


def unit_lower_inverse(strictly_lower):
    inverse = jnp.eye(SPAN, dtype=jnp.float32) - strictly_lower
    power = jnp.matmul(strictly_lower, strictly_lower, precision=LOCAL_PRECISION)
    covered = 2
    while covered < SPAN:
        if 2 * covered < SPAN:
            both = jnp.matmul(
                jnp.concatenate([inverse, power], axis=-2), power, precision=LOCAL_PRECISION
            )
            inverse = inverse + both[..., :SPAN, :]
            power = both[..., SPAN:, :]
        else:
            inverse = inverse + jnp.matmul(inverse, power, precision=LOCAL_PRECISION)
        covered = covered * 2
    return inverse


def span_pass(key_unit, value_f, beta_gate, decay_log, group_size):
    rowpos = lax.broadcasted_iota(jnp.int32, (SPAN, SPAN), 0)
    colpos = lax.broadcasted_iota(jnp.int32, (SPAN, SPAN), 1)
    cum_log = jnp.cumsum(decay_log, axis=2)
    spread = cum_log[..., :, None] - cum_log[..., None, :]
    strict = jnp.exp(jnp.where(colpos < rowpos, spread, -jnp.inf))
    key_inner = jnp.repeat(
        jnp.einsum("hmik,hmjk->hmij", key_unit, key_unit, precision=LOCAL_PRECISION),
        group_size,
        axis=0,
    )
    inverse = unit_lower_inverse(beta_gate[..., :, None] * strict * key_inner)
    wide_keys = jnp.repeat(key_unit, group_size, axis=0)
    targets = jnp.concatenate(
        [beta_gate[..., None] * value_f, (beta_gate * jnp.exp(cum_log))[..., None] * wide_keys],
        axis=-1,
    )
    solved = jnp.matmul(inverse, targets, precision=LOCAL_PRECISION)
    written = solved[..., :DV]
    weights = solved[..., DV:]
    faded_keys = wide_keys * jnp.exp(cum_log[..., -1:] - cum_log)[..., None]
    tail_decay = jnp.exp(cum_log[..., -1])
    carry_mat = tail_decay[..., None, None] * jnp.eye(DK, dtype=jnp.float32) - jnp.einsum(
        "hmck,hmcj->hmkj", faded_keys, weights, precision=LOCAL_PRECISION
    )
    write_mat = jnp.einsum("hmck,hmcv->hmkv", faded_keys, written, precision=LOCAL_PRECISION)
    return (cum_log, spread, written, weights, carry_mat, write_mat)


def span_prep(query_unit, key_unit, group_size, pieces):
    cum_log, spread, written, weights, carry_mat, write_mat = pieces
    rowpos = lax.broadcasted_iota(jnp.int32, (SPAN, SPAN), 0)
    colpos = lax.broadcasted_iota(jnp.int32, (SPAN, SPAN), 1)
    within = jnp.exp(jnp.where(colpos <= rowpos, spread, -jnp.inf))
    scores = (
        jnp.repeat(
            jnp.einsum("hmik,hmjk->hmij", query_unit, key_unit, precision=LOCAL_PRECISION),
            group_size,
            axis=0,
        )
        * within
    )
    wide_query = jnp.repeat(query_unit, group_size, axis=0)
    inner = jnp.einsum("hmij,hmjv->hmiv", scores, written, precision=LOCAL_PRECISION)
    reach = wide_query * jnp.exp(cum_log)[..., None] - jnp.einsum(
        "hmij,hmjk->hmik", scores, weights, precision=LOCAL_PRECISION
    )
    blocks = carry_mat.shape[1]
    fixed, scaled = ([inner[:, 0]], [reach[:, 0]])
    reach_map, reach_add = (carry_mat[:, 0], write_mat[:, 0])
    for m in range(1, blocks):
        fixed.append(
            inner[:, m] + jnp.matmul(reach[:, m], reach_add, precision=LOCAL_PRECISION)
        )
        scaled.append(jnp.matmul(reach[:, m], reach_map, precision=LOCAL_PRECISION))
        reach_map, reach_add = compose((reach_map, reach_add), (carry_mat[:, m], write_mat[:, m]))
    return (jnp.stack(fixed, axis=1), jnp.stack(scaled, axis=1), reach_map, reach_add)


def span_out(fixed, scaled, state_in):
    return fixed + jnp.einsum("hmck,hkv->hmcv", scaled, state_in, precision=FULL_PRECISION)


def to_rows(core_out):
    head_count, blocks = (core_out.shape[0], core_out.shape[1])
    return core_out.transpose(1, 2, 0, 3).reshape(blocks * SPAN, head_count * DV)


def joined(carry, write):
    return jnp.concatenate([carry, write], axis=-1)


def split(both):
    return (both[..., :DK], both[..., DK:])


def exclusive_scan(carry, write, size, stride):
    count = size // stride
    if count == 1:
        return jnp.zeros_like(write)
    rounds = 0
    while 2 ** (rounds + 1) < count:
        rounds += 1
    shift = 1
    for _ in range(rounds):
        pairs = [(i, i + shift * stride) for i in range(size - shift * stride)]
        got = lax.ppermute(joined(carry, write), "ctx", pairs)
        carry, write = compose(split(got), (carry, write))
        shift *= 2
    near = [(i, i + stride) for i in range(size - stride)]
    far = 2**rounds + 1
    if far >= count:
        return lax.ppermute(write, "ctx", near)
    got_carry, got_write = split(lax.ppermute(joined(carry, write), "ctx", near))
    far_write = lax.ppermute(
        write, "ctx", [(i, i + far * stride) for i in range(size - far * stride)]
    )
    return jnp.matmul(got_carry, far_write, precision=FULL_PRECISION) + got_write


def chain_states(block_carry, block_write):
    size = lax.axis_size("ctx")
    me = lax.axis_index("ctx")
    levels = 0
    while (
        levels < 2
        and size % 2 ** (levels + 1) == 0
        and block_carry.shape[0] % 2 ** (levels + 1) == 0
    ):
        levels += 1
    current = joined(block_carry, block_write)
    saved = []
    for level in range(levels):
        stride = 2**level
        upper = (me // stride) % 2 == 1
        half = current.shape[0] // 2
        mine = jnp.where(upper, current[half:], current[:half])
        other = jnp.where(upper, current[:half], current[half:])
        got = lax.ppermute(other, "ctx", [(i, i ^ stride) for i in range(size)])
        earlier = jnp.where(upper, got, mine)
        later = jnp.where(upper, mine, got)
        saved.append((upper, earlier))
        current = joined(*compose(split(earlier), split(later)))
    state = exclusive_scan(*split(current), size, 2**levels)
    for level in reversed(range(levels)):
        stride = 2**level
        upper, earlier = saved[level]
        earlier_carry, earlier_write = split(earlier)
        after = jnp.matmul(earlier_carry, state, precision=FULL_PRECISION) + earlier_write
        mine = jnp.where(upper, after, state)
        other = jnp.where(upper, state, after)
        got = lax.ppermute(other, "ctx", [(i, i ^ stride) for i in range(size)])
        state = jnp.where(
            upper, jnp.concatenate([got, mine], axis=0), jnp.concatenate([mine, got], axis=0)
        )
    return state


def gated_norm(core_rows, output_gate, norm_gain):
    token_count = core_rows.shape[0]
    head_count = core_rows.shape[1] // DV
    core_f = core_rows.astype(jnp.float32).reshape(token_count, head_count, DV)
    inv_rms = lax.rsqrt(jnp.mean(core_f * core_f, axis=-1, keepdims=True) + 1e-06)
    gate_f = output_gate.astype(jnp.float32).reshape(token_count, head_count, DV)
    gated_rows = core_f * inv_rms * norm_gain.astype(jnp.float32) * jax.nn.silu(gate_f)
    return gated_rows.reshape(token_count, head_count * DV).astype(jnp.bfloat16)


def head_swap(rows):
    width = rows.shape[-1] // 2
    first = lax.axis_index("head") == 0
    own = jnp.where(first, rows[..., :width], rows[..., width:])
    sent = jnp.where(first, rows[..., width:], rows[..., :width])
    got = lax.ppermute(sent, "head", [(0, 1), (1, 0)])
    axis = rows.ndim - 2
    return jnp.where(
        first, jnp.concatenate([own, got], axis), jnp.concatenate([got, own], axis)
    )


def head_return(rows):
    tokens = rows.shape[0] // 2
    first = lax.axis_index("head") == 0
    own = jnp.where(first, rows[:tokens], rows[tokens:])
    sent = jnp.where(first, rows[tokens:], rows[:tokens])
    got = lax.ppermute(sent, "head", [(0, 1), (1, 0)])
    return jnp.where(first, jnp.concatenate([own, got], 1), jnp.concatenate([got, own], 1))


def head_inputs(pieces_in):
    parts = lax.axis_size("head")
    if parts == 2:
        query_rows, key_rows, value_rows, beta_logit, log_decay = pieces_in
        query_key = head_swap(jnp.stack([query_rows, key_rows]))
        gates = head_swap(jnp.stack([beta_logit, log_decay]))
        return [query_key[0], query_key[1], head_swap(value_rows), gates[0], gates[1]]
    tokens = pieces_in[0].shape[0]
    widths = [part.shape[1] // parts for part in pieces_in]
    packed = jnp.concatenate(
        [part.reshape(tokens, parts, width) for part, width in zip(pieces_in, widths)], axis=-1
    )
    packed = lax.all_to_all(packed, "head", split_axis=1, concat_axis=0, tiled=True)
    packed = packed.reshape(tokens * parts, sum(widths))
    ends = [sum(widths[: i + 1]) for i in range(len(widths))]
    return [packed[:, end - width : end] for end, width in zip(ends, widths)]


def head_outputs(rows):
    if lax.axis_size("head") == 2:
        return head_return(rows)
    return lax.all_to_all(rows, "head", split_axis=0, concat_axis=1, tiled=True)


def on_device(query_rows, key_rows, value_rows, output_gate, beta_logit, log_decay, norm_gain):
    q_head, k_head, v_head, b_head, d_head = head_inputs(
        [query_rows, key_rows, value_rows, beta_logit, log_decay]
    )
    key_unit, value_f, beta_gate, decay_log = arrange(k_head, v_head, b_head, d_head)
    group_size = value_f.shape[0] // key_unit.shape[0]
    pieces = span_pass(key_unit, value_f, beta_gate, decay_log, group_size)
    query_unit = arrange_query(q_head)
    fixed, scaled, total_carry, total_write = span_prep(query_unit, key_unit, group_size, pieces)
    state_in = chain_states(total_carry, total_write)
    core_out = span_out(fixed, scaled, state_in)
    core_rows = head_outputs(to_rows(core_out).astype(jnp.bfloat16))
    return gated_norm(core_rows, output_gate, norm_gain)


def solution(mesh):
    placed = (
        P(("ctx", "head"), None),
        P(("ctx", "head"), None),
        P(("ctx", "head"), None),
        P(("ctx", "head"), None),
        P(("ctx", "head"), None),
        P(("ctx", "head"), None),
        P(),
    )
    return jax.shard_map(
        on_device, mesh=mesh, in_specs=placed, out_specs=P(("ctx", "head"), None), check_vma=False
    )
```

```python
import jax
import jax.numpy as jnp
from jax import lax
from jax.sharding import PartitionSpec as P

DK = 128
DV = 128
SPAN = 128


FULL_PRECISION = lax.Precision.HIGH
LOCAL_PRECISION = lax.Precision.HIGH


def unit_rows(rows):
    return rows * lax.rsqrt(jnp.sum(rows * rows, axis=-1, keepdims=True) + 1e-06)


def compose(earlier, later):
    return (
        jnp.matmul(later[0], earlier[0], precision=FULL_PRECISION),
        jnp.matmul(later[0], earlier[1], precision=FULL_PRECISION) + later[1],
    )


def arrange(key_part, value_part, beta_part, decay_part):
    blocks = key_part.shape[0] // SPAN
    key_heads = key_part.shape[1] // DK
    value_heads = value_part.shape[1] // DV
    key_unit = unit_rows(
        key_part.astype(jnp.float32).reshape(blocks, SPAN, key_heads, DK)
    ).transpose(2, 0, 1, 3)
    value_f = (
        value_part.astype(jnp.float32).reshape(blocks, SPAN, value_heads, DV).transpose(2, 0, 1, 3)
    )
    beta_gate = (
        jax.nn.sigmoid(beta_part.astype(jnp.float32))
        .reshape(blocks, SPAN, value_heads)
        .transpose(2, 0, 1)
    )
    decay_log = decay_part.astype(jnp.float32).reshape(blocks, SPAN, value_heads).transpose(2, 0, 1)
    return (key_unit, value_f, beta_gate, decay_log)


def arrange_query(query_part):
    blocks = query_part.shape[0] // SPAN
    key_heads = query_part.shape[1] // DK
    query_f = query_part.astype(jnp.float32).reshape(blocks, SPAN, key_heads, DK)
    return (unit_rows(query_f) * DK ** (-0.5)).transpose(2, 0, 1, 3)


def unit_lower_inverse(strictly_lower):
    inverse = jnp.eye(SPAN, dtype=jnp.float32) - strictly_lower
    power = jnp.matmul(strictly_lower, strictly_lower, precision=LOCAL_PRECISION)
    covered = 2
    while covered < SPAN:
        if 2 * covered < SPAN:
            both = jnp.matmul(
                jnp.concatenate([inverse, power], axis=-2), power, precision=LOCAL_PRECISION
            )
            inverse = inverse + both[..., :SPAN, :]
            power = both[..., SPAN:, :]
        else:
            inverse = inverse + jnp.matmul(inverse, power, precision=LOCAL_PRECISION)
        covered = covered * 2
    return inverse


def span_pass(key_unit, value_f, beta_gate, decay_log, group_size):
    rowpos = lax.broadcasted_iota(jnp.int32, (SPAN, SPAN), 0)
    colpos = lax.broadcasted_iota(jnp.int32, (SPAN, SPAN), 1)
    cum_log = jnp.cumsum(decay_log, axis=2)
    spread = cum_log[..., :, None] - cum_log[..., None, :]
    strict = jnp.exp(jnp.where(colpos < rowpos, spread, -jnp.inf))
    key_inner = jnp.repeat(
        jnp.einsum("hmik,hmjk->hmij", key_unit, key_unit, precision=LOCAL_PRECISION),
        group_size,
        axis=0,
    )
    inverse = unit_lower_inverse(beta_gate[..., :, None] * strict * key_inner)
    wide_keys = jnp.repeat(key_unit, group_size, axis=0)
    targets = jnp.concatenate(
        [beta_gate[..., None] * value_f, (beta_gate * jnp.exp(cum_log))[..., None] * wide_keys],
        axis=-1,
    )
    solved = jnp.matmul(inverse, targets, precision=LOCAL_PRECISION)
    written = solved[..., :DV]
    weights = solved[..., DV:]
    faded_keys = wide_keys * jnp.exp(cum_log[..., -1:] - cum_log)[..., None]
    tail_decay = jnp.exp(cum_log[..., -1])
    carry_mat = tail_decay[..., None, None] * jnp.eye(DK, dtype=jnp.float32) - jnp.einsum(
        "hmck,hmcj->hmkj", faded_keys, weights, precision=LOCAL_PRECISION
    )
    write_mat = jnp.einsum("hmck,hmcv->hmkv", faded_keys, written, precision=LOCAL_PRECISION)
    return (cum_log, spread, written, weights, carry_mat, write_mat)


def span_prep(query_unit, key_unit, group_size, pieces):
    cum_log, spread, written, weights, carry_mat, write_mat = pieces
    rowpos = lax.broadcasted_iota(jnp.int32, (SPAN, SPAN), 0)
    colpos = lax.broadcasted_iota(jnp.int32, (SPAN, SPAN), 1)
    within = jnp.exp(jnp.where(colpos <= rowpos, spread, -jnp.inf))
    scores = (
        jnp.repeat(
            jnp.einsum("hmik,hmjk->hmij", query_unit, key_unit, precision=LOCAL_PRECISION),
            group_size,
            axis=0,
        )
        * within
    )
    wide_query = jnp.repeat(query_unit, group_size, axis=0)
    inner = jnp.einsum("hmij,hmjv->hmiv", scores, written, precision=LOCAL_PRECISION)
    reach = wide_query * jnp.exp(cum_log)[..., None] - jnp.einsum(
        "hmij,hmjk->hmik", scores, weights, precision=LOCAL_PRECISION
    )
    blocks = carry_mat.shape[1]
    fixed, scaled = ([inner[:, 0]], [reach[:, 0]])
    reach_map, reach_add = (carry_mat[:, 0], write_mat[:, 0])
    for m in range(1, blocks):
        fixed.append(
            inner[:, m] + jnp.matmul(reach[:, m], reach_add, precision=LOCAL_PRECISION)
        )
        scaled.append(jnp.matmul(reach[:, m], reach_map, precision=LOCAL_PRECISION))
        reach_map, reach_add = compose((reach_map, reach_add), (carry_mat[:, m], write_mat[:, m]))
    return (jnp.stack(fixed, axis=1), jnp.stack(scaled, axis=1), reach_map, reach_add)


def span_out(fixed, scaled, state_in):
    return fixed + jnp.einsum("hmck,hkv->hmcv", scaled, state_in, precision=FULL_PRECISION)


def to_rows(core_out):
    head_count, blocks = (core_out.shape[0], core_out.shape[1])
    return core_out.transpose(1, 2, 0, 3).reshape(blocks * SPAN, head_count * DV)


def joined(carry, write):
    return jnp.concatenate([carry, write], axis=-1)


def split(both):
    return (both[..., :DK], both[..., DK:])


def exclusive_scan(carry, write, size, stride):
    count = size // stride
    if count == 1:
        return jnp.zeros_like(write)
    rounds = 0
    while 2 ** (rounds + 1) < count:
        rounds += 1
    shift = 1
    for _ in range(rounds):
        pairs = [(i, i + shift * stride) for i in range(size - shift * stride)]
        got = lax.ppermute(joined(carry, write), "ctx", pairs)
        carry, write = compose(split(got), (carry, write))
        shift *= 2
    near = [(i, i + stride) for i in range(size - stride)]
    far = 2**rounds + 1
    if far >= count:
        return lax.ppermute(write, "ctx", near)
    got_carry, got_write = split(lax.ppermute(joined(carry, write), "ctx", near))
    far_write = lax.ppermute(
        write, "ctx", [(i, i + far * stride) for i in range(size - far * stride)]
    )
    return jnp.matmul(got_carry, far_write, precision=FULL_PRECISION) + got_write


def chain_states(block_carry, block_write):
    size = lax.axis_size("ctx")
    me = lax.axis_index("ctx")
    levels = 0
    while size % 2 ** (levels + 1) == 0 and block_carry.shape[0] % 2 ** (levels + 1) == 0:
        levels += 1
    current = joined(block_carry, block_write)
    saved = []
    for level in range(levels):
        stride = 2**level
        upper = (me // stride) % 2 == 1
        half = current.shape[0] // 2
        mine = jnp.where(upper, current[half:], current[:half])
        other = jnp.where(upper, current[:half], current[half:])
        got = lax.ppermute(other, "ctx", [(i, i ^ stride) for i in range(size)])
        earlier = jnp.where(upper, got, mine)
        later = jnp.where(upper, mine, got)
        saved.append((upper, earlier))
        current = joined(*compose(split(earlier), split(later)))
    state = exclusive_scan(*split(current), size, 2**levels)
    for level in reversed(range(levels)):
        stride = 2**level
        upper, earlier = saved[level]
        earlier_carry, earlier_write = split(earlier)
        after = jnp.matmul(earlier_carry, state, precision=FULL_PRECISION) + earlier_write
        mine = jnp.where(upper, after, state)
        other = jnp.where(upper, state, after)
        got = lax.ppermute(other, "ctx", [(i, i ^ stride) for i in range(size)])
        state = jnp.where(
            upper, jnp.concatenate([got, mine], axis=0), jnp.concatenate([mine, got], axis=0)
        )
    return state


def gated_norm(core_rows, output_gate, norm_gain):
    token_count = core_rows.shape[0]
    head_count = core_rows.shape[1] // DV
    core_f = core_rows.astype(jnp.float32).reshape(token_count, head_count, DV)
    inv_rms = lax.rsqrt(jnp.mean(core_f * core_f, axis=-1, keepdims=True) + 1e-06)
    gate_f = output_gate.astype(jnp.float32).reshape(token_count, head_count, DV)
    gated_rows = core_f * inv_rms * norm_gain.astype(jnp.float32) * jax.nn.silu(gate_f)
    return gated_rows.reshape(token_count, head_count * DV).astype(jnp.bfloat16)


def head_swap(rows):
    width = rows.shape[-1] // 2
    first = lax.axis_index("head") == 0
    own = jnp.where(first, rows[..., :width], rows[..., width:])
    sent = jnp.where(first, rows[..., width:], rows[..., :width])
    got = lax.ppermute(sent, "head", [(0, 1), (1, 0)])
    axis = rows.ndim - 2
    return jnp.where(
        first, jnp.concatenate([own, got], axis), jnp.concatenate([got, own], axis)
    )


def head_return(rows):
    tokens = rows.shape[0] // 2
    first = lax.axis_index("head") == 0
    own = jnp.where(first, rows[:tokens], rows[tokens:])
    sent = jnp.where(first, rows[tokens:], rows[:tokens])
    got = lax.ppermute(sent, "head", [(0, 1), (1, 0)])
    return jnp.where(first, jnp.concatenate([own, got], 1), jnp.concatenate([got, own], 1))


def head_inputs(pieces_in):
    parts = lax.axis_size("head")
    if parts == 2:
        query_rows, key_rows, value_rows, beta_logit, log_decay = pieces_in
        query_key = head_swap(jnp.stack([query_rows, key_rows]))
        gates = head_swap(jnp.stack([beta_logit, log_decay]))
        return [query_key[0], query_key[1], head_swap(value_rows), gates[0], gates[1]]
    tokens = pieces_in[0].shape[0]
    widths = [part.shape[1] // parts for part in pieces_in]
    packed = jnp.concatenate(
        [part.reshape(tokens, parts, width) for part, width in zip(pieces_in, widths)], axis=-1
    )
    packed = lax.all_to_all(packed, "head", split_axis=1, concat_axis=0, tiled=True)
    packed = packed.reshape(tokens * parts, sum(widths))
    ends = [sum(widths[: i + 1]) for i in range(len(widths))]
    return [packed[:, end - width : end] for end, width in zip(ends, widths)]


def head_outputs(rows):
    if lax.axis_size("head") == 2:
        return head_return(rows)
    return lax.all_to_all(rows, "head", split_axis=0, concat_axis=1, tiled=True)


def on_device(query_rows, key_rows, value_rows, output_gate, beta_logit, log_decay, norm_gain):
    q_head, k_head, v_head, b_head, d_head = head_inputs(
        [query_rows, key_rows, value_rows, beta_logit, log_decay]
    )
    key_unit, value_f, beta_gate, decay_log = arrange(k_head, v_head, b_head, d_head)
    group_size = value_f.shape[0] // key_unit.shape[0]
    pieces = span_pass(key_unit, value_f, beta_gate, decay_log, group_size)
    query_unit = arrange_query(q_head)
    fixed, scaled, total_carry, total_write = span_prep(query_unit, key_unit, group_size, pieces)
    state_in = chain_states(total_carry, total_write)
    core_out = span_out(fixed, scaled, state_in)
    core_rows = to_rows(core_out).astype(jnp.bfloat16)
    if lax.axis_size("head") != 2:
        return gated_norm(head_outputs(core_rows), output_gate, norm_gain)
    width = output_gate.shape[1] // 2
    tokens = output_gate.shape[0]
    first = lax.axis_index("head") == 0
    own_gate = jnp.where(first, output_gate[:, :width], output_gate[:, width:])
    sent_gate = jnp.where(first, output_gate[:, width:], output_gate[:, :width])
    sent_gate, v_head = lax.optimization_barrier((sent_gate, v_head))
    got_gate = lax.ppermute(sent_gate, "head", [(0, 1), (1, 0)])
    own_core = jnp.where(first, core_rows[:tokens], core_rows[tokens:])
    sent_core = jnp.where(first, core_rows[tokens:], core_rows[:tokens])
    got = lax.ppermute(gated_norm(sent_core, got_gate, norm_gain), "head", [(0, 1), (1, 0)])
    own = gated_norm(own_core, own_gate, norm_gain)
    return jnp.where(first, jnp.concatenate([own, got], 1), jnp.concatenate([got, own], 1))


def solution(mesh):
    placed = (
        P(("ctx", "head"), None),
        P(("ctx", "head"), None),
        P(("ctx", "head"), None),
        P(("ctx", "head"), None),
        P(("ctx", "head"), None),
        P(("ctx", "head"), None),
        P(),
    )
    return jax.shard_map(
        on_device, mesh=mesh, in_specs=placed, out_specs=P(("ctx", "head"), None), check_vma=False
    )
```

```python
import jax
import jax.numpy as jnp
from jax import lax
from jax.sharding import PartitionSpec as P

DK = 128
DV = 128
SPAN = 128


FULL_PRECISION = lax.Precision.HIGH
LOCAL_PRECISION = lax.Precision.HIGH


def unit_rows(rows):
    return rows * lax.rsqrt(jnp.sum(rows * rows, axis=-1, keepdims=True) + 1e-06)


def compose(earlier, later):
    return (
        jnp.matmul(later[0], earlier[0], precision=FULL_PRECISION),
        jnp.matmul(later[0], earlier[1], precision=FULL_PRECISION) + later[1],
    )


def arrange(key_part, value_part, beta_part, decay_part):
    blocks = key_part.shape[0] // SPAN
    key_heads = key_part.shape[1] // DK
    value_heads = value_part.shape[1] // DV
    key_unit = unit_rows(
        key_part.astype(jnp.float32).reshape(blocks, SPAN, key_heads, DK)
    ).transpose(2, 0, 1, 3)
    value_f = (
        value_part.astype(jnp.float32).reshape(blocks, SPAN, value_heads, DV).transpose(2, 0, 1, 3)
    )
    beta_gate = (
        jax.nn.sigmoid(beta_part.astype(jnp.float32))
        .reshape(blocks, SPAN, value_heads)
        .transpose(2, 0, 1)
    )
    decay_log = decay_part.astype(jnp.float32).reshape(blocks, SPAN, value_heads).transpose(2, 0, 1)
    return (key_unit, value_f, beta_gate, decay_log)


def arrange_query(query_part):
    blocks = query_part.shape[0] // SPAN
    key_heads = query_part.shape[1] // DK
    query_f = query_part.astype(jnp.float32).reshape(blocks, SPAN, key_heads, DK)
    return (unit_rows(query_f) * DK ** (-0.5)).transpose(2, 0, 1, 3)


def unit_lower_inverse(strictly_lower):
    inverse = jnp.eye(SPAN, dtype=jnp.float32) - strictly_lower
    power = jnp.matmul(strictly_lower, strictly_lower, precision=LOCAL_PRECISION)
    covered = 2
    while covered < SPAN:
        if 2 * covered < SPAN:
            both = jnp.matmul(
                jnp.concatenate([inverse, power], axis=-2), power, precision=LOCAL_PRECISION
            )
            inverse = inverse + both[..., :SPAN, :]
            power = both[..., SPAN:, :]
        else:
            inverse = inverse + jnp.matmul(inverse, power, precision=LOCAL_PRECISION)
        covered = covered * 2
    return inverse


def span_pass(key_unit, value_f, beta_gate, decay_log, group_size):
    rowpos = lax.broadcasted_iota(jnp.int32, (SPAN, SPAN), 0)
    colpos = lax.broadcasted_iota(jnp.int32, (SPAN, SPAN), 1)
    cum_log = jnp.cumsum(decay_log, axis=2)
    spread = cum_log[..., :, None] - cum_log[..., None, :]
    strict = jnp.exp(jnp.where(colpos < rowpos, spread, -jnp.inf))
    key_inner = jnp.repeat(
        jnp.einsum("hmik,hmjk->hmij", key_unit, key_unit, precision=LOCAL_PRECISION),
        group_size,
        axis=0,
    )
    inverse = unit_lower_inverse(beta_gate[..., :, None] * strict * key_inner)
    wide_keys = jnp.repeat(key_unit, group_size, axis=0)
    targets = jnp.concatenate(
        [beta_gate[..., None] * value_f, (beta_gate * jnp.exp(cum_log))[..., None] * wide_keys],
        axis=-1,
    )
    solved = jnp.matmul(inverse, targets, precision=LOCAL_PRECISION)
    written = solved[..., :DV]
    weights = solved[..., DV:]
    faded_keys = wide_keys * jnp.exp(cum_log[..., -1:] - cum_log)[..., None]
    tail_decay = jnp.exp(cum_log[..., -1])
    carry_mat = tail_decay[..., None, None] * jnp.eye(DK, dtype=jnp.float32) - jnp.einsum(
        "hmck,hmcj->hmkj", faded_keys, weights, precision=LOCAL_PRECISION
    )
    write_mat = jnp.einsum("hmck,hmcv->hmkv", faded_keys, written, precision=LOCAL_PRECISION)
    return (cum_log, spread, written, weights, carry_mat, write_mat)


def span_prep(query_unit, key_unit, group_size, pieces):
    cum_log, spread, written, weights, carry_mat, write_mat = pieces
    rowpos = lax.broadcasted_iota(jnp.int32, (SPAN, SPAN), 0)
    colpos = lax.broadcasted_iota(jnp.int32, (SPAN, SPAN), 1)
    within = jnp.exp(jnp.where(colpos <= rowpos, spread, -jnp.inf))
    scores = (
        jnp.repeat(
            jnp.einsum("hmik,hmjk->hmij", query_unit, key_unit, precision=LOCAL_PRECISION),
            group_size,
            axis=0,
        )
        * within
    )
    wide_query = jnp.repeat(query_unit, group_size, axis=0)
    inner = jnp.einsum("hmij,hmjv->hmiv", scores, written, precision=LOCAL_PRECISION)
    reach = wide_query * jnp.exp(cum_log)[..., None] - jnp.einsum(
        "hmij,hmjk->hmik", scores, weights, precision=LOCAL_PRECISION
    )
    blocks = carry_mat.shape[1]
    fixed, scaled = ([inner[:, 0]], [reach[:, 0]])
    reach_map, reach_add = (carry_mat[:, 0], write_mat[:, 0])
    for m in range(1, blocks):
        fixed.append(
            inner[:, m] + jnp.matmul(reach[:, m], reach_add, precision=LOCAL_PRECISION)
        )
        scaled.append(jnp.matmul(reach[:, m], reach_map, precision=LOCAL_PRECISION))
        reach_map, reach_add = compose((reach_map, reach_add), (carry_mat[:, m], write_mat[:, m]))
    return (jnp.stack(fixed, axis=1), jnp.stack(scaled, axis=1), reach_map, reach_add)


def span_out(fixed, scaled, state_in):
    return fixed + jnp.einsum("hmck,hkv->hmcv", scaled, state_in, precision=FULL_PRECISION)


def to_rows(core_out):
    head_count, blocks = (core_out.shape[0], core_out.shape[1])
    return core_out.transpose(1, 2, 0, 3).reshape(blocks * SPAN, head_count * DV)


def joined(carry, write):
    return jnp.concatenate([carry, write], axis=-1)


def split(both):
    return (both[..., :DK], both[..., DK:])


def exclusive_scan(carry, write, size, stride):
    count = size // stride
    if count == 1:
        return jnp.zeros_like(write)
    rounds = 0
    while 2 ** (rounds + 1) < count:
        rounds += 1
    shift = 1
    for _ in range(rounds):
        pairs = [(i, i + shift * stride) for i in range(size - shift * stride)]
        got = lax.ppermute(joined(carry, write), "ctx", pairs)
        carry, write = compose(split(got), (carry, write))
        shift *= 2
    near = [(i, i + stride) for i in range(size - stride)]
    far = 2**rounds + 1
    if far >= count:
        return lax.ppermute(write, "ctx", near)
    got_carry, got_write = split(lax.ppermute(joined(carry, write), "ctx", near))
    far_write = lax.ppermute(
        write, "ctx", [(i, i + far * stride) for i in range(size - far * stride)]
    )
    return jnp.matmul(got_carry, far_write, precision=FULL_PRECISION) + got_write


def chain_states(block_carry, block_write):
    size = lax.axis_size("ctx")
    me = lax.axis_index("ctx")
    levels = 0
    while size % 2 ** (levels + 1) == 0 and block_carry.shape[0] % 2 ** (levels + 1) == 0:
        levels += 1
    current = joined(block_carry, block_write)
    saved = []
    for level in range(levels):
        stride = 2**level
        upper = (me // stride) % 2 == 1
        half = current.shape[0] // 2
        mine = jnp.where(upper, current[half:], current[:half])
        other = jnp.where(upper, current[:half], current[half:])
        got = lax.ppermute(other, "ctx", [(i, i ^ stride) for i in range(size)])

        def ordered(earlier, later):
            return (joined(*compose(split(earlier), split(later))), earlier)

        current, earlier = lax.cond(
            upper, lambda a, b: ordered(b, a), lambda a, b: ordered(a, b), mine, got
        )
        saved.append((upper, earlier))
    state = exclusive_scan(*split(current), size, 2**levels)
    for level in reversed(range(levels)):
        stride = 2**level
        upper, earlier = saved[level]
        earlier_carry, earlier_write = split(earlier)
        after = jnp.matmul(earlier_carry, state, precision=FULL_PRECISION) + earlier_write
        mine = jnp.where(upper, after, state)
        other = jnp.where(upper, state, after)
        got = lax.ppermute(other, "ctx", [(i, i ^ stride) for i in range(size)])
        state = jnp.where(
            upper, jnp.concatenate([got, mine], axis=0), jnp.concatenate([mine, got], axis=0)
        )
    return state


def gated_norm(core_rows, output_gate, norm_gain):
    token_count = core_rows.shape[0]
    head_count = core_rows.shape[1] // DV
    core_f = core_rows.astype(jnp.float32).reshape(token_count, head_count, DV)
    inv_rms = lax.rsqrt(jnp.mean(core_f * core_f, axis=-1, keepdims=True) + 1e-06)
    gate_f = output_gate.astype(jnp.float32).reshape(token_count, head_count, DV)
    gated_rows = core_f * inv_rms * norm_gain.astype(jnp.float32) * jax.nn.silu(gate_f)
    return gated_rows.reshape(token_count, head_count * DV).astype(jnp.bfloat16)


def head_swap(rows):
    width = rows.shape[-1] // 2
    first = lax.axis_index("head") == 0
    own = jnp.where(first, rows[..., :width], rows[..., width:])
    sent = jnp.where(first, rows[..., width:], rows[..., :width])
    got = lax.ppermute(sent, "head", [(0, 1), (1, 0)])
    axis = rows.ndim - 2
    return jnp.where(
        first, jnp.concatenate([own, got], axis), jnp.concatenate([got, own], axis)
    )


def head_return(rows):
    tokens = rows.shape[0] // 2
    first = lax.axis_index("head") == 0
    own = jnp.where(first, rows[:tokens], rows[tokens:])
    sent = jnp.where(first, rows[tokens:], rows[:tokens])
    got = lax.ppermute(sent, "head", [(0, 1), (1, 0)])
    return jnp.where(first, jnp.concatenate([own, got], 1), jnp.concatenate([got, own], 1))


def head_inputs(pieces_in):
    parts = lax.axis_size("head")
    if parts == 2:
        query_rows, key_rows, value_rows, beta_logit, log_decay = pieces_in
        query_key = head_swap(jnp.stack([query_rows, key_rows]))
        gates = head_swap(jnp.stack([beta_logit, log_decay]))
        return [query_key[0], query_key[1], head_swap(value_rows), gates[0], gates[1]]
    tokens = pieces_in[0].shape[0]
    widths = [part.shape[1] // parts for part in pieces_in]
    packed = jnp.concatenate(
        [part.reshape(tokens, parts, width) for part, width in zip(pieces_in, widths)], axis=-1
    )
    packed = lax.all_to_all(packed, "head", split_axis=1, concat_axis=0, tiled=True)
    packed = packed.reshape(tokens * parts, sum(widths))
    ends = [sum(widths[: i + 1]) for i in range(len(widths))]
    return [packed[:, end - width : end] for end, width in zip(ends, widths)]


def head_outputs(rows):
    if lax.axis_size("head") == 2:
        return head_return(rows)
    return lax.all_to_all(rows, "head", split_axis=0, concat_axis=1, tiled=True)


def on_device(query_rows, key_rows, value_rows, output_gate, beta_logit, log_decay, norm_gain):
    q_head, k_head, v_head, b_head, d_head = head_inputs(
        [query_rows, key_rows, value_rows, beta_logit, log_decay]
    )
    key_unit, value_f, beta_gate, decay_log = arrange(k_head, v_head, b_head, d_head)
    group_size = value_f.shape[0] // key_unit.shape[0]
    pieces = span_pass(key_unit, value_f, beta_gate, decay_log, group_size)
    query_unit = arrange_query(q_head)
    fixed, scaled, total_carry, total_write = span_prep(query_unit, key_unit, group_size, pieces)
    state_in = chain_states(total_carry, total_write)
    core_out = span_out(fixed, scaled, state_in)
    core_rows = head_outputs(to_rows(core_out).astype(jnp.bfloat16))
    return gated_norm(core_rows, output_gate, norm_gain)


def solution(mesh):
    placed = (
        P(("ctx", "head"), None),
        P(("ctx", "head"), None),
        P(("ctx", "head"), None),
        P(("ctx", "head"), None),
        P(("ctx", "head"), None),
        P(("ctx", "head"), None),
        P(),
    )
    return jax.shard_map(
        on_device, mesh=mesh, in_specs=placed, out_specs=P(("ctx", "head"), None), check_vma=False
    )
```

```python
import jax
import jax.numpy as jnp
from jax import lax
from jax.sharding import PartitionSpec as P

DK = 128
DV = 128
SPAN = 128


FULL_PRECISION = lax.Precision.HIGH
LOCAL_PRECISION = lax.Precision.HIGH


def unit_rows(rows):
    return rows * lax.rsqrt(jnp.sum(rows * rows, axis=-1, keepdims=True) + 1e-06)


def compose(earlier, later):
    return (
        jnp.matmul(later[0], earlier[0], precision=FULL_PRECISION),
        jnp.matmul(later[0], earlier[1], precision=FULL_PRECISION) + later[1],
    )


def arrange(key_part, value_part, beta_part, decay_part):
    blocks = key_part.shape[0] // SPAN
    key_heads = key_part.shape[1] // DK
    value_heads = value_part.shape[1] // DV
    key_unit = unit_rows(
        key_part.astype(jnp.float32).reshape(blocks, SPAN, key_heads, DK)
    ).transpose(2, 0, 1, 3)
    value_f = (
        value_part.astype(jnp.float32).reshape(blocks, SPAN, value_heads, DV).transpose(2, 0, 1, 3)
    )
    beta_gate = (
        jax.nn.sigmoid(beta_part.astype(jnp.float32))
        .reshape(blocks, SPAN, value_heads)
        .transpose(2, 0, 1)
    )
    decay_log = decay_part.astype(jnp.float32).reshape(blocks, SPAN, value_heads).transpose(2, 0, 1)
    return (key_unit, value_f, beta_gate, decay_log)


def arrange_query(query_part):
    blocks = query_part.shape[0] // SPAN
    key_heads = query_part.shape[1] // DK
    query_f = query_part.astype(jnp.float32).reshape(blocks, SPAN, key_heads, DK)
    return (unit_rows(query_f) * DK ** (-0.5)).transpose(2, 0, 1, 3)


def unit_lower_inverse(strictly_lower):
    inverse = jnp.eye(SPAN, dtype=jnp.float32) - strictly_lower
    power = jnp.matmul(strictly_lower, strictly_lower, precision=LOCAL_PRECISION)
    covered = 2
    while covered < SPAN:
        if 2 * covered < SPAN:
            both = jnp.matmul(
                jnp.concatenate([inverse, power], axis=-2), power, precision=LOCAL_PRECISION
            )
            inverse = inverse + both[..., :SPAN, :]
            power = both[..., SPAN:, :]
        else:
            inverse = inverse + jnp.matmul(inverse, power, precision=LOCAL_PRECISION)
        covered = covered * 2
    return inverse


def span_pass(key_unit, value_f, beta_gate, decay_log, group_size):
    rowpos = lax.broadcasted_iota(jnp.int32, (SPAN, SPAN), 0)
    colpos = lax.broadcasted_iota(jnp.int32, (SPAN, SPAN), 1)
    cum_log = jnp.cumsum(decay_log, axis=2)
    spread = cum_log[..., :, None] - cum_log[..., None, :]
    strict = jnp.exp(jnp.where(colpos < rowpos, spread, -jnp.inf))
    key_inner = jnp.repeat(
        jnp.einsum("hmik,hmjk->hmij", key_unit, key_unit, precision=LOCAL_PRECISION),
        group_size,
        axis=0,
    )
    inverse = unit_lower_inverse(beta_gate[..., :, None] * strict * key_inner)
    wide_keys = jnp.repeat(key_unit, group_size, axis=0)
    targets = jnp.concatenate(
        [beta_gate[..., None] * value_f, (beta_gate * jnp.exp(cum_log))[..., None] * wide_keys],
        axis=-1,
    )
    solved = jnp.matmul(inverse, targets, precision=LOCAL_PRECISION)
    written = solved[..., :DV]
    weights = solved[..., DV:]
    faded_keys = wide_keys * jnp.exp(cum_log[..., -1:] - cum_log)[..., None]
    tail_decay = jnp.exp(cum_log[..., -1])
    maps = jnp.einsum("hmck,hmcj->hmkj", faded_keys, solved, precision=LOCAL_PRECISION)
    carry_mat = tail_decay[..., None, None] * jnp.eye(DK, dtype=jnp.float32) - maps[..., DV:]
    write_mat = maps[..., :DV]
    return (cum_log, spread, written, weights, carry_mat, write_mat)


def span_prep(query_unit, key_unit, group_size, pieces):
    cum_log, spread, written, weights, carry_mat, write_mat = pieces
    rowpos = lax.broadcasted_iota(jnp.int32, (SPAN, SPAN), 0)
    colpos = lax.broadcasted_iota(jnp.int32, (SPAN, SPAN), 1)
    within = jnp.exp(jnp.where(colpos <= rowpos, spread, -jnp.inf))
    scores = (
        jnp.repeat(
            jnp.einsum("hmik,hmjk->hmij", query_unit, key_unit, precision=LOCAL_PRECISION),
            group_size,
            axis=0,
        )
        * within
    )
    wide_query = jnp.repeat(query_unit, group_size, axis=0)
    inner = jnp.einsum("hmij,hmjv->hmiv", scores, written, precision=LOCAL_PRECISION)
    reach = wide_query * jnp.exp(cum_log)[..., None] - jnp.einsum(
        "hmij,hmjk->hmik", scores, weights, precision=LOCAL_PRECISION
    )
    blocks = carry_mat.shape[1]
    fixed, scaled = ([inner[:, 0]], [reach[:, 0]])
    reach_map, reach_add = (carry_mat[:, 0], write_mat[:, 0])
    for m in range(1, blocks):
        fixed.append(
            inner[:, m] + jnp.matmul(reach[:, m], reach_add, precision=LOCAL_PRECISION)
        )
        scaled.append(jnp.matmul(reach[:, m], reach_map, precision=LOCAL_PRECISION))
        reach_map, reach_add = compose((reach_map, reach_add), (carry_mat[:, m], write_mat[:, m]))
    return (jnp.stack(fixed, axis=1), jnp.stack(scaled, axis=1), reach_map, reach_add)


def span_out(fixed, scaled, state_in):
    return fixed + jnp.einsum("hmck,hkv->hmcv", scaled, state_in, precision=FULL_PRECISION)


def to_rows(core_out):
    head_count, blocks = (core_out.shape[0], core_out.shape[1])
    return core_out.transpose(1, 2, 0, 3).reshape(blocks * SPAN, head_count * DV)


def joined(carry, write):
    return jnp.concatenate([carry, write], axis=-1)


def split(both):
    return (both[..., :DK], both[..., DK:])


def exclusive_scan(carry, write, size, stride):
    count = size // stride
    if count == 1:
        return jnp.zeros_like(write)
    rounds = 0
    while 2 ** (rounds + 1) < count:
        rounds += 1
    shift = 1
    for _ in range(rounds):
        pairs = [(i, i + shift * stride) for i in range(size - shift * stride)]
        got = lax.ppermute(joined(carry, write), "ctx", pairs)
        carry, write = compose(split(got), (carry, write))
        shift *= 2
    near = [(i, i + stride) for i in range(size - stride)]
    far = 2**rounds + 1
    if far >= count:
        return lax.ppermute(write, "ctx", near)
    got_carry, got_write = split(lax.ppermute(joined(carry, write), "ctx", near))
    far_write = lax.ppermute(
        write, "ctx", [(i, i + far * stride) for i in range(size - far * stride)]
    )
    return jnp.matmul(got_carry, far_write, precision=FULL_PRECISION) + got_write


def chain_states(block_carry, block_write):
    size = lax.axis_size("ctx")
    me = lax.axis_index("ctx")
    levels = 0
    while size % 2 ** (levels + 1) == 0 and block_carry.shape[0] % 2 ** (levels + 1) == 0:
        levels += 1
    current = joined(block_carry, block_write)
    saved = []
    for level in range(levels):
        stride = 2**level
        upper = (me // stride) % 2 == 1
        half = current.shape[0] // 2
        mine = jnp.where(upper, current[half:], current[:half])
        other = jnp.where(upper, current[:half], current[half:])
        got = lax.ppermute(other, "ctx", [(i, i ^ stride) for i in range(size)])
        earlier = jnp.where(upper, got, mine)
        later = jnp.where(upper, mine, got)
        saved.append((upper, earlier))
        current = joined(*compose(split(earlier), split(later)))
    state = exclusive_scan(*split(current), size, 2**levels)
    for level in reversed(range(levels)):
        stride = 2**level
        upper, earlier = saved[level]
        earlier_carry, earlier_write = split(earlier)
        after = jnp.matmul(earlier_carry, state, precision=FULL_PRECISION) + earlier_write
        mine = jnp.where(upper, after, state)
        other = jnp.where(upper, state, after)
        got = lax.ppermute(other, "ctx", [(i, i ^ stride) for i in range(size)])
        state = jnp.where(
            upper, jnp.concatenate([got, mine], axis=0), jnp.concatenate([mine, got], axis=0)
        )
    return state


def gated_norm(core_rows, output_gate, norm_gain):
    token_count = core_rows.shape[0]
    head_count = core_rows.shape[1] // DV
    core_f = core_rows.astype(jnp.float32).reshape(token_count, head_count, DV)
    inv_rms = lax.rsqrt(jnp.mean(core_f * core_f, axis=-1, keepdims=True) + 1e-06)
    gate_f = output_gate.astype(jnp.float32).reshape(token_count, head_count, DV)
    gated_rows = core_f * inv_rms * norm_gain.astype(jnp.float32) * jax.nn.silu(gate_f)
    return gated_rows.reshape(token_count, head_count * DV).astype(jnp.bfloat16)


def head_swap(rows):
    width = rows.shape[-1] // 2
    first = lax.axis_index("head") == 0
    own = jnp.where(first, rows[..., :width], rows[..., width:])
    sent = jnp.where(first, rows[..., width:], rows[..., :width])
    got = lax.ppermute(sent, "head", [(0, 1), (1, 0)])
    axis = rows.ndim - 2
    return jnp.where(
        first, jnp.concatenate([own, got], axis), jnp.concatenate([got, own], axis)
    )


def head_return(rows):
    tokens = rows.shape[0] // 2
    first = lax.axis_index("head") == 0
    own = jnp.where(first, rows[:tokens], rows[tokens:])
    sent = jnp.where(first, rows[tokens:], rows[:tokens])
    got = lax.ppermute(sent, "head", [(0, 1), (1, 0)])
    return jnp.where(first, jnp.concatenate([own, got], 1), jnp.concatenate([got, own], 1))


def head_inputs(pieces_in):
    parts = lax.axis_size("head")
    if parts == 2:
        query_rows, key_rows, value_rows, beta_logit, log_decay = pieces_in
        query_key = head_swap(jnp.stack([query_rows, key_rows]))
        gates = head_swap(jnp.stack([beta_logit, log_decay]))
        return [query_key[0], query_key[1], head_swap(value_rows), gates[0], gates[1]]
    tokens = pieces_in[0].shape[0]
    widths = [part.shape[1] // parts for part in pieces_in]
    packed = jnp.concatenate(
        [part.reshape(tokens, parts, width) for part, width in zip(pieces_in, widths)], axis=-1
    )
    packed = lax.all_to_all(packed, "head", split_axis=1, concat_axis=0, tiled=True)
    packed = packed.reshape(tokens * parts, sum(widths))
    ends = [sum(widths[: i + 1]) for i in range(len(widths))]
    return [packed[:, end - width : end] for end, width in zip(ends, widths)]


def head_outputs(rows):
    if lax.axis_size("head") == 2:
        return head_return(rows)
    return lax.all_to_all(rows, "head", split_axis=0, concat_axis=1, tiled=True)


def on_device(query_rows, key_rows, value_rows, output_gate, beta_logit, log_decay, norm_gain):
    q_head, k_head, v_head, b_head, d_head = head_inputs(
        [query_rows, key_rows, value_rows, beta_logit, log_decay]
    )
    key_unit, value_f, beta_gate, decay_log = arrange(k_head, v_head, b_head, d_head)
    group_size = value_f.shape[0] // key_unit.shape[0]
    pieces = span_pass(key_unit, value_f, beta_gate, decay_log, group_size)
    query_unit = arrange_query(q_head)
    fixed, scaled, total_carry, total_write = span_prep(query_unit, key_unit, group_size, pieces)
    state_in = chain_states(total_carry, total_write)
    core_out = span_out(fixed, scaled, state_in)
    core_rows = head_outputs(to_rows(core_out).astype(jnp.bfloat16))
    return gated_norm(core_rows, output_gate, norm_gain)


def solution(mesh):
    placed = (
        P(("ctx", "head"), None),
        P(("ctx", "head"), None),
        P(("ctx", "head"), None),
        P(("ctx", "head"), None),
        P(("ctx", "head"), None),
        P(("ctx", "head"), None),
        P(),
    )
    return jax.shard_map(
        on_device, mesh=mesh, in_specs=placed, out_specs=P(("ctx", "head"), None), check_vma=False
    )
```

```python
import jax
import jax.numpy as jnp
from jax import lax
from jax.sharding import PartitionSpec as P

DK = 128
DV = 128
SPAN = 128


FULL_PRECISION = lax.Precision.HIGH
LOCAL_PRECISION = lax.Precision.HIGH


def unit_rows(rows):
    return rows * lax.rsqrt(jnp.sum(rows * rows, axis=-1, keepdims=True) + 1e-06)


def compose(earlier, later):
    both = jnp.matmul(
        later[0], jnp.concatenate([earlier[0], earlier[1]], axis=-1), precision=FULL_PRECISION
    )
    return (both[..., : earlier[0].shape[-1]], both[..., earlier[0].shape[-1] :] + later[1])


def arrange(key_part, value_part, beta_part, decay_part):
    blocks = key_part.shape[0] // SPAN
    key_heads = key_part.shape[1] // DK
    value_heads = value_part.shape[1] // DV
    key_unit = unit_rows(
        key_part.astype(jnp.float32).reshape(blocks, SPAN, key_heads, DK)
    ).transpose(2, 0, 1, 3)
    value_f = (
        value_part.astype(jnp.float32).reshape(blocks, SPAN, value_heads, DV).transpose(2, 0, 1, 3)
    )
    beta_gate = (
        jax.nn.sigmoid(beta_part.astype(jnp.float32))
        .reshape(blocks, SPAN, value_heads)
        .transpose(2, 0, 1)
    )
    decay_log = decay_part.astype(jnp.float32).reshape(blocks, SPAN, value_heads).transpose(2, 0, 1)
    return (key_unit, value_f, beta_gate, decay_log)


def arrange_query(query_part):
    blocks = query_part.shape[0] // SPAN
    key_heads = query_part.shape[1] // DK
    query_f = query_part.astype(jnp.float32).reshape(blocks, SPAN, key_heads, DK)
    return (unit_rows(query_f) * DK ** (-0.5)).transpose(2, 0, 1, 3)


def unit_lower_inverse(strictly_lower):
    inverse = jnp.eye(SPAN, dtype=jnp.float32) - strictly_lower
    power = jnp.matmul(strictly_lower, strictly_lower, precision=LOCAL_PRECISION)
    covered = 2
    while covered < SPAN:
        if 2 * covered < SPAN:
            both = jnp.matmul(
                jnp.concatenate([inverse, power], axis=-2), power, precision=LOCAL_PRECISION
            )
            inverse = inverse + both[..., :SPAN, :]
            power = both[..., SPAN:, :]
        else:
            inverse = inverse + jnp.matmul(inverse, power, precision=LOCAL_PRECISION)
        covered = covered * 2
    return inverse


def span_pass(key_unit, value_f, beta_gate, decay_log, group_size):
    rowpos = lax.broadcasted_iota(jnp.int32, (SPAN, SPAN), 0)
    colpos = lax.broadcasted_iota(jnp.int32, (SPAN, SPAN), 1)
    cum_log = jnp.cumsum(decay_log, axis=2)
    spread = cum_log[..., :, None] - cum_log[..., None, :]
    strict = jnp.exp(jnp.where(colpos < rowpos, spread, -jnp.inf))
    key_inner = jnp.repeat(
        jnp.einsum("hmik,hmjk->hmij", key_unit, key_unit, precision=LOCAL_PRECISION),
        group_size,
        axis=0,
    )
    inverse = unit_lower_inverse(beta_gate[..., :, None] * strict * key_inner)
    wide_keys = jnp.repeat(key_unit, group_size, axis=0)
    targets = jnp.concatenate(
        [beta_gate[..., None] * value_f, (beta_gate * jnp.exp(cum_log))[..., None] * wide_keys],
        axis=-1,
    )
    solved = jnp.matmul(inverse, targets, precision=LOCAL_PRECISION)
    written = solved[..., :DV]
    weights = solved[..., DV:]
    faded_keys = wide_keys * jnp.exp(cum_log[..., -1:] - cum_log)[..., None]
    tail_decay = jnp.exp(cum_log[..., -1])
    maps = jnp.einsum("hmck,hmcj->hmkj", faded_keys, solved, precision=LOCAL_PRECISION)
    carry_mat = tail_decay[..., None, None] * jnp.eye(DK, dtype=jnp.float32) - maps[..., DV:]
    write_mat = maps[..., :DV]
    return (cum_log, spread, written, weights, carry_mat, write_mat)


def span_prep(query_unit, key_unit, group_size, pieces):
    cum_log, spread, written, weights, carry_mat, write_mat = pieces
    rowpos = lax.broadcasted_iota(jnp.int32, (SPAN, SPAN), 0)
    colpos = lax.broadcasted_iota(jnp.int32, (SPAN, SPAN), 1)
    within = jnp.exp(jnp.where(colpos <= rowpos, spread, -jnp.inf))
    scores = (
        jnp.repeat(
            jnp.einsum("hmik,hmjk->hmij", query_unit, key_unit, precision=LOCAL_PRECISION),
            group_size,
            axis=0,
        )
        * within
    )
    wide_query = jnp.repeat(query_unit, group_size, axis=0)
    mixed = jnp.einsum(
        "hmij,hmjv->hmiv",
        scores,
        jnp.concatenate([written, weights], axis=-1),
        precision=LOCAL_PRECISION,
    )
    inner = mixed[..., :DV]
    reach = wide_query * jnp.exp(cum_log)[..., None] - mixed[..., DV:]
    blocks = carry_mat.shape[1]
    fixed, scaled = ([inner[:, 0]], [reach[:, 0]])
    reach_map, reach_add = (carry_mat[:, 0], write_mat[:, 0])
    for m in range(1, blocks):
        both = jnp.matmul(
            reach[:, m], jnp.concatenate([reach_add, reach_map], axis=-1), precision=LOCAL_PRECISION
        )
        fixed.append(inner[:, m] + both[..., :DV])
        scaled.append(both[..., DV:])
        reach_map, reach_add = compose((reach_map, reach_add), (carry_mat[:, m], write_mat[:, m]))
    return (jnp.stack(fixed, axis=1), jnp.stack(scaled, axis=1), reach_map, reach_add)


def span_out(fixed, scaled, state_in):
    return fixed + jnp.einsum("hmck,hkv->hmcv", scaled, state_in, precision=FULL_PRECISION)


def to_rows(core_out):
    head_count, blocks = (core_out.shape[0], core_out.shape[1])
    return core_out.transpose(1, 2, 0, 3).reshape(blocks * SPAN, head_count * DV)


def joined(carry, write):
    return jnp.concatenate([carry, write], axis=-1)


def split(both):
    return (both[..., :DK], both[..., DK:])


def exclusive_scan(carry, write, size, stride):
    count = size // stride
    if count == 1:
        return jnp.zeros_like(write)
    rounds = 0
    while 2 ** (rounds + 1) < count:
        rounds += 1
    shift = 1
    for _ in range(rounds):
        pairs = [(i, i + shift * stride) for i in range(size - shift * stride)]
        got = lax.ppermute(joined(carry, write), "ctx", pairs)
        carry, write = compose(split(got), (carry, write))
        shift *= 2
    near = [(i, i + stride) for i in range(size - stride)]
    far = 2**rounds + 1
    if far >= count:
        return lax.ppermute(write, "ctx", near)
    got_carry, got_write = split(lax.ppermute(joined(carry, write), "ctx", near))
    far_write = lax.ppermute(
        write, "ctx", [(i, i + far * stride) for i in range(size - far * stride)]
    )
    return jnp.matmul(got_carry, far_write, precision=FULL_PRECISION) + got_write


def chain_states(block_carry, block_write):
    size = lax.axis_size("ctx")
    me = lax.axis_index("ctx")
    levels = 0
    while size % 2 ** (levels + 1) == 0 and block_carry.shape[0] % 2 ** (levels + 1) == 0:
        levels += 1
    current = joined(block_carry, block_write)
    saved = []
    for level in range(levels):
        stride = 2**level
        upper = (me // stride) % 2 == 1
        half = current.shape[0] // 2
        mine = jnp.where(upper, current[half:], current[:half])
        other = jnp.where(upper, current[:half], current[half:])
        got = lax.ppermute(other, "ctx", [(i, i ^ stride) for i in range(size)])
        earlier = jnp.where(upper, got, mine)
        later = jnp.where(upper, mine, got)
        saved.append((upper, earlier))
        current = joined(*compose(split(earlier), split(later)))
    state = exclusive_scan(*split(current), size, 2**levels)
    for level in reversed(range(levels)):
        stride = 2**level
        upper, earlier = saved[level]
        earlier_carry, earlier_write = split(earlier)
        after = jnp.matmul(earlier_carry, state, precision=FULL_PRECISION) + earlier_write
        mine = jnp.where(upper, after, state)
        other = jnp.where(upper, state, after)
        got = lax.ppermute(other, "ctx", [(i, i ^ stride) for i in range(size)])
        state = jnp.where(
            upper, jnp.concatenate([got, mine], axis=0), jnp.concatenate([mine, got], axis=0)
        )
    return state


def gated_norm(core_rows, output_gate, norm_gain):
    token_count = core_rows.shape[0]
    head_count = core_rows.shape[1] // DV
    core_f = core_rows.astype(jnp.float32).reshape(token_count, head_count, DV)
    inv_rms = lax.rsqrt(jnp.mean(core_f * core_f, axis=-1, keepdims=True) + 1e-06)
    gate_f = output_gate.astype(jnp.float32).reshape(token_count, head_count, DV)
    gated_rows = core_f * inv_rms * norm_gain.astype(jnp.float32) * jax.nn.silu(gate_f)
    return gated_rows.reshape(token_count, head_count * DV).astype(jnp.bfloat16)


def head_swap(rows):
    width = rows.shape[-1] // 2
    first = lax.axis_index("head") == 0
    own = jnp.where(first, rows[..., :width], rows[..., width:])
    sent = jnp.where(first, rows[..., width:], rows[..., :width])
    got = lax.ppermute(sent, "head", [(0, 1), (1, 0)])
    axis = rows.ndim - 2
    return jnp.where(
        first, jnp.concatenate([own, got], axis), jnp.concatenate([got, own], axis)
    )


def head_return(rows):
    tokens = rows.shape[0] // 2
    first = lax.axis_index("head") == 0
    own = jnp.where(first, rows[:tokens], rows[tokens:])
    sent = jnp.where(first, rows[tokens:], rows[:tokens])
    got = lax.ppermute(sent, "head", [(0, 1), (1, 0)])
    return jnp.where(first, jnp.concatenate([own, got], 1), jnp.concatenate([got, own], 1))


def head_inputs(pieces_in):
    parts = lax.axis_size("head")
    if parts == 2:
        query_rows, key_rows, value_rows, beta_logit, log_decay = pieces_in
        query_key = head_swap(jnp.stack([query_rows, key_rows]))
        gates = head_swap(jnp.stack([beta_logit, log_decay]))
        return [query_key[0], query_key[1], head_swap(value_rows), gates[0], gates[1]]
    tokens = pieces_in[0].shape[0]
    widths = [part.shape[1] // parts for part in pieces_in]
    packed = jnp.concatenate(
        [part.reshape(tokens, parts, width) for part, width in zip(pieces_in, widths)], axis=-1
    )
    packed = lax.all_to_all(packed, "head", split_axis=1, concat_axis=0, tiled=True)
    packed = packed.reshape(tokens * parts, sum(widths))
    ends = [sum(widths[: i + 1]) for i in range(len(widths))]
    return [packed[:, end - width : end] for end, width in zip(ends, widths)]


def head_outputs(rows):
    if lax.axis_size("head") == 2:
        return head_return(rows)
    return lax.all_to_all(rows, "head", split_axis=0, concat_axis=1, tiled=True)


def on_device(query_rows, key_rows, value_rows, output_gate, beta_logit, log_decay, norm_gain):
    q_head, k_head, v_head, b_head, d_head = head_inputs(
        [query_rows, key_rows, value_rows, beta_logit, log_decay]
    )
    key_unit, value_f, beta_gate, decay_log = arrange(k_head, v_head, b_head, d_head)
    group_size = value_f.shape[0] // key_unit.shape[0]
    pieces = span_pass(key_unit, value_f, beta_gate, decay_log, group_size)
    query_unit = arrange_query(q_head)
    fixed, scaled, total_carry, total_write = span_prep(query_unit, key_unit, group_size, pieces)
    state_in = chain_states(total_carry, total_write)
    core_out = span_out(fixed, scaled, state_in)
    core_rows = head_outputs(to_rows(core_out).astype(jnp.bfloat16))
    return gated_norm(core_rows, output_gate, norm_gain)


def solution(mesh):
    placed = (
        P(("ctx", "head"), None),
        P(("ctx", "head"), None),
        P(("ctx", "head"), None),
        P(("ctx", "head"), None),
        P(("ctx", "head"), None),
        P(("ctx", "head"), None),
        P(),
    )
    return jax.shard_map(
        on_device, mesh=mesh, in_specs=placed, out_specs=P(("ctx", "head"), None), check_vma=False
    )
```

```python
import jax
import jax.numpy as jnp
from jax import lax
from jax.sharding import PartitionSpec as P

DK = 128
DV = 128
SPAN = 128


FULL_PRECISION = lax.Precision.HIGH
LOCAL_PRECISION = lax.Precision.HIGH


def unit_rows(rows):
    return rows * lax.rsqrt(jnp.sum(rows * rows, axis=-1, keepdims=True) + 1e-06)


def compose(earlier, later):
    both = jnp.matmul(
        later[0], jnp.concatenate([earlier[0], earlier[1]], axis=-1), precision=FULL_PRECISION
    )
    return (both[..., : earlier[0].shape[-1]], both[..., earlier[0].shape[-1] :] + later[1])


def compose_joined(earlier, later):
    lane = lax.broadcasted_iota(jnp.int32, later.shape, later.ndim - 1)
    return jnp.matmul(
        later[..., : later.shape[-2]], earlier, precision=FULL_PRECISION
    ) + jnp.where(lane >= later.shape[-2], later, 0.0)


def arrange(key_part, value_part, beta_part, decay_part):
    blocks = key_part.shape[0] // SPAN
    key_heads = key_part.shape[1] // DK
    value_heads = value_part.shape[1] // DV
    key_unit = unit_rows(
        key_part.astype(jnp.float32).reshape(blocks, SPAN, key_heads, DK)
    ).transpose(2, 0, 1, 3)
    value_f = (
        value_part.astype(jnp.float32).reshape(blocks, SPAN, value_heads, DV).transpose(2, 0, 1, 3)
    )
    beta_gate = (
        jax.nn.sigmoid(beta_part.astype(jnp.float32))
        .reshape(blocks, SPAN, value_heads)
        .transpose(2, 0, 1)
    )
    decay_log = decay_part.astype(jnp.float32).reshape(blocks, SPAN, value_heads).transpose(2, 0, 1)
    return (key_unit, value_f, beta_gate, decay_log)


def arrange_query(query_part):
    blocks = query_part.shape[0] // SPAN
    key_heads = query_part.shape[1] // DK
    query_f = query_part.astype(jnp.float32).reshape(blocks, SPAN, key_heads, DK)
    return (unit_rows(query_f) * DK ** (-0.5)).transpose(2, 0, 1, 3)


def unit_lower_inverse(strictly_lower):
    inverse = jnp.eye(SPAN, dtype=jnp.float32) - strictly_lower
    power = jnp.matmul(strictly_lower, strictly_lower, precision=LOCAL_PRECISION)
    covered = 2
    while covered < SPAN:
        if 2 * covered < SPAN:
            both = jnp.matmul(
                jnp.concatenate([inverse, power], axis=-2), power, precision=LOCAL_PRECISION
            )
            inverse = inverse + both[..., :SPAN, :]
            power = both[..., SPAN:, :]
        else:
            inverse = inverse + jnp.matmul(inverse, power, precision=LOCAL_PRECISION)
        covered = covered * 2
    return inverse


def span_pass(key_unit, value_f, beta_gate, decay_log, group_size):
    rowpos = lax.broadcasted_iota(jnp.int32, (SPAN, SPAN), 0)
    colpos = lax.broadcasted_iota(jnp.int32, (SPAN, SPAN), 1)
    cum_log = jnp.cumsum(decay_log, axis=2)
    spread = cum_log[..., :, None] - cum_log[..., None, :]
    strict = jnp.exp(jnp.where(colpos < rowpos, spread, -jnp.inf))
    key_inner = jnp.repeat(
        jnp.einsum("hmik,hmjk->hmij", key_unit, key_unit, precision=LOCAL_PRECISION),
        group_size,
        axis=0,
    )
    inverse = unit_lower_inverse(beta_gate[..., :, None] * strict * key_inner)
    wide_keys = jnp.repeat(key_unit, group_size, axis=0)
    targets = jnp.concatenate(
        [beta_gate[..., None] * value_f, (beta_gate * jnp.exp(cum_log))[..., None] * wide_keys],
        axis=-1,
    )
    solved = jnp.matmul(inverse, targets, precision=LOCAL_PRECISION)
    written = solved[..., :DV]
    weights = solved[..., DV:]
    faded_keys = wide_keys * jnp.exp(cum_log[..., -1:] - cum_log)[..., None]
    tail_decay = jnp.exp(cum_log[..., -1])
    maps = jnp.einsum("hmck,hmcj->hmkj", faded_keys, solved, precision=LOCAL_PRECISION)
    carry_mat = tail_decay[..., None, None] * jnp.eye(DK, dtype=jnp.float32) - maps[..., DV:]
    write_mat = maps[..., :DV]
    return (cum_log, spread, written, weights, carry_mat, write_mat)


def span_prep(query_unit, key_unit, group_size, pieces):
    cum_log, spread, written, weights, carry_mat, write_mat = pieces
    rowpos = lax.broadcasted_iota(jnp.int32, (SPAN, SPAN), 0)
    colpos = lax.broadcasted_iota(jnp.int32, (SPAN, SPAN), 1)
    within = jnp.exp(jnp.where(colpos <= rowpos, spread, -jnp.inf))
    scores = (
        jnp.repeat(
            jnp.einsum("hmik,hmjk->hmij", query_unit, key_unit, precision=LOCAL_PRECISION),
            group_size,
            axis=0,
        )
        * within
    )
    wide_query = jnp.repeat(query_unit, group_size, axis=0)
    mixed = jnp.einsum(
        "hmij,hmjv->hmiv",
        scores,
        jnp.concatenate([written, weights], axis=-1),
        precision=LOCAL_PRECISION,
    )
    inner = mixed[..., :DV]
    reach = wide_query * jnp.exp(cum_log)[..., None] - mixed[..., DV:]
    blocks = carry_mat.shape[1]
    fixed, scaled = ([inner[:, 0]], [reach[:, 0]])
    reach_both = jnp.concatenate([carry_mat, write_mat], axis=-1)
    total = reach_both[:, 0]
    for m in range(1, blocks):
        both = jnp.matmul(reach[:, m], total, precision=LOCAL_PRECISION)
        scaled.append(both[..., :DK])
        fixed.append(inner[:, m] + both[..., DK:])
        total = compose_joined(total, reach_both[:, m])
    return (jnp.stack(fixed, axis=1), jnp.stack(scaled, axis=1), total)


def span_out(fixed, scaled, state_in):
    return fixed + jnp.einsum("hmck,hkv->hmcv", scaled, state_in, precision=FULL_PRECISION)


def to_rows(core_out):
    head_count, blocks = (core_out.shape[0], core_out.shape[1])
    return core_out.transpose(1, 2, 0, 3).reshape(blocks * SPAN, head_count * DV)


def joined(carry, write):
    return jnp.concatenate([carry, write], axis=-1)


def split(both):
    return (both[..., :DK], both[..., DK:])


def exclusive_scan(carry, write, size, stride):
    count = size // stride
    if count == 1:
        return jnp.zeros_like(write)
    rounds = 0
    while 2 ** (rounds + 1) < count:
        rounds += 1
    shift = 1
    for _ in range(rounds):
        pairs = [(i, i + shift * stride) for i in range(size - shift * stride)]
        got = lax.ppermute(joined(carry, write), "ctx", pairs)
        carry, write = compose(split(got), (carry, write))
        shift *= 2
    near = [(i, i + stride) for i in range(size - stride)]
    far = 2**rounds + 1
    if far >= count:
        return lax.ppermute(write, "ctx", near)
    got_carry, got_write = split(lax.ppermute(joined(carry, write), "ctx", near))
    far_write = lax.ppermute(
        write, "ctx", [(i, i + far * stride) for i in range(size - far * stride)]
    )
    return jnp.matmul(got_carry, far_write, precision=FULL_PRECISION) + got_write


def chain_states(block_both):
    size = lax.axis_size("ctx")
    me = lax.axis_index("ctx")
    levels = 0
    while size % 2 ** (levels + 1) == 0 and block_both.shape[0] % 2 ** (levels + 1) == 0:
        levels += 1
    current = block_both
    saved = []
    for level in range(levels):
        stride = 2**level
        upper = (me // stride) % 2 == 1
        half = current.shape[0] // 2
        mine = jnp.where(upper, current[half:], current[:half])
        other = jnp.where(upper, current[:half], current[half:])
        got = lax.ppermute(other, "ctx", [(i, i ^ stride) for i in range(size)])
        earlier = jnp.where(upper, got, mine)
        later = jnp.where(upper, mine, got)
        saved.append((upper, earlier))
        current = compose_joined(earlier, later)
    state = exclusive_scan(*split(current), size, 2**levels)
    for level in reversed(range(levels)):
        stride = 2**level
        upper, earlier = saved[level]
        earlier_carry, earlier_write = split(earlier)
        after = jnp.matmul(earlier_carry, state, precision=FULL_PRECISION) + earlier_write
        mine = jnp.where(upper, after, state)
        other = jnp.where(upper, state, after)
        got = lax.ppermute(other, "ctx", [(i, i ^ stride) for i in range(size)])
        state = jnp.where(
            upper, jnp.concatenate([got, mine], axis=0), jnp.concatenate([mine, got], axis=0)
        )
    return state


def gated_norm(core_rows, output_gate, norm_gain):
    token_count = core_rows.shape[0]
    head_count = core_rows.shape[1] // DV
    core_f = core_rows.astype(jnp.float32).reshape(token_count, head_count, DV)
    inv_rms = lax.rsqrt(jnp.mean(core_f * core_f, axis=-1, keepdims=True) + 1e-06)
    gate_f = output_gate.astype(jnp.float32).reshape(token_count, head_count, DV)
    gated_rows = core_f * inv_rms * norm_gain.astype(jnp.float32) * jax.nn.silu(gate_f)
    return gated_rows.reshape(token_count, head_count * DV).astype(jnp.bfloat16)


def head_swap(rows):
    width = rows.shape[-1] // 2
    first = lax.axis_index("head") == 0
    own = jnp.where(first, rows[..., :width], rows[..., width:])
    sent = jnp.where(first, rows[..., width:], rows[..., :width])
    got = lax.ppermute(sent, "head", [(0, 1), (1, 0)])
    axis = rows.ndim - 2
    return jnp.where(
        first, jnp.concatenate([own, got], axis), jnp.concatenate([got, own], axis)
    )


def head_return(rows):
    tokens = rows.shape[0] // 2
    first = lax.axis_index("head") == 0
    own = jnp.where(first, rows[:tokens], rows[tokens:])
    sent = jnp.where(first, rows[tokens:], rows[:tokens])
    got = lax.ppermute(sent, "head", [(0, 1), (1, 0)])
    return jnp.where(first, jnp.concatenate([own, got], 1), jnp.concatenate([got, own], 1))


def head_inputs(pieces_in):
    parts = lax.axis_size("head")
    if parts == 2:
        query_rows, key_rows, value_rows, beta_logit, log_decay = pieces_in
        query_key = head_swap(jnp.stack([query_rows, key_rows]))
        gates = head_swap(jnp.stack([beta_logit, log_decay]))
        return [query_key[0], query_key[1], head_swap(value_rows), gates[0], gates[1]]
    tokens = pieces_in[0].shape[0]
    widths = [part.shape[1] // parts for part in pieces_in]
    packed = jnp.concatenate(
        [part.reshape(tokens, parts, width) for part, width in zip(pieces_in, widths)], axis=-1
    )
    packed = lax.all_to_all(packed, "head", split_axis=1, concat_axis=0, tiled=True)
    packed = packed.reshape(tokens * parts, sum(widths))
    ends = [sum(widths[: i + 1]) for i in range(len(widths))]
    return [packed[:, end - width : end] for end, width in zip(ends, widths)]


def head_outputs(rows):
    if lax.axis_size("head") == 2:
        return head_return(rows)
    return lax.all_to_all(rows, "head", split_axis=0, concat_axis=1, tiled=True)


def on_device(query_rows, key_rows, value_rows, output_gate, beta_logit, log_decay, norm_gain):
    q_head, k_head, v_head, b_head, d_head = head_inputs(
        [query_rows, key_rows, value_rows, beta_logit, log_decay]
    )
    key_unit, value_f, beta_gate, decay_log = arrange(k_head, v_head, b_head, d_head)
    group_size = value_f.shape[0] // key_unit.shape[0]
    pieces = span_pass(key_unit, value_f, beta_gate, decay_log, group_size)
    query_unit = arrange_query(q_head)
    fixed, scaled, total = span_prep(query_unit, key_unit, group_size, pieces)
    state_in = chain_states(total)
    core_out = span_out(fixed, scaled, state_in)
    core_rows = head_outputs(to_rows(core_out).astype(jnp.bfloat16))
    return gated_norm(core_rows, output_gate, norm_gain)


def solution(mesh):
    placed = (
        P(("ctx", "head"), None),
        P(("ctx", "head"), None),
        P(("ctx", "head"), None),
        P(("ctx", "head"), None),
        P(("ctx", "head"), None),
        P(("ctx", "head"), None),
        P(),
    )
    return jax.shard_map(
        on_device, mesh=mesh, in_specs=placed, out_specs=P(("ctx", "head"), None), check_vma=False
    )
```

```python
import jax
import jax.numpy as jnp
from jax import lax
from jax.sharding import PartitionSpec as P

DK = 128
DV = 128
SPAN = 128


FULL_PRECISION = lax.Precision.HIGH
LOCAL_PRECISION = lax.Precision.HIGH


def unit_rows(rows):
    return rows * lax.rsqrt(jnp.sum(rows * rows, axis=-1, keepdims=True) + 1e-06)


def compose(earlier, later):
    both = jnp.matmul(
        later[0], jnp.concatenate([earlier[0], earlier[1]], axis=-1), precision=FULL_PRECISION
    )
    return (both[..., : earlier[0].shape[-1]], both[..., earlier[0].shape[-1] :] + later[1])


def compose_joined(earlier, later):
    lane = lax.broadcasted_iota(jnp.int32, later.shape, later.ndim - 1)
    return jnp.matmul(
        later[..., : later.shape[-2]], earlier, precision=FULL_PRECISION
    ) + jnp.where(lane >= later.shape[-2], later, 0.0)


def by_head(rows, width):
    count = rows.shape[1] // width
    parts = [rows[:, g * width : (g + 1) * width] for g in range(count)]
    return jnp.stack(parts).reshape(count, rows.shape[0] // SPAN, SPAN, width)


def arrange(key_part, value_part, beta_part, decay_part):
    blocks = key_part.shape[0] // SPAN
    key_heads = key_part.shape[1] // DK
    value_heads = value_part.shape[1] // DV
    key_unit = unit_rows(
        key_part.astype(jnp.float32).reshape(blocks, SPAN, key_heads, DK)
    ).transpose(2, 0, 1, 3)
    value_f = (
        value_part.astype(jnp.float32).reshape(blocks, SPAN, value_heads, DV).transpose(2, 0, 1, 3)
    )
    beta_gate = (
        jax.nn.sigmoid(beta_part.astype(jnp.float32))
        .reshape(blocks, SPAN, value_heads)
        .transpose(2, 0, 1)
    )
    decay_log = decay_part.astype(jnp.float32).reshape(blocks, SPAN, value_heads).transpose(2, 0, 1)
    return (key_unit, value_f, beta_gate, decay_log)


def arrange_query(query_part):
    blocks = query_part.shape[0] // SPAN
    key_heads = query_part.shape[1] // DK
    query_f = by_head(query_part, DK).astype(jnp.float32)
    return unit_rows(query_f) * DK ** (-0.5)


def unit_lower_inverse(strictly_lower):
    inverse = jnp.eye(SPAN, dtype=jnp.float32) - strictly_lower
    power = jnp.matmul(strictly_lower, strictly_lower, precision=LOCAL_PRECISION)
    covered = 2
    while covered < SPAN:
        if 2 * covered < SPAN:
            both = jnp.matmul(
                jnp.concatenate([inverse, power], axis=-2), power, precision=LOCAL_PRECISION
            )
            inverse = inverse + both[..., :SPAN, :]
            power = both[..., SPAN:, :]
        else:
            inverse = inverse + jnp.matmul(inverse, power, precision=LOCAL_PRECISION)
        covered = covered * 2
    return inverse


def span_pass(key_unit, value_f, beta_gate, decay_log, group_size):
    rowpos = lax.broadcasted_iota(jnp.int32, (SPAN, SPAN), 0)
    colpos = lax.broadcasted_iota(jnp.int32, (SPAN, SPAN), 1)
    cum_log = jnp.cumsum(decay_log, axis=2)
    spread = cum_log[..., :, None] - cum_log[..., None, :]
    strict = jnp.exp(jnp.where(colpos < rowpos, spread, -jnp.inf))
    key_inner = jnp.repeat(
        jnp.einsum("hmik,hmjk->hmij", key_unit, key_unit, precision=LOCAL_PRECISION),
        group_size,
        axis=0,
    )
    inverse = unit_lower_inverse(beta_gate[..., :, None] * strict * key_inner)
    wide_keys = jnp.repeat(key_unit, group_size, axis=0)
    targets = jnp.concatenate(
        [beta_gate[..., None] * value_f, (beta_gate * jnp.exp(cum_log))[..., None] * wide_keys],
        axis=-1,
    )
    solved = jnp.matmul(inverse, targets, precision=LOCAL_PRECISION)
    written = solved[..., :DV]
    weights = solved[..., DV:]
    faded_keys = wide_keys * jnp.exp(cum_log[..., -1:] - cum_log)[..., None]
    tail_decay = jnp.exp(cum_log[..., -1])
    maps = jnp.einsum("hmck,hmcj->hmkj", faded_keys, solved, precision=LOCAL_PRECISION)
    carry_mat = tail_decay[..., None, None] * jnp.eye(DK, dtype=jnp.float32) - maps[..., DV:]
    write_mat = maps[..., :DV]
    return (cum_log, spread, written, weights, carry_mat, write_mat)


def span_prep(query_unit, key_unit, group_size, pieces):
    cum_log, spread, written, weights, carry_mat, write_mat = pieces
    rowpos = lax.broadcasted_iota(jnp.int32, (SPAN, SPAN), 0)
    colpos = lax.broadcasted_iota(jnp.int32, (SPAN, SPAN), 1)
    within = jnp.exp(jnp.where(colpos <= rowpos, spread, -jnp.inf))
    scores = (
        jnp.repeat(
            jnp.einsum("hmik,hmjk->hmij", query_unit, key_unit, precision=LOCAL_PRECISION),
            group_size,
            axis=0,
        )
        * within
    )
    wide_query = jnp.repeat(query_unit, group_size, axis=0)
    mixed = jnp.einsum(
        "hmij,hmjv->hmiv",
        scores,
        jnp.concatenate([written, weights], axis=-1),
        precision=LOCAL_PRECISION,
    )
    inner = mixed[..., :DV]
    reach = wide_query * jnp.exp(cum_log)[..., None] - mixed[..., DV:]
    blocks = carry_mat.shape[1]
    fixed, scaled = ([inner[:, 0]], [reach[:, 0]])
    reach_both = jnp.concatenate([carry_mat, write_mat], axis=-1)
    total = reach_both[:, 0]
    for m in range(1, blocks):
        both = jnp.matmul(reach[:, m], total, precision=LOCAL_PRECISION)
        scaled.append(both[..., :DK])
        fixed.append(inner[:, m] + both[..., DK:])
        total = compose_joined(total, reach_both[:, m])
    return (jnp.stack(fixed, axis=1), jnp.stack(scaled, axis=1), total)


def span_out(fixed, scaled, state_in):
    return fixed + jnp.einsum("hmck,hkv->hmcv", scaled, state_in, precision=FULL_PRECISION)


def to_rows(core_out):
    head_count, blocks = (core_out.shape[0], core_out.shape[1])
    return core_out.transpose(1, 2, 0, 3).reshape(blocks * SPAN, head_count * DV)


def joined(carry, write):
    return jnp.concatenate([carry, write], axis=-1)


def split(both):
    return (both[..., :DK], both[..., DK:])


def exclusive_scan(carry, write, size, stride):
    count = size // stride
    if count == 1:
        return jnp.zeros_like(write)
    rounds = 0
    while 2 ** (rounds + 1) < count:
        rounds += 1
    shift = 1
    for _ in range(rounds):
        pairs = [(i, i + shift * stride) for i in range(size - shift * stride)]
        got = lax.ppermute(joined(carry, write), "ctx", pairs)
        carry, write = compose(split(got), (carry, write))
        shift *= 2
    near = [(i, i + stride) for i in range(size - stride)]
    far = 2**rounds + 1
    if far >= count:
        return lax.ppermute(write, "ctx", near)
    got_carry, got_write = split(lax.ppermute(joined(carry, write), "ctx", near))
    far_write = lax.ppermute(
        write, "ctx", [(i, i + far * stride) for i in range(size - far * stride)]
    )
    return jnp.matmul(got_carry, far_write, precision=FULL_PRECISION) + got_write


def chain_states(block_both):
    size = lax.axis_size("ctx")
    me = lax.axis_index("ctx")
    levels = 0
    while size % 2 ** (levels + 1) == 0 and block_both.shape[0] % 2 ** (levels + 1) == 0:
        levels += 1
    current = block_both
    saved = []
    for level in range(levels):
        stride = 2**level
        upper = (me // stride) % 2 == 1
        half = current.shape[0] // 2
        mine = jnp.where(upper, current[half:], current[:half])
        other = jnp.where(upper, current[:half], current[half:])
        got = lax.ppermute(other, "ctx", [(i, i ^ stride) for i in range(size)])
        earlier = jnp.where(upper, got, mine)
        later = jnp.where(upper, mine, got)
        saved.append((upper, earlier))
        current = compose_joined(earlier, later)
    state = exclusive_scan(*split(current), size, 2**levels)
    for level in reversed(range(levels)):
        stride = 2**level
        upper, earlier = saved[level]
        earlier_carry, earlier_write = split(earlier)
        after = jnp.matmul(earlier_carry, state, precision=FULL_PRECISION) + earlier_write
        mine = jnp.where(upper, after, state)
        other = jnp.where(upper, state, after)
        got = lax.ppermute(other, "ctx", [(i, i ^ stride) for i in range(size)])
        state = jnp.where(
            upper, jnp.concatenate([got, mine], axis=0), jnp.concatenate([mine, got], axis=0)
        )
    return state


def gated_norm(core_rows, output_gate, norm_gain):
    token_count = core_rows.shape[0]
    head_count = core_rows.shape[1] // DV
    core_f = core_rows.astype(jnp.float32).reshape(token_count, head_count, DV)
    inv_rms = lax.rsqrt(jnp.mean(core_f * core_f, axis=-1, keepdims=True) + 1e-06)
    gate_f = output_gate.astype(jnp.float32).reshape(token_count, head_count, DV)
    gated_rows = core_f * inv_rms * norm_gain.astype(jnp.float32) * jax.nn.silu(gate_f)
    return gated_rows.reshape(token_count, head_count * DV).astype(jnp.bfloat16)


def head_swap(rows):
    width = rows.shape[-1] // 2
    first = lax.axis_index("head") == 0
    own = jnp.where(first, rows[..., :width], rows[..., width:])
    sent = jnp.where(first, rows[..., width:], rows[..., :width])
    got = lax.ppermute(sent, "head", [(0, 1), (1, 0)])
    axis = rows.ndim - 2
    return jnp.where(
        first, jnp.concatenate([own, got], axis), jnp.concatenate([got, own], axis)
    )


def head_return(rows):
    tokens = rows.shape[0] // 2
    first = lax.axis_index("head") == 0
    own = jnp.where(first, rows[:tokens], rows[tokens:])
    sent = jnp.where(first, rows[tokens:], rows[:tokens])
    got = lax.ppermute(sent, "head", [(0, 1), (1, 0)])
    return jnp.where(first, jnp.concatenate([own, got], 1), jnp.concatenate([got, own], 1))


def head_inputs(pieces_in):
    parts = lax.axis_size("head")
    if parts == 2:
        query_rows, key_rows, value_rows, beta_logit, log_decay = pieces_in
        query_key = head_swap(jnp.stack([query_rows, key_rows]))
        gates = head_swap(jnp.stack([beta_logit, log_decay]))
        return [query_key[0], query_key[1], head_swap(value_rows), gates[0], gates[1]]
    tokens = pieces_in[0].shape[0]
    widths = [part.shape[1] // parts for part in pieces_in]
    packed = jnp.concatenate(
        [part.reshape(tokens, parts, width) for part, width in zip(pieces_in, widths)], axis=-1
    )
    packed = lax.all_to_all(packed, "head", split_axis=1, concat_axis=0, tiled=True)
    packed = packed.reshape(tokens * parts, sum(widths))
    ends = [sum(widths[: i + 1]) for i in range(len(widths))]
    return [packed[:, end - width : end] for end, width in zip(ends, widths)]


def head_outputs(rows):
    if lax.axis_size("head") == 2:
        return head_return(rows)
    return lax.all_to_all(rows, "head", split_axis=0, concat_axis=1, tiled=True)


def on_device(query_rows, key_rows, value_rows, output_gate, beta_logit, log_decay, norm_gain):
    q_head, k_head, v_head, b_head, d_head = head_inputs(
        [query_rows, key_rows, value_rows, beta_logit, log_decay]
    )
    key_unit, value_f, beta_gate, decay_log = arrange(k_head, v_head, b_head, d_head)
    group_size = value_f.shape[0] // key_unit.shape[0]
    pieces = span_pass(key_unit, value_f, beta_gate, decay_log, group_size)
    query_unit = arrange_query(q_head)
    fixed, scaled, total = span_prep(query_unit, key_unit, group_size, pieces)
    state_in = chain_states(total)
    core_out = span_out(fixed, scaled, state_in)
    core_rows = head_outputs(to_rows(core_out).astype(jnp.bfloat16))
    return gated_norm(core_rows, output_gate, norm_gain)


def solution(mesh):
    placed = (
        P(("ctx", "head"), None),
        P(("ctx", "head"), None),
        P(("ctx", "head"), None),
        P(("ctx", "head"), None),
        P(("ctx", "head"), None),
        P(("ctx", "head"), None),
        P(),
    )
    return jax.shard_map(
        on_device, mesh=mesh, in_specs=placed, out_specs=P(("ctx", "head"), None), check_vma=False
    )
```

```python
import jax
import jax.numpy as jnp
from jax import lax
from jax.sharding import PartitionSpec as P

DK = 128
DV = 128
SPAN = 128


FULL_PRECISION = lax.Precision.HIGH
LOCAL_PRECISION = lax.Precision.HIGH


def unit_rows(rows):
    return rows * lax.rsqrt(jnp.sum(rows * rows, axis=-1, keepdims=True) + 1e-06)


def compose(earlier, later):
    both = jnp.matmul(
        later[0], jnp.concatenate([earlier[0], earlier[1]], axis=-1), precision=FULL_PRECISION
    )
    return (both[..., : earlier[0].shape[-1]], both[..., earlier[0].shape[-1] :] + later[1])


def compose_joined(earlier, later):
    lane = lax.broadcasted_iota(jnp.int32, later.shape, later.ndim - 1)
    return jnp.matmul(
        later[..., : later.shape[-2]], earlier, precision=FULL_PRECISION
    ) + jnp.where(lane >= later.shape[-2], later, 0.0)


def by_head(rows, width):
    count = rows.shape[1] // width
    parts = [rows[:, g * width : (g + 1) * width] for g in range(count)]
    return jnp.stack(parts).reshape(count, rows.shape[0] // SPAN, SPAN, width)


def arrange(key_part, value_part, beta_part, decay_part):
    blocks = key_part.shape[0] // SPAN
    key_heads = key_part.shape[1] // DK
    value_heads = value_part.shape[1] // DV
    key_unit = unit_rows(by_head(key_part, DK).astype(jnp.float32))
    value_f = by_head(value_part, DV).astype(jnp.float32)
    beta_gate = (
        jax.nn.sigmoid(beta_part.astype(jnp.float32))
        .reshape(blocks, SPAN, value_heads)
        .transpose(2, 0, 1)
    )
    decay_log = decay_part.astype(jnp.float32).reshape(blocks, SPAN, value_heads).transpose(2, 0, 1)
    return (key_unit, value_f, beta_gate, decay_log)


def arrange_query(query_part):
    blocks = query_part.shape[0] // SPAN
    key_heads = query_part.shape[1] // DK
    query_f = by_head(query_part, DK).astype(jnp.float32)
    return unit_rows(query_f) * DK ** (-0.5)


def unit_lower_inverse(strictly_lower):
    inverse = jnp.eye(SPAN, dtype=jnp.float32) - strictly_lower
    power = jnp.matmul(strictly_lower, strictly_lower, precision=LOCAL_PRECISION)
    covered = 2
    while covered < SPAN:
        if 2 * covered < SPAN:
            both = jnp.matmul(
                jnp.concatenate([inverse, power], axis=-2), power, precision=LOCAL_PRECISION
            )
            inverse = inverse + both[..., :SPAN, :]
            power = both[..., SPAN:, :]
        else:
            inverse = inverse + jnp.matmul(inverse, power, precision=LOCAL_PRECISION)
        covered = covered * 2
    return inverse


def span_pass(key_unit, value_f, beta_gate, decay_log, group_size):
    rowpos = lax.broadcasted_iota(jnp.int32, (SPAN, SPAN), 0)
    colpos = lax.broadcasted_iota(jnp.int32, (SPAN, SPAN), 1)
    cum_log = jnp.cumsum(decay_log, axis=2)
    spread = cum_log[..., :, None] - cum_log[..., None, :]
    strict = jnp.exp(jnp.where(colpos < rowpos, spread, -jnp.inf))
    key_inner = jnp.repeat(
        jnp.einsum("hmik,hmjk->hmij", key_unit, key_unit, precision=LOCAL_PRECISION),
        group_size,
        axis=0,
    )
    inverse = unit_lower_inverse(beta_gate[..., :, None] * strict * key_inner)
    wide_keys = jnp.repeat(key_unit, group_size, axis=0)
    targets = jnp.concatenate(
        [beta_gate[..., None] * value_f, (beta_gate * jnp.exp(cum_log))[..., None] * wide_keys],
        axis=-1,
    )
    solved = jnp.matmul(inverse, targets, precision=LOCAL_PRECISION)
    written = solved[..., :DV]
    weights = solved[..., DV:]
    faded_keys = wide_keys * jnp.exp(cum_log[..., -1:] - cum_log)[..., None]
    tail_decay = jnp.exp(cum_log[..., -1])
    maps = jnp.einsum("hmck,hmcj->hmkj", faded_keys, solved, precision=LOCAL_PRECISION)
    carry_mat = tail_decay[..., None, None] * jnp.eye(DK, dtype=jnp.float32) - maps[..., DV:]
    write_mat = maps[..., :DV]
    return (cum_log, spread, written, weights, carry_mat, write_mat)


def span_prep(query_unit, key_unit, group_size, pieces):
    cum_log, spread, written, weights, carry_mat, write_mat = pieces
    rowpos = lax.broadcasted_iota(jnp.int32, (SPAN, SPAN), 0)
    colpos = lax.broadcasted_iota(jnp.int32, (SPAN, SPAN), 1)
    within = jnp.exp(jnp.where(colpos <= rowpos, spread, -jnp.inf))
    scores = (
        jnp.repeat(
            jnp.einsum("hmik,hmjk->hmij", query_unit, key_unit, precision=LOCAL_PRECISION),
            group_size,
            axis=0,
        )
        * within
    )
    wide_query = jnp.repeat(query_unit, group_size, axis=0)
    mixed = jnp.einsum(
        "hmij,hmjv->hmiv",
        scores,
        jnp.concatenate([written, weights], axis=-1),
        precision=LOCAL_PRECISION,
    )
    inner = mixed[..., :DV]
    reach = wide_query * jnp.exp(cum_log)[..., None] - mixed[..., DV:]
    blocks = carry_mat.shape[1]
    fixed, scaled = ([inner[:, 0]], [reach[:, 0]])
    reach_both = jnp.concatenate([carry_mat, write_mat], axis=-1)
    total = reach_both[:, 0]
    for m in range(1, blocks):
        both = jnp.matmul(reach[:, m], total, precision=LOCAL_PRECISION)
        scaled.append(both[..., :DK])
        fixed.append(inner[:, m] + both[..., DK:])
        total = compose_joined(total, reach_both[:, m])
    return (jnp.stack(fixed, axis=1), jnp.stack(scaled, axis=1), total)


def span_out(fixed, scaled, state_in):
    return fixed + jnp.einsum("hmck,hkv->hmcv", scaled, state_in, precision=FULL_PRECISION)


def to_rows(core_out):
    head_count, blocks = (core_out.shape[0], core_out.shape[1])
    return core_out.transpose(1, 2, 0, 3).reshape(blocks * SPAN, head_count * DV)


def joined(carry, write):
    return jnp.concatenate([carry, write], axis=-1)


def split(both):
    return (both[..., :DK], both[..., DK:])


def exclusive_scan(carry, write, size, stride):
    count = size // stride
    if count == 1:
        return jnp.zeros_like(write)
    rounds = 0
    while 2 ** (rounds + 1) < count:
        rounds += 1
    shift = 1
    for _ in range(rounds):
        pairs = [(i, i + shift * stride) for i in range(size - shift * stride)]
        got = lax.ppermute(joined(carry, write), "ctx", pairs)
        carry, write = compose(split(got), (carry, write))
        shift *= 2
    near = [(i, i + stride) for i in range(size - stride)]
    far = 2**rounds + 1
    if far >= count:
        return lax.ppermute(write, "ctx", near)
    got_carry, got_write = split(lax.ppermute(joined(carry, write), "ctx", near))
    far_write = lax.ppermute(
        write, "ctx", [(i, i + far * stride) for i in range(size - far * stride)]
    )
    return jnp.matmul(got_carry, far_write, precision=FULL_PRECISION) + got_write


def chain_states(block_both):
    size = lax.axis_size("ctx")
    me = lax.axis_index("ctx")
    levels = 0
    while size % 2 ** (levels + 1) == 0 and block_both.shape[0] % 2 ** (levels + 1) == 0:
        levels += 1
    current = block_both
    saved = []
    for level in range(levels):
        stride = 2**level
        upper = (me // stride) % 2 == 1
        half = current.shape[0] // 2
        mine = jnp.where(upper, current[half:], current[:half])
        other = jnp.where(upper, current[:half], current[half:])
        got = lax.ppermute(other, "ctx", [(i, i ^ stride) for i in range(size)])
        earlier = jnp.where(upper, got, mine)
        later = jnp.where(upper, mine, got)
        saved.append((upper, earlier))
        current = compose_joined(earlier, later)
    state = exclusive_scan(*split(current), size, 2**levels)
    for level in reversed(range(levels)):
        stride = 2**level
        upper, earlier = saved[level]
        earlier_carry, earlier_write = split(earlier)
        after = jnp.matmul(earlier_carry, state, precision=FULL_PRECISION) + earlier_write
        mine = jnp.where(upper, after, state)
        other = jnp.where(upper, state, after)
        got = lax.ppermute(other, "ctx", [(i, i ^ stride) for i in range(size)])
        state = jnp.where(
            upper, jnp.concatenate([got, mine], axis=0), jnp.concatenate([mine, got], axis=0)
        )
    return state


def gated_norm(core_rows, output_gate, norm_gain):
    token_count = core_rows.shape[0]
    head_count = core_rows.shape[1] // DV
    core_f = core_rows.astype(jnp.float32).reshape(token_count, head_count, DV)
    inv_rms = lax.rsqrt(jnp.mean(core_f * core_f, axis=-1, keepdims=True) + 1e-06)
    gate_f = output_gate.astype(jnp.float32).reshape(token_count, head_count, DV)
    gated_rows = core_f * inv_rms * norm_gain.astype(jnp.float32) * jax.nn.silu(gate_f)
    return gated_rows.reshape(token_count, head_count * DV).astype(jnp.bfloat16)


def head_swap(rows):
    width = rows.shape[-1] // 2
    first = lax.axis_index("head") == 0
    own = jnp.where(first, rows[..., :width], rows[..., width:])
    sent = jnp.where(first, rows[..., width:], rows[..., :width])
    got = lax.ppermute(sent, "head", [(0, 1), (1, 0)])
    axis = rows.ndim - 2
    return jnp.where(
        first, jnp.concatenate([own, got], axis), jnp.concatenate([got, own], axis)
    )


def head_return(rows):
    tokens = rows.shape[0] // 2
    first = lax.axis_index("head") == 0
    own = jnp.where(first, rows[:tokens], rows[tokens:])
    sent = jnp.where(first, rows[tokens:], rows[:tokens])
    got = lax.ppermute(sent, "head", [(0, 1), (1, 0)])
    return jnp.where(first, jnp.concatenate([own, got], 1), jnp.concatenate([got, own], 1))


def head_inputs(pieces_in):
    parts = lax.axis_size("head")
    if parts == 2:
        query_rows, key_rows, value_rows, beta_logit, log_decay = pieces_in
        query_key = head_swap(jnp.stack([query_rows, key_rows]))
        gates = head_swap(jnp.stack([beta_logit, log_decay]))
        return [query_key[0], query_key[1], head_swap(value_rows), gates[0], gates[1]]
    tokens = pieces_in[0].shape[0]
    widths = [part.shape[1] // parts for part in pieces_in]
    packed = jnp.concatenate(
        [part.reshape(tokens, parts, width) for part, width in zip(pieces_in, widths)], axis=-1
    )
    packed = lax.all_to_all(packed, "head", split_axis=1, concat_axis=0, tiled=True)
    packed = packed.reshape(tokens * parts, sum(widths))
    ends = [sum(widths[: i + 1]) for i in range(len(widths))]
    return [packed[:, end - width : end] for end, width in zip(ends, widths)]


def head_outputs(rows):
    if lax.axis_size("head") == 2:
        return head_return(rows)
    return lax.all_to_all(rows, "head", split_axis=0, concat_axis=1, tiled=True)


def on_device(query_rows, key_rows, value_rows, output_gate, beta_logit, log_decay, norm_gain):
    q_head, k_head, v_head, b_head, d_head = head_inputs(
        [query_rows, key_rows, value_rows, beta_logit, log_decay]
    )
    key_unit, value_f, beta_gate, decay_log = arrange(k_head, v_head, b_head, d_head)
    group_size = value_f.shape[0] // key_unit.shape[0]
    pieces = span_pass(key_unit, value_f, beta_gate, decay_log, group_size)
    query_unit = arrange_query(q_head)
    fixed, scaled, total = span_prep(query_unit, key_unit, group_size, pieces)
    state_in = chain_states(total)
    core_out = span_out(fixed, scaled, state_in)
    core_rows = head_outputs(to_rows(core_out).astype(jnp.bfloat16))
    return gated_norm(core_rows, output_gate, norm_gain)


def solution(mesh):
    placed = (
        P(("ctx", "head"), None),
        P(("ctx", "head"), None),
        P(("ctx", "head"), None),
        P(("ctx", "head"), None),
        P(("ctx", "head"), None),
        P(("ctx", "head"), None),
        P(),
    )
    return jax.shard_map(
        on_device, mesh=mesh, in_specs=placed, out_specs=P(("ctx", "head"), None), check_vma=False
    )
```

```python
import jax
import jax.numpy as jnp
from jax import lax
from jax.sharding import PartitionSpec as P

DK = 128
DV = 128
SPAN = 128


FULL_PRECISION = lax.Precision.HIGH
LOCAL_PRECISION = lax.Precision.HIGH


def unit_rows(rows):
    return rows * lax.rsqrt(jnp.sum(rows * rows, axis=-1, keepdims=True) + 1e-06)


def compose(earlier, later):
    both = jnp.matmul(
        later[0], jnp.concatenate([earlier[0], earlier[1]], axis=-1), precision=FULL_PRECISION
    )
    return (both[..., : earlier[0].shape[-1]], both[..., earlier[0].shape[-1] :] + later[1])


def compose_joined(earlier, later):
    lane = lax.broadcasted_iota(jnp.int32, later.shape, later.ndim - 1)
    return jnp.matmul(
        later[..., : later.shape[-2]], earlier, precision=FULL_PRECISION
    ) + jnp.where(lane >= later.shape[-2], later, 0.0)


def by_head(rows, width):
    count = rows.shape[1] // width
    parts = [rows[:, g * width : (g + 1) * width] for g in range(count)]
    return jnp.stack(parts).reshape(count, rows.shape[0] // SPAN, SPAN, width)


def arrange(key_part, value_part, beta_part, decay_part):
    blocks = key_part.shape[0] // SPAN
    key_heads = key_part.shape[1] // DK
    value_heads = value_part.shape[1] // DV
    key_unit = unit_rows(by_head(key_part, DK).astype(jnp.float32))
    value_f = (
        value_part.astype(jnp.float32).reshape(blocks, SPAN, value_heads, DV).transpose(2, 0, 1, 3)
    )
    beta_gate = (
        jax.nn.sigmoid(beta_part.astype(jnp.float32))
        .reshape(blocks, SPAN, value_heads)
        .transpose(2, 0, 1)
    )
    decay_log = decay_part.astype(jnp.float32).reshape(blocks, SPAN, value_heads).transpose(2, 0, 1)
    return (key_unit, value_f, beta_gate, decay_log)


def arrange_query(query_part):
    blocks = query_part.shape[0] // SPAN
    key_heads = query_part.shape[1] // DK
    query_f = by_head(query_part, DK).astype(jnp.float32)
    return unit_rows(query_f) * DK ** (-0.5)


def unit_lower_inverse(strictly_lower):
    inverse = jnp.eye(SPAN, dtype=jnp.float32) - strictly_lower
    power = jnp.matmul(strictly_lower, strictly_lower, precision=LOCAL_PRECISION)
    covered = 2
    while covered < SPAN:
        if 2 * covered < SPAN:
            both = jnp.matmul(
                jnp.concatenate([inverse, power], axis=-2), power, precision=LOCAL_PRECISION
            )
            inverse = inverse + both[..., :SPAN, :]
            power = both[..., SPAN:, :]
        else:
            inverse = inverse + jnp.matmul(inverse, power, precision=LOCAL_PRECISION)
        covered = covered * 2
    return inverse


def span_pass(key_unit, value_f, beta_gate, decay_log, group_size):
    rowpos = lax.broadcasted_iota(jnp.int32, (SPAN, SPAN), 0)
    colpos = lax.broadcasted_iota(jnp.int32, (SPAN, SPAN), 1)
    cum_log = jnp.cumsum(decay_log, axis=2)
    spread = cum_log[..., :, None] - cum_log[..., None, :]
    strict = jnp.exp(jnp.where(colpos < rowpos, spread, -jnp.inf))
    key_inner = jnp.repeat(
        jnp.einsum("hmik,hmjk->hmij", key_unit, key_unit, precision=LOCAL_PRECISION),
        group_size,
        axis=0,
    )
    inverse = unit_lower_inverse(beta_gate[..., :, None] * strict * key_inner)
    wide_keys = jnp.repeat(key_unit, group_size, axis=0)
    targets = jnp.concatenate(
        [beta_gate[..., None] * value_f, (beta_gate * jnp.exp(cum_log))[..., None] * wide_keys],
        axis=-1,
    )
    solved = jnp.matmul(inverse, targets, precision=LOCAL_PRECISION)
    written = solved[..., :DV]
    weights = solved[..., DV:]
    faded_keys = wide_keys * jnp.exp(cum_log[..., -1:] - cum_log)[..., None]
    tail_decay = jnp.exp(cum_log[..., -1])
    maps = jnp.einsum("hmck,hmcj->hmkj", faded_keys, solved, precision=LOCAL_PRECISION)
    carry_mat = tail_decay[..., None, None] * jnp.eye(DK, dtype=jnp.float32) - maps[..., DV:]
    write_mat = maps[..., :DV]
    return (cum_log, spread, written, weights, carry_mat, write_mat)


def span_prep(query_unit, key_unit, group_size, pieces):
    cum_log, spread, written, weights, carry_mat, write_mat = pieces
    rowpos = lax.broadcasted_iota(jnp.int32, (SPAN, SPAN), 0)
    colpos = lax.broadcasted_iota(jnp.int32, (SPAN, SPAN), 1)
    within = jnp.exp(jnp.where(colpos <= rowpos, spread, -jnp.inf))
    scores = (
        jnp.repeat(
            jnp.einsum("hmik,hmjk->hmij", query_unit, key_unit, precision=LOCAL_PRECISION),
            group_size,
            axis=0,
        )
        * within
    )
    wide_query = jnp.repeat(query_unit, group_size, axis=0)
    mixed = jnp.einsum(
        "hmij,hmjv->hmiv",
        scores,
        jnp.concatenate([written, weights], axis=-1),
        precision=LOCAL_PRECISION,
    )
    inner = mixed[..., :DV]
    reach = wide_query * jnp.exp(cum_log)[..., None] - mixed[..., DV:]
    blocks = carry_mat.shape[1]
    fixed, scaled = ([inner[:, 0]], [reach[:, 0]])
    reach_both = jnp.concatenate([carry_mat, write_mat], axis=-1)
    total = reach_both[:, 0]
    for m in range(1, blocks):
        both = jnp.matmul(reach[:, m], total, precision=LOCAL_PRECISION)
        scaled.append(both[..., :DK])
        fixed.append(inner[:, m] + both[..., DK:])
        total = compose_joined(total, reach_both[:, m])
    return (jnp.stack(fixed, axis=1), jnp.stack(scaled, axis=1), total)


def span_out(fixed, scaled, state_in):
    return fixed + jnp.einsum("hmck,hkv->hmcv", scaled, state_in, precision=FULL_PRECISION)


def to_rows(core_out):
    head_count, blocks = (core_out.shape[0], core_out.shape[1])
    return core_out.transpose(1, 2, 0, 3).reshape(blocks * SPAN, head_count * DV)


def joined(carry, write):
    return jnp.concatenate([carry, write], axis=-1)


def split(both):
    return (both[..., :DK], both[..., DK:])


def exclusive_scan(carry, write, size, stride):
    count = size // stride
    if count == 1:
        return jnp.zeros_like(write)
    rounds = 0
    while 2 ** (rounds + 1) < count:
        rounds += 1
    shift = 1
    for _ in range(rounds):
        pairs = [(i, i + shift * stride) for i in range(size - shift * stride)]
        got = lax.ppermute(joined(carry, write), "ctx", pairs)
        carry, write = compose(split(got), (carry, write))
        shift *= 2
    near = [(i, i + stride) for i in range(size - stride)]
    far = 2**rounds + 1
    if far >= count:
        return lax.ppermute(write, "ctx", near)
    got_carry, got_write = split(lax.ppermute(joined(carry, write), "ctx", near))
    far_write = lax.ppermute(
        write, "ctx", [(i, i + far * stride) for i in range(size - far * stride)]
    )
    return jnp.matmul(got_carry, far_write, precision=FULL_PRECISION) + got_write


def chain_states(block_both):
    size = lax.axis_size("ctx")
    me = lax.axis_index("ctx")
    levels = 0
    while size % 2 ** (levels + 1) == 0 and block_both.shape[0] % 2 ** (levels + 1) == 0:
        levels += 1
    current = block_both
    saved = []
    for level in range(levels):
        stride = 2**level
        upper = (me // stride) % 2 == 1
        half = current.shape[0] // 2
        mine = jnp.where(upper, current[half:], current[:half])
        other = jnp.where(upper, current[:half], current[half:])
        got = lax.ppermute(other, "ctx", [(i, i ^ stride) for i in range(size)])
        earlier = jnp.where(upper, got, mine)
        later = jnp.where(upper, mine, got)
        saved.append((upper, earlier))
        current = compose_joined(earlier, later)
    state = exclusive_scan(*split(current), size, 2**levels)
    for level in reversed(range(levels)):
        stride = 2**level
        upper, earlier = saved[level]
        earlier_carry, earlier_write = split(earlier)
        after = jnp.matmul(earlier_carry, state, precision=FULL_PRECISION) + earlier_write
        mine = jnp.where(upper, after, state)
        other = jnp.where(upper, state, after)
        got = lax.ppermute(other, "ctx", [(i, i ^ stride) for i in range(size)])
        state = jnp.where(
            upper, jnp.concatenate([got, mine], axis=0), jnp.concatenate([mine, got], axis=0)
        )
    return state


def gated_norm(core_rows, output_gate, norm_gain):
    token_count = core_rows.shape[0]
    head_count = core_rows.shape[1] // DV
    core_f = core_rows.astype(jnp.float32).reshape(token_count, head_count, DV)
    inv_rms = lax.rsqrt(jnp.mean(core_f * core_f, axis=-1, keepdims=True) + 1e-06)
    gate_f = output_gate.astype(jnp.float32).reshape(token_count, head_count, DV)
    gated_rows = core_f * inv_rms * norm_gain.astype(jnp.float32) * jax.nn.silu(gate_f)
    return gated_rows.reshape(token_count, head_count * DV).astype(jnp.bfloat16)


def head_swap(rows):
    width = rows.shape[-1] // 2
    first = lax.axis_index("head") == 0
    own = jnp.where(first, rows[..., :width], rows[..., width:])
    sent = jnp.where(first, rows[..., width:], rows[..., :width])
    got = lax.ppermute(sent, "head", [(0, 1), (1, 0)])
    axis = rows.ndim - 2
    return jnp.where(
        first, jnp.concatenate([own, got], axis), jnp.concatenate([got, own], axis)
    )


def head_return(rows):
    tokens = rows.shape[0] // 2
    first = lax.axis_index("head") == 0
    own = jnp.where(first, rows[:tokens], rows[tokens:])
    sent = jnp.where(first, rows[tokens:], rows[:tokens])
    got = lax.ppermute(sent, "head", [(0, 1), (1, 0)])
    return jnp.where(first, jnp.concatenate([own, got], 1), jnp.concatenate([got, own], 1))


def head_inputs(pieces_in):
    parts = lax.axis_size("head")
    if parts == 2:
        query_rows, key_rows, value_rows, beta_logit, log_decay = pieces_in
        query_key = head_swap(jnp.stack([query_rows, key_rows]))
        gates = head_swap(jnp.stack([beta_logit, log_decay]))
        return [query_key[0], query_key[1], head_swap(value_rows), gates[0], gates[1]]
    tokens = pieces_in[0].shape[0]
    widths = [part.shape[1] // parts for part in pieces_in]
    packed = jnp.concatenate(
        [part.reshape(tokens, parts, width) for part, width in zip(pieces_in, widths)], axis=-1
    )
    packed = lax.all_to_all(packed, "head", split_axis=1, concat_axis=0, tiled=True)
    packed = packed.reshape(tokens * parts, sum(widths))
    ends = [sum(widths[: i + 1]) for i in range(len(widths))]
    return [packed[:, end - width : end] for end, width in zip(ends, widths)]


def head_outputs(rows):
    if lax.axis_size("head") == 2:
        return head_return(rows)
    return lax.all_to_all(rows, "head", split_axis=0, concat_axis=1, tiled=True)


def on_device(query_rows, key_rows, value_rows, output_gate, beta_logit, log_decay, norm_gain):
    q_head, k_head, v_head, b_head, d_head = head_inputs(
        [query_rows, key_rows, value_rows, beta_logit, log_decay]
    )
    key_unit, value_f, beta_gate, decay_log = arrange(k_head, v_head, b_head, d_head)
    group_size = value_f.shape[0] // key_unit.shape[0]
    pieces = span_pass(key_unit, value_f, beta_gate, decay_log, group_size)
    query_unit = arrange_query(q_head)
    fixed, scaled, total = span_prep(query_unit, key_unit, group_size, pieces)
    state_in = chain_states(total)
    core_out = span_out(fixed, scaled, state_in)
    core_rows = head_outputs(to_rows(core_out).astype(jnp.bfloat16))
    return gated_norm(core_rows, output_gate, norm_gain)


def solution(mesh):
    placed = (
        P(("ctx", "head"), None),
        P(("ctx", "head"), None),
        P(("ctx", "head"), None),
        P(("ctx", "head"), None),
        P(("ctx", "head"), None),
        P(("ctx", "head"), None),
        P(),
    )
    return jax.shard_map(
        on_device, mesh=mesh, in_specs=placed, out_specs=P(("ctx", "head"), None), check_vma=False
    )
```

```python
import jax
import jax.numpy as jnp
from jax import lax
from jax.sharding import PartitionSpec as P

DK = 128
DV = 128
SPAN = 128


FULL_PRECISION = lax.Precision.HIGH
LOCAL_PRECISION = lax.Precision.HIGH


def unit_rows(rows):
    return rows * lax.rsqrt(jnp.sum(rows * rows, axis=-1, keepdims=True) + 1e-06)


def compose(earlier, later):
    both = jnp.matmul(
        later[0], jnp.concatenate([earlier[0], earlier[1]], axis=-1), precision=FULL_PRECISION
    )
    return (both[..., : earlier[0].shape[-1]], both[..., earlier[0].shape[-1] :] + later[1])


def compose_joined(earlier, later):
    lane = lax.broadcasted_iota(jnp.int32, later.shape, later.ndim - 1)
    return jnp.matmul(
        later[..., : later.shape[-2]], earlier, precision=FULL_PRECISION
    ) + jnp.where(lane >= later.shape[-2], later, 0.0)


def by_head(rows, width):
    count = rows.shape[1] // width
    parts = [rows[:, g * width : (g + 1) * width] for g in range(count)]
    return jnp.stack(parts).reshape(count, rows.shape[0] // SPAN, SPAN, width)


def arrange(key_part, value_part, beta_part, decay_part):
    blocks = key_part.shape[0] // SPAN
    key_heads = key_part.shape[1] // DK
    value_heads = value_part.shape[1] // DV
    key_unit = unit_rows(
        key_part.astype(jnp.float32).reshape(blocks, SPAN, key_heads, DK)
    ).transpose(2, 0, 1, 3)
    value_f = (
        value_part.astype(jnp.float32).reshape(blocks, SPAN, value_heads, DV).transpose(2, 0, 1, 3)
    )
    beta_gate = (
        jax.nn.sigmoid(beta_part.astype(jnp.float32))
        .reshape(blocks, SPAN, value_heads)
        .transpose(2, 0, 1)
    )
    decay_log = decay_part.astype(jnp.float32).reshape(blocks, SPAN, value_heads).transpose(2, 0, 1)
    return (key_unit, value_f, beta_gate, decay_log)


def arrange_query(query_part):
    blocks = query_part.shape[0] // SPAN
    key_heads = query_part.shape[1] // DK
    query_f = by_head(query_part, DK).astype(jnp.float32)
    return unit_rows(query_f) * DK ** (-0.5)


def unit_lower_inverse(strictly_lower):
    inverse = jnp.eye(SPAN, dtype=jnp.float32) - strictly_lower
    power = jnp.matmul(strictly_lower, strictly_lower, precision=LOCAL_PRECISION)
    covered = 2
    while covered < SPAN:
        if 2 * covered < SPAN:
            both = jnp.matmul(
                jnp.concatenate([inverse, power], axis=-2), power, precision=LOCAL_PRECISION
            )
            inverse = inverse + both[..., :SPAN, :]
            power = both[..., SPAN:, :]
        else:
            inverse = inverse + jnp.matmul(inverse, power, precision=LOCAL_PRECISION)
        covered = covered * 2
    return inverse


def span_pass(key_unit, value_f, beta_gate, decay_log, group_size):
    rowpos = lax.broadcasted_iota(jnp.int32, (SPAN, SPAN), 0)
    colpos = lax.broadcasted_iota(jnp.int32, (SPAN, SPAN), 1)
    cum_log = jnp.cumsum(decay_log, axis=2)
    spread = cum_log[..., :, None] - cum_log[..., None, :]
    strict = jnp.exp(jnp.where(colpos < rowpos, spread, -jnp.inf))
    key_inner = jnp.repeat(
        jnp.einsum("hmik,hmjk->hmij", key_unit, key_unit, precision=LOCAL_PRECISION),
        group_size,
        axis=0,
    )
    inverse = unit_lower_inverse(beta_gate[..., :, None] * strict * key_inner)
    wide_keys = jnp.repeat(key_unit, group_size, axis=0)
    targets = jnp.concatenate(
        [beta_gate[..., None] * value_f, (beta_gate * jnp.exp(cum_log))[..., None] * wide_keys],
        axis=-1,
    )
    solved = jnp.matmul(inverse, targets, precision=LOCAL_PRECISION)
    written = solved[..., :DV]
    weights = solved[..., DV:]
    faded_keys = wide_keys * jnp.exp(cum_log[..., -1:] - cum_log)[..., None]
    tail_decay = jnp.exp(cum_log[..., -1])
    maps = jnp.einsum("hmck,hmcj->hmkj", faded_keys, solved, precision=LOCAL_PRECISION)
    carry_mat = tail_decay[..., None, None] * jnp.eye(DK, dtype=jnp.float32) - maps[..., DV:]
    write_mat = maps[..., :DV]
    return (cum_log, spread, written, weights, carry_mat, write_mat)


def span_prep(query_unit, key_unit, group_size, pieces):
    cum_log, spread, written, weights, carry_mat, write_mat = pieces
    rowpos = lax.broadcasted_iota(jnp.int32, (SPAN, SPAN), 0)
    colpos = lax.broadcasted_iota(jnp.int32, (SPAN, SPAN), 1)
    within = jnp.exp(jnp.where(colpos <= rowpos, spread, -jnp.inf))
    scores = (
        jnp.repeat(
            jnp.einsum("hmik,hmjk->hmij", query_unit, key_unit, precision=LOCAL_PRECISION),
            group_size,
            axis=0,
        )
        * within
    )
    wide_query = jnp.repeat(query_unit, group_size, axis=0)
    mixed = jnp.einsum(
        "hmij,hmjv->hmiv",
        scores,
        jnp.concatenate([written, weights], axis=-1),
        precision=LOCAL_PRECISION,
    )
    inner = mixed[..., :DV]
    reach = wide_query * jnp.exp(cum_log)[..., None] - mixed[..., DV:]
    blocks = carry_mat.shape[1]
    fixed, scaled = ([inner[:, 0]], [reach[:, 0]])
    reach_both = jnp.concatenate([carry_mat, write_mat], axis=-1)
    total = reach_both[:, 0]
    for m in range(1, blocks):
        both = jnp.matmul(reach[:, m], total, precision=LOCAL_PRECISION)
        scaled.append(both[..., :DK])
        fixed.append(inner[:, m] + both[..., DK:])
        total = compose_joined(total, reach_both[:, m])
    return (jnp.stack(fixed, axis=1), jnp.stack(scaled, axis=1), total)


def span_out(fixed, scaled, state_in):
    return fixed + jnp.einsum("hmck,hkv->hmcv", scaled, state_in, precision=FULL_PRECISION)


def to_rows(core_out):
    head_count, blocks = (core_out.shape[0], core_out.shape[1])
    return core_out.transpose(1, 2, 0, 3).reshape(blocks * SPAN, head_count * DV)


def joined(carry, write):
    return jnp.concatenate([carry, write], axis=-1)


def split(both):
    return (both[..., :DK], both[..., DK:])


def exclusive_scan(carry, write, size, stride):
    count = size // stride
    if count == 1:
        return jnp.zeros_like(write)
    rounds = 0
    while 2 ** (rounds + 1) < count:
        rounds += 1
    shift = 1
    for _ in range(rounds):
        pairs = [(i, i + shift * stride) for i in range(size - shift * stride)]
        got = lax.ppermute(joined(carry, write), "ctx", pairs)
        carry, write = compose(split(got), (carry, write))
        shift *= 2
    near = [(i, i + stride) for i in range(size - stride)]
    far = 2**rounds + 1
    if far >= count:
        return lax.ppermute(write, "ctx", near)
    got_carry, got_write = split(lax.ppermute(joined(carry, write), "ctx", near))
    far_write = lax.ppermute(
        write, "ctx", [(i, i + far * stride) for i in range(size - far * stride)]
    )
    return jnp.matmul(got_carry, far_write, precision=FULL_PRECISION) + got_write


def chain_states(block_both):
    size = lax.axis_size("ctx")
    me = lax.axis_index("ctx")
    levels = 0
    while size % 2 ** (levels + 1) == 0 and block_both.shape[0] % 2 ** (levels + 1) == 0:
        levels += 1
    current = block_both
    saved = []
    for level in range(levels):
        stride = 2**level
        upper = (me // stride) % 2 == 1
        half = current.shape[0] // 2
        mine = jnp.where(upper, current[half:], current[:half])
        other = jnp.where(upper, current[:half], current[half:])
        got = lax.ppermute(other, "ctx", [(i, i ^ stride) for i in range(size)])
        earlier = jnp.where(upper, got, mine)
        later = jnp.where(upper, mine, got)
        saved.append((upper, earlier))
        current = compose_joined(earlier, later)
    state = exclusive_scan(*split(current), size, 2**levels)
    for level in reversed(range(levels)):
        stride = 2**level
        upper, earlier = saved[level]
        earlier_carry, earlier_write = split(earlier)
        after = jnp.matmul(earlier_carry, state, precision=FULL_PRECISION) + earlier_write
        mine = jnp.where(upper, after, state)
        other = jnp.where(upper, state, after)
        got = lax.ppermute(other, "ctx", [(i, i ^ stride) for i in range(size)])
        state = jnp.where(
            upper, jnp.concatenate([got, mine], axis=0), jnp.concatenate([mine, got], axis=0)
        )
    return state


def gated_norm(core_rows, output_gate, norm_gain):
    token_count = core_rows.shape[0]
    head_count = core_rows.shape[1] // DV
    core_f = core_rows.astype(jnp.float32).reshape(token_count, head_count, DV)
    inv_rms = lax.rsqrt(jnp.mean(core_f * core_f, axis=-1, keepdims=True) + 1e-06)
    gate_f = output_gate.astype(jnp.float32).reshape(token_count, head_count, DV)
    gated_rows = core_f * inv_rms * norm_gain.astype(jnp.float32) * jax.nn.silu(gate_f)
    return gated_rows.reshape(token_count, head_count * DV).astype(jnp.bfloat16)


def head_swap(rows):
    width = rows.shape[-1] // 2
    first = lax.axis_index("head") == 0
    own = jnp.where(first, rows[..., :width], rows[..., width:])
    sent = jnp.where(first, rows[..., width:], rows[..., :width])
    got = lax.ppermute(sent, "head", [(0, 1), (1, 0)])
    axis = rows.ndim - 2
    return jnp.where(
        first, jnp.concatenate([own, got], axis), jnp.concatenate([got, own], axis)
    )


def head_return(rows):
    tokens = rows.shape[0] // 2
    first = lax.axis_index("head") == 0
    half = lax.axis_index("head")
    own = lax.dynamic_slice_in_dim(rows, half * tokens, tokens, 0)
    sent = lax.dynamic_slice_in_dim(rows, (1 - half) * tokens, tokens, 0)
    got = lax.ppermute(sent, "head", [(0, 1), (1, 0)])
    return jnp.where(first, jnp.concatenate([own, got], 1), jnp.concatenate([got, own], 1))


def head_inputs(pieces_in):
    parts = lax.axis_size("head")
    if parts == 2:
        query_rows, key_rows, value_rows, beta_logit, log_decay = pieces_in
        query_key = head_swap(jnp.stack([query_rows, key_rows]))
        gates = head_swap(jnp.stack([beta_logit, log_decay]))
        return [query_key[0], query_key[1], head_swap(value_rows), gates[0], gates[1]]
    tokens = pieces_in[0].shape[0]
    widths = [part.shape[1] // parts for part in pieces_in]
    packed = jnp.concatenate(
        [part.reshape(tokens, parts, width) for part, width in zip(pieces_in, widths)], axis=-1
    )
    packed = lax.all_to_all(packed, "head", split_axis=1, concat_axis=0, tiled=True)
    packed = packed.reshape(tokens * parts, sum(widths))
    ends = [sum(widths[: i + 1]) for i in range(len(widths))]
    return [packed[:, end - width : end] for end, width in zip(ends, widths)]


def head_outputs(rows):
    if lax.axis_size("head") == 2:
        return head_return(rows)
    return lax.all_to_all(rows, "head", split_axis=0, concat_axis=1, tiled=True)


def on_device(query_rows, key_rows, value_rows, output_gate, beta_logit, log_decay, norm_gain):
    q_head, k_head, v_head, b_head, d_head = head_inputs(
        [query_rows, key_rows, value_rows, beta_logit, log_decay]
    )
    key_unit, value_f, beta_gate, decay_log = arrange(k_head, v_head, b_head, d_head)
    group_size = value_f.shape[0] // key_unit.shape[0]
    pieces = span_pass(key_unit, value_f, beta_gate, decay_log, group_size)
    query_unit = arrange_query(q_head)
    fixed, scaled, total = span_prep(query_unit, key_unit, group_size, pieces)
    state_in = chain_states(total)
    core_out = span_out(fixed, scaled, state_in)
    core_rows = head_outputs(to_rows(core_out).astype(jnp.bfloat16))
    return gated_norm(core_rows, output_gate, norm_gain)


def solution(mesh):
    placed = (
        P(("ctx", "head"), None),
        P(("ctx", "head"), None),
        P(("ctx", "head"), None),
        P(("ctx", "head"), None),
        P(("ctx", "head"), None),
        P(("ctx", "head"), None),
        P(),
    )
    return jax.shard_map(
        on_device, mesh=mesh, in_specs=placed, out_specs=P(("ctx", "head"), None), check_vma=False
    )
```

```python
import jax
import jax.numpy as jnp
from jax import lax
from jax.sharding import PartitionSpec as P

DK = 128
DV = 128
SPAN = 128


FULL_PRECISION = lax.Precision.HIGH
LOCAL_PRECISION = lax.Precision.HIGH


def unit_rows(rows):
    return rows * lax.rsqrt(jnp.sum(rows * rows, axis=-1, keepdims=True) + 1e-06)


def compose(earlier, later):
    both = jnp.matmul(
        later[0], jnp.concatenate([earlier[0], earlier[1]], axis=-1), precision=FULL_PRECISION
    )
    return (both[..., : earlier[0].shape[-1]], both[..., earlier[0].shape[-1] :] + later[1])


def compose_joined(earlier, later):
    lane = lax.broadcasted_iota(jnp.int32, later.shape, later.ndim - 1)
    return jnp.matmul(
        later[..., : later.shape[-2]], earlier, precision=FULL_PRECISION
    ) + jnp.where(lane >= later.shape[-2], later, 0.0)


def by_head(rows, width):
    count = rows.shape[1] // width
    parts = [rows[:, g * width : (g + 1) * width] for g in range(count)]
    return jnp.stack(parts).reshape(count, rows.shape[0] // SPAN, SPAN, width)


def arrange(key_part, value_part, beta_part, decay_part):
    blocks = key_part.shape[0] // SPAN
    key_heads = key_part.shape[1] // DK
    value_heads = value_part.shape[1] // DV
    key_unit = unit_rows(
        key_part.astype(jnp.float32).reshape(blocks, SPAN, key_heads, DK)
    ).transpose(2, 0, 1, 3)
    value_f = (
        value_part.astype(jnp.float32).reshape(blocks, SPAN, value_heads, DV).transpose(2, 0, 1, 3)
    )
    beta_gate = (
        jax.nn.sigmoid(beta_part.astype(jnp.float32))
        .reshape(blocks, SPAN, value_heads)
        .transpose(2, 0, 1)
    )
    decay_log = decay_part.astype(jnp.float32).reshape(blocks, SPAN, value_heads).transpose(2, 0, 1)
    return (key_unit, value_f, beta_gate, decay_log)


def arrange_query(query_part):
    blocks = query_part.shape[0] // SPAN
    key_heads = query_part.shape[1] // DK
    query_f = by_head(query_part, DK).astype(jnp.float32)
    return unit_rows(query_f) * DK ** (-0.5)


def unit_lower_inverse(strictly_lower):
    inverse = jnp.eye(SPAN, dtype=jnp.float32) - strictly_lower
    power = jnp.matmul(strictly_lower, strictly_lower, precision=LOCAL_PRECISION)
    covered = 2
    while covered < SPAN:
        if 2 * covered < SPAN:
            both = jnp.matmul(
                jnp.concatenate([inverse, power], axis=-2), power, precision=LOCAL_PRECISION
            )
            inverse = inverse + both[..., :SPAN, :]
            power = both[..., SPAN:, :]
        else:
            inverse = inverse + jnp.matmul(inverse, power, precision=LOCAL_PRECISION)
        covered = covered * 2
    return inverse


def span_pass(key_unit, value_f, beta_gate, decay_log, group_size):
    rowpos = lax.broadcasted_iota(jnp.int32, (SPAN, SPAN), 0)
    colpos = lax.broadcasted_iota(jnp.int32, (SPAN, SPAN), 1)
    cum_log = jnp.cumsum(decay_log, axis=2)
    spread = cum_log[..., :, None] - cum_log[..., None, :]
    strict = jnp.exp(jnp.where(colpos < rowpos, spread, -jnp.inf))
    key_inner = jnp.repeat(
        jnp.einsum("hmik,hmjk->hmij", key_unit, key_unit, precision=LOCAL_PRECISION),
        group_size,
        axis=0,
    )
    inverse = unit_lower_inverse(beta_gate[..., :, None] * strict * key_inner)
    wide_keys = jnp.repeat(key_unit, group_size, axis=0)
    targets = jnp.concatenate(
        [beta_gate[..., None] * value_f, (beta_gate * jnp.exp(cum_log))[..., None] * wide_keys],
        axis=-1,
    )
    solved = jnp.matmul(inverse, targets, precision=LOCAL_PRECISION)
    written = solved[..., :DV]
    weights = solved[..., DV:]
    faded_keys = wide_keys * jnp.exp(cum_log[..., -1:] - cum_log)[..., None]
    tail_decay = jnp.exp(cum_log[..., -1])
    maps = jnp.einsum("hmck,hmcj->hmkj", faded_keys, solved, precision=LOCAL_PRECISION)
    carry_mat = tail_decay[..., None, None] * jnp.eye(DK, dtype=jnp.float32) - maps[..., DV:]
    write_mat = maps[..., :DV]
    return (cum_log, spread, written, weights, carry_mat, write_mat)


def span_prep(query_unit, key_unit, group_size, pieces):
    cum_log, spread, written, weights, carry_mat, write_mat = pieces
    rowpos = lax.broadcasted_iota(jnp.int32, (SPAN, SPAN), 0)
    colpos = lax.broadcasted_iota(jnp.int32, (SPAN, SPAN), 1)
    within = jnp.exp(jnp.where(colpos <= rowpos, spread, -jnp.inf))
    scores = (
        jnp.repeat(
            jnp.einsum("hmik,hmjk->hmij", query_unit, key_unit, precision=LOCAL_PRECISION),
            group_size,
            axis=0,
        )
        * within
    )
    wide_query = jnp.repeat(query_unit, group_size, axis=0)
    mixed = jnp.einsum(
        "hmij,hmjv->hmiv",
        scores,
        jnp.concatenate([written, weights], axis=-1),
        precision=LOCAL_PRECISION,
    )
    inner = mixed[..., :DV]
    reach = wide_query * jnp.exp(cum_log)[..., None] - mixed[..., DV:]
    blocks = carry_mat.shape[1]
    fixed, scaled = ([inner[:, 0]], [reach[:, 0]])
    reach_both = jnp.concatenate([carry_mat, write_mat], axis=-1)
    total = reach_both[:, 0]
    for m in range(1, blocks):
        both = jnp.matmul(reach[:, m], total, precision=LOCAL_PRECISION)
        scaled.append(both[..., :DK])
        fixed.append(inner[:, m] + both[..., DK:])
        total = compose_joined(total, reach_both[:, m])
    return (jnp.stack(fixed, axis=1), jnp.stack(scaled, axis=1), total)


def span_out(fixed, scaled, state_in):
    return fixed + jnp.einsum("hmck,hkv->hmcv", scaled, state_in, precision=FULL_PRECISION)


def to_rows(core_out):
    head_count, blocks = (core_out.shape[0], core_out.shape[1])
    return core_out.transpose(1, 2, 0, 3).reshape(blocks * SPAN, head_count * DV)


def joined(carry, write):
    return jnp.concatenate([carry, write], axis=-1)


def split(both):
    return (both[..., :DK], both[..., DK:])


def exclusive_scan(carry, write, size, stride):
    count = size // stride
    if count == 1:
        return jnp.zeros_like(write)
    rounds = 0
    while 2 ** (rounds + 1) < count:
        rounds += 1
    shift = 1
    for _ in range(rounds):
        pairs = [(i, i + shift * stride) for i in range(size - shift * stride)]
        got = lax.ppermute(joined(carry, write), "ctx", pairs)
        carry, write = compose(split(got), (carry, write))
        shift *= 2
    near = [(i, i + stride) for i in range(size - stride)]
    far = 2**rounds + 1
    if far >= count:
        return lax.ppermute(write, "ctx", near)
    got_carry, got_write = split(lax.ppermute(joined(carry, write), "ctx", near))
    far_write = lax.ppermute(
        write, "ctx", [(i, i + far * stride) for i in range(size - far * stride)]
    )
    return jnp.matmul(got_carry, far_write, precision=FULL_PRECISION) + got_write


def chain_states(block_both):
    size = lax.axis_size("ctx")
    me = lax.axis_index("ctx")
    levels = 0
    while size % 2 ** (levels + 1) == 0 and block_both.shape[0] % 2 ** (levels + 1) == 0:
        levels += 1
    current = block_both
    saved = []
    for level in range(levels):
        stride = 2**level
        upper = (me // stride) % 2 == 1
        half = current.shape[0] // 2
        bit = (me // stride) % 2
        mine = lax.dynamic_slice_in_dim(current, bit * half, half, 0)
        other = lax.dynamic_slice_in_dim(current, (1 - bit) * half, half, 0)
        got = lax.ppermute(other, "ctx", [(i, i ^ stride) for i in range(size)])
        earlier = jnp.where(upper, got, mine)
        later = jnp.where(upper, mine, got)
        saved.append((upper, earlier))
        current = compose_joined(earlier, later)
    state = exclusive_scan(*split(current), size, 2**levels)
    for level in reversed(range(levels)):
        stride = 2**level
        upper, earlier = saved[level]
        earlier_carry, earlier_write = split(earlier)
        after = jnp.matmul(earlier_carry, state, precision=FULL_PRECISION) + earlier_write
        mine = jnp.where(upper, after, state)
        other = jnp.where(upper, state, after)
        got = lax.ppermute(other, "ctx", [(i, i ^ stride) for i in range(size)])
        state = jnp.where(
            upper, jnp.concatenate([got, mine], axis=0), jnp.concatenate([mine, got], axis=0)
        )
    return state


def gated_norm(core_rows, output_gate, norm_gain):
    token_count = core_rows.shape[0]
    head_count = core_rows.shape[1] // DV
    core_f = core_rows.astype(jnp.float32).reshape(token_count, head_count, DV)
    inv_rms = lax.rsqrt(jnp.mean(core_f * core_f, axis=-1, keepdims=True) + 1e-06)
    gate_f = output_gate.astype(jnp.float32).reshape(token_count, head_count, DV)
    gated_rows = core_f * inv_rms * norm_gain.astype(jnp.float32) * jax.nn.silu(gate_f)
    return gated_rows.reshape(token_count, head_count * DV).astype(jnp.bfloat16)


def head_swap(rows):
    width = rows.shape[-1] // 2
    first = lax.axis_index("head") == 0
    own = jnp.where(first, rows[..., :width], rows[..., width:])
    sent = jnp.where(first, rows[..., width:], rows[..., :width])
    got = lax.ppermute(sent, "head", [(0, 1), (1, 0)])
    axis = rows.ndim - 2
    return jnp.where(
        first, jnp.concatenate([own, got], axis), jnp.concatenate([got, own], axis)
    )


def head_return(rows):
    tokens = rows.shape[0] // 2
    first = lax.axis_index("head") == 0
    half = lax.axis_index("head")
    own = lax.dynamic_slice_in_dim(rows, half * tokens, tokens, 0)
    sent = lax.dynamic_slice_in_dim(rows, (1 - half) * tokens, tokens, 0)
    got = lax.ppermute(sent, "head", [(0, 1), (1, 0)])
    return jnp.where(first, jnp.concatenate([own, got], 1), jnp.concatenate([got, own], 1))


def head_inputs(pieces_in):
    parts = lax.axis_size("head")
    if parts == 2:
        query_rows, key_rows, value_rows, beta_logit, log_decay = pieces_in
        query_key = head_swap(jnp.stack([query_rows, key_rows]))
        gates = head_swap(jnp.stack([beta_logit, log_decay]))
        return [query_key[0], query_key[1], head_swap(value_rows), gates[0], gates[1]]
    tokens = pieces_in[0].shape[0]
    widths = [part.shape[1] // parts for part in pieces_in]
    packed = jnp.concatenate(
        [part.reshape(tokens, parts, width) for part, width in zip(pieces_in, widths)], axis=-1
    )
    packed = lax.all_to_all(packed, "head", split_axis=1, concat_axis=0, tiled=True)
    packed = packed.reshape(tokens * parts, sum(widths))
    ends = [sum(widths[: i + 1]) for i in range(len(widths))]
    return [packed[:, end - width : end] for end, width in zip(ends, widths)]


def head_outputs(rows):
    if lax.axis_size("head") == 2:
        return head_return(rows)
    return lax.all_to_all(rows, "head", split_axis=0, concat_axis=1, tiled=True)


def on_device(query_rows, key_rows, value_rows, output_gate, beta_logit, log_decay, norm_gain):
    q_head, k_head, v_head, b_head, d_head = head_inputs(
        [query_rows, key_rows, value_rows, beta_logit, log_decay]
    )
    key_unit, value_f, beta_gate, decay_log = arrange(k_head, v_head, b_head, d_head)
    group_size = value_f.shape[0] // key_unit.shape[0]
    pieces = span_pass(key_unit, value_f, beta_gate, decay_log, group_size)
    query_unit = arrange_query(q_head)
    fixed, scaled, total = span_prep(query_unit, key_unit, group_size, pieces)
    state_in = chain_states(total)
    core_out = span_out(fixed, scaled, state_in)
    core_rows = head_outputs(to_rows(core_out).astype(jnp.bfloat16))
    return gated_norm(core_rows, output_gate, norm_gain)


def solution(mesh):
    placed = (
        P(("ctx", "head"), None),
        P(("ctx", "head"), None),
        P(("ctx", "head"), None),
        P(("ctx", "head"), None),
        P(("ctx", "head"), None),
        P(("ctx", "head"), None),
        P(),
    )
    return jax.shard_map(
        on_device, mesh=mesh, in_specs=placed, out_specs=P(("ctx", "head"), None), check_vma=False
    )
```

```python
import jax
import jax.numpy as jnp
from jax import lax
from jax.sharding import PartitionSpec as P

DK = 128
DV = 128
SPAN = 128


FULL_PRECISION = lax.Precision.HIGH
LOCAL_PRECISION = lax.Precision.HIGH


def unit_rows(rows):
    return rows * lax.rsqrt(jnp.sum(rows * rows, axis=-1, keepdims=True) + 1e-06)


def compose(earlier, later):
    both = jnp.matmul(
        later[0], jnp.concatenate([earlier[0], earlier[1]], axis=-1), precision=FULL_PRECISION
    )
    return (both[..., : earlier[0].shape[-1]], both[..., earlier[0].shape[-1] :] + later[1])


def compose_joined(earlier, later):
    lane = lax.broadcasted_iota(jnp.int32, later.shape, later.ndim - 1)
    return jnp.matmul(
        later[..., : later.shape[-2]], earlier, precision=FULL_PRECISION
    ) + jnp.where(lane >= later.shape[-2], later, 0.0)


def by_head(rows, width):
    count = rows.shape[1] // width
    parts = [rows[:, g * width : (g + 1) * width] for g in range(count)]
    return jnp.stack(parts).reshape(count, rows.shape[0] // SPAN, SPAN, width)


def arrange(key_part, value_part, beta_part, decay_part):
    blocks = key_part.shape[0] // SPAN
    key_heads = key_part.shape[1] // DK
    value_heads = value_part.shape[1] // DV
    key_unit = unit_rows(
        key_part.astype(jnp.float32).reshape(blocks, SPAN, key_heads, DK)
    ).transpose(2, 0, 1, 3)
    value_f = (
        value_part.astype(jnp.float32).reshape(blocks, SPAN, value_heads, DV).transpose(2, 0, 1, 3)
    )
    beta_gate = (
        jax.nn.sigmoid(beta_part.astype(jnp.float32))
        .reshape(blocks, SPAN, value_heads)
        .transpose(2, 0, 1)
    )
    decay_log = decay_part.astype(jnp.float32).reshape(blocks, SPAN, value_heads).transpose(2, 0, 1)
    return (key_unit, value_f, beta_gate, decay_log)


def arrange_query(query_part):
    blocks = query_part.shape[0] // SPAN
    key_heads = query_part.shape[1] // DK
    query_f = by_head(query_part, DK).astype(jnp.float32)
    return unit_rows(query_f) * DK ** (-0.5)


def unit_lower_inverse(strictly_lower):
    inverse = jnp.eye(SPAN, dtype=jnp.float32) - strictly_lower
    power = jnp.matmul(strictly_lower, strictly_lower, precision=LOCAL_PRECISION)
    covered = 2
    while covered < SPAN:
        if 2 * covered < SPAN:
            both = jnp.matmul(
                jnp.concatenate([inverse, power], axis=-2), power, precision=LOCAL_PRECISION
            )
            inverse = inverse + both[..., :SPAN, :]
            power = both[..., SPAN:, :]
        else:
            inverse = inverse + jnp.matmul(inverse, power, precision=LOCAL_PRECISION)
        covered = covered * 2
    return inverse


def span_pass(key_unit, value_f, beta_gate, decay_log, group_size):
    rowpos = lax.broadcasted_iota(jnp.int32, (SPAN, SPAN), 0)
    colpos = lax.broadcasted_iota(jnp.int32, (SPAN, SPAN), 1)
    cum_log = jnp.cumsum(decay_log, axis=2)
    spread = cum_log[..., :, None] - cum_log[..., None, :]
    strict = jnp.exp(jnp.where(colpos < rowpos, spread, -jnp.inf))
    key_inner = jnp.repeat(
        jnp.einsum("hmik,hmjk->hmij", key_unit, key_unit, precision=LOCAL_PRECISION),
        group_size,
        axis=0,
    )
    inverse = unit_lower_inverse(beta_gate[..., :, None] * strict * key_inner)
    wide_keys = jnp.repeat(key_unit, group_size, axis=0)
    targets = jnp.concatenate(
        [beta_gate[..., None] * value_f, (beta_gate * jnp.exp(cum_log))[..., None] * wide_keys],
        axis=-1,
    )
    solved = jnp.matmul(inverse, targets, precision=LOCAL_PRECISION)
    written = solved[..., :DV]
    weights = solved[..., DV:]
    faded_keys = wide_keys * jnp.exp(cum_log[..., -1:] - cum_log)[..., None]
    tail_decay = jnp.exp(cum_log[..., -1])
    maps = jnp.einsum("hmck,hmcj->hmkj", faded_keys, solved, precision=LOCAL_PRECISION)
    carry_mat = tail_decay[..., None, None] * jnp.eye(DK, dtype=jnp.float32) - maps[..., DV:]
    write_mat = maps[..., :DV]
    return (cum_log, spread, written, weights, carry_mat, write_mat)


def span_prep(query_unit, key_unit, group_size, pieces):
    cum_log, spread, written, weights, carry_mat, write_mat = pieces
    rowpos = lax.broadcasted_iota(jnp.int32, (SPAN, SPAN), 0)
    colpos = lax.broadcasted_iota(jnp.int32, (SPAN, SPAN), 1)
    within = jnp.exp(jnp.where(colpos <= rowpos, spread, -jnp.inf))
    scores = (
        jnp.repeat(
            jnp.einsum("hmik,hmjk->hmij", query_unit, key_unit, precision=LOCAL_PRECISION),
            group_size,
            axis=0,
        )
        * within
    )
    wide_query = jnp.repeat(query_unit, group_size, axis=0)
    mixed = jnp.einsum(
        "hmij,hmjv->hmiv",
        scores,
        jnp.concatenate([written, weights], axis=-1),
        precision=LOCAL_PRECISION,
    )
    inner = mixed[..., :DV]
    reach = wide_query * jnp.exp(cum_log)[..., None] - mixed[..., DV:]
    blocks = carry_mat.shape[1]
    fixed, scaled = ([inner[:, 0]], [reach[:, 0]])
    reach_both = jnp.concatenate([carry_mat, write_mat], axis=-1)
    total = reach_both[:, 0]
    for m in range(1, blocks):
        both = jnp.matmul(reach[:, m], total, precision=LOCAL_PRECISION)
        scaled.append(both[..., :DK])
        fixed.append(inner[:, m] + both[..., DK:])
        total = compose_joined(total, reach_both[:, m])
    return (jnp.stack(fixed, axis=1), jnp.stack(scaled, axis=1), total)


def span_out(fixed, scaled, state_in):
    return fixed + jnp.einsum("hmck,hkv->hmcv", scaled, state_in, precision=FULL_PRECISION)


def to_rows(core_out):
    head_count, blocks = (core_out.shape[0], core_out.shape[1])
    return core_out.transpose(1, 2, 0, 3).reshape(blocks * SPAN, head_count * DV)


def joined(carry, write):
    return jnp.concatenate([carry, write], axis=-1)


def split(both):
    return (both[..., :DK], both[..., DK:])


def exclusive_scan(carry, write, size, stride):
    count = size // stride
    if count == 1:
        return jnp.zeros_like(write)
    rounds = 0
    while 2 ** (rounds + 1) < count:
        rounds += 1
    shift = 1
    for _ in range(rounds):
        pairs = [(i, i + shift * stride) for i in range(size - shift * stride)]
        got = lax.ppermute(joined(carry, write), "ctx", pairs)
        carry, write = compose(split(got), (carry, write))
        shift *= 2
    near = [(i, i + stride) for i in range(size - stride)]
    far = 2**rounds + 1
    if far >= count:
        return lax.ppermute(write, "ctx", near)
    got_carry, got_write = split(lax.ppermute(joined(carry, write), "ctx", near))
    far_write = lax.ppermute(
        write, "ctx", [(i, i + far * stride) for i in range(size - far * stride)]
    )
    return jnp.matmul(got_carry, far_write, precision=FULL_PRECISION) + got_write


def chain_states(block_both):
    size = lax.axis_size("ctx")
    me = lax.axis_index("ctx")
    levels = 0
    while size % 2 ** (levels + 1) == 0 and block_both.shape[0] % 2 ** (levels + 1) == 0:
        levels += 1
    current = block_both
    saved = []
    for level in range(levels):
        stride = 2**level
        upper = (me // stride) % 2 == 1
        half = current.shape[0] // 2
        bit = (me // stride) % 2
        mine = lax.dynamic_slice_in_dim(current, bit * half, half, 0)
        other = lax.dynamic_slice_in_dim(current, (1 - bit) * half, half, 0)
        got = lax.ppermute(other, "ctx", [(i, i ^ stride) for i in range(size)])
        earlier = jnp.where(upper, got, mine)
        later = jnp.where(upper, mine, got)
        saved.append((upper, earlier))
        current = compose_joined(earlier, later)
    state = exclusive_scan(*split(current), size, 2**levels)
    for level in reversed(range(levels)):
        stride = 2**level
        upper, earlier = saved[level]
        earlier_carry, earlier_write = split(earlier)
        after = jnp.matmul(earlier_carry, state, precision=FULL_PRECISION) + earlier_write
        mine = jnp.where(upper, after, state)
        other = jnp.where(upper, state, after)
        got = lax.ppermute(other, "ctx", [(i, i ^ stride) for i in range(size)])
        state = jnp.where(
            upper, jnp.concatenate([got, mine], axis=0), jnp.concatenate([mine, got], axis=0)
        )
    return state


def gated_norm(core_rows, output_gate, norm_gain):
    token_count = core_rows.shape[0]
    head_count = core_rows.shape[1] // DV
    core_f = core_rows.astype(jnp.float32).reshape(token_count, head_count, DV)
    inv_rms = lax.rsqrt(jnp.mean(core_f * core_f, axis=-1, keepdims=True) + 1e-06)
    gate_f = output_gate.astype(jnp.float32).reshape(token_count, head_count, DV)
    gated_rows = core_f * inv_rms * norm_gain.astype(jnp.float32) * jax.nn.silu(gate_f)
    return gated_rows.reshape(token_count, head_count * DV).astype(jnp.bfloat16)


def head_swap(rows):
    width = rows.shape[-1] // 2
    first = lax.axis_index("head") == 0
    half = lax.axis_index("head")
    own = lax.dynamic_slice_in_dim(rows, half * width, width, rows.ndim - 1)
    sent = lax.dynamic_slice_in_dim(rows, (1 - half) * width, width, rows.ndim - 1)
    got = lax.ppermute(sent, "head", [(0, 1), (1, 0)])
    axis = rows.ndim - 2
    return jnp.where(
        first, jnp.concatenate([own, got], axis), jnp.concatenate([got, own], axis)
    )


def head_return(rows):
    tokens = rows.shape[0] // 2
    first = lax.axis_index("head") == 0
    half = lax.axis_index("head")
    own = lax.dynamic_slice_in_dim(rows, half * tokens, tokens, 0)
    sent = lax.dynamic_slice_in_dim(rows, (1 - half) * tokens, tokens, 0)
    got = lax.ppermute(sent, "head", [(0, 1), (1, 0)])
    return jnp.where(first, jnp.concatenate([own, got], 1), jnp.concatenate([got, own], 1))


def head_inputs(pieces_in):
    parts = lax.axis_size("head")
    if parts == 2:
        query_rows, key_rows, value_rows, beta_logit, log_decay = pieces_in
        query_key = head_swap(jnp.stack([query_rows, key_rows]))
        gates = head_swap(jnp.stack([beta_logit, log_decay]))
        return [query_key[0], query_key[1], head_swap(value_rows), gates[0], gates[1]]
    tokens = pieces_in[0].shape[0]
    widths = [part.shape[1] // parts for part in pieces_in]
    packed = jnp.concatenate(
        [part.reshape(tokens, parts, width) for part, width in zip(pieces_in, widths)], axis=-1
    )
    packed = lax.all_to_all(packed, "head", split_axis=1, concat_axis=0, tiled=True)
    packed = packed.reshape(tokens * parts, sum(widths))
    ends = [sum(widths[: i + 1]) for i in range(len(widths))]
    return [packed[:, end - width : end] for end, width in zip(ends, widths)]


def head_outputs(rows):
    if lax.axis_size("head") == 2:
        return head_return(rows)
    return lax.all_to_all(rows, "head", split_axis=0, concat_axis=1, tiled=True)


def on_device(query_rows, key_rows, value_rows, output_gate, beta_logit, log_decay, norm_gain):
    q_head, k_head, v_head, b_head, d_head = head_inputs(
        [query_rows, key_rows, value_rows, beta_logit, log_decay]
    )
    key_unit, value_f, beta_gate, decay_log = arrange(k_head, v_head, b_head, d_head)
    group_size = value_f.shape[0] // key_unit.shape[0]
    pieces = span_pass(key_unit, value_f, beta_gate, decay_log, group_size)
    query_unit = arrange_query(q_head)
    fixed, scaled, total = span_prep(query_unit, key_unit, group_size, pieces)
    state_in = chain_states(total)
    core_out = span_out(fixed, scaled, state_in)
    core_rows = head_outputs(to_rows(core_out).astype(jnp.bfloat16))
    return gated_norm(core_rows, output_gate, norm_gain)


def solution(mesh):
    placed = (
        P(("ctx", "head"), None),
        P(("ctx", "head"), None),
        P(("ctx", "head"), None),
        P(("ctx", "head"), None),
        P(("ctx", "head"), None),
        P(("ctx", "head"), None),
        P(),
    )
    return jax.shard_map(
        on_device, mesh=mesh, in_specs=placed, out_specs=P(("ctx", "head"), None), check_vma=False
    )
```
